32 devices in a mesh: slab: 4 (over y, x), rad: 8 (over z, core).
Axes of the slice: x: 2, y: 2, z: 4, core: 2. Of those that a mesh axis runs over, the one named last changes fastest.
Arguments:
- q_state: float32 [3, 524288], P(None, ('slab', 'rad')), may hold values from -6.71 to 6.71, as said below
- increments: float32 [3, 524288], P(None, ('slab', 'rad')), may hold values from -6 to 6
- velocity_grad: float32 [5, 12288], P(None, 'slab'), may hold values from -40 to 40
- element: int32 [524288], P(('slab', 'rad')), may hold values from 0 to 3071
- migration: int32 [524288], P(('slab', 'rad')), may hold values from -1 to 1, as said below
- volume: float32 [12288], P(('slab', 'rad')), may hold values from 14.222222 to 128
- div_map: float32 [192, 192], replicated, may hold values from -0.4375 to 0.4375
- stiffness: float32 [256, 4, 192, 192], P(('slab', 'rad')), may hold values from -0.06 to 1.06
- pattern: int32 [256, 4], P(('slab', 'rad')), may hold values from 0 to 191, as said below
- preconditioner: float32 [256, 192, 192], P(('slab', 'rad')), may hold values from -0.03 to 1.03
Outputs:
- q_out: float32 [3, 524288], P(None, ('slab', 'rad'))
- arrivals: float32 [2, 3, 32768], P(None, None, ('slab', 'rad'))
- element_stress: float32 [4, 12288], P(None, ('slab', 'rad'))
- velocity: float32 [256, 192], P(('slab', 'rad'))
The draws below stay inside these ranges and needn't reach their ends.
Inputs may be any that keep to these rules, and one draw needn't show every extreme that they name: `q_state`: every dumbbell's stretch r^2 + z^2 + t^2 is below 45. Of the dumbbells of one device at most 1024 have migration 1 and at most 1024 have migration -1; some device has exactly 1024 with 1 and some device exactly 1024 with -1. pattern[b, 0] = 64 + b % 64; pattern[b, 1] lies in 0 .. 63, pattern[b, 2] in 64 .. 127, pattern[b, 3] in 128 .. 191.
All inputs are finite; a program needn't handle non-finite values.
Results may differ from the reference program's by a relative error of at most 0.0003.
Values sent between devices are 32-bit elements; how exact they have to be, the bound alone decides.
No kernel may reach another device: no remote copies, remote signals or barrier semaphores. Data moves between devices by JAX's collectives and lax.ppermute only.
A program may use at most 64 MiB of HBM per device.

```python
import math
import jax
import jax.numpy as jnp
from jax import lax

DB_DEV = 16384
BLOCK = 192
NNZ = 4
ITERS = 6
MIG = 1024
E_SLAB = 3072
E_TOTAL = 12288
SLAB_BLK = 64
BLK_TOTAL = 256
DB_TOTAL = 524288
N_SLAB = 4
N_RAD = 8


def shuffled(subkey):
    return jax.random.permutation(subkey, DB_DEV)


def draw_q_state(key, part):
    shape = (3, DB_TOTAL)
    raw = jax.random.truncated_normal(key, -3.5, 3.5, shape, jnp.float32) * 1.5
    stretch = jnp.sum(raw * raw, axis=0, keepdims=True)
    return raw / jnp.sqrt(1.0 + stretch / 45.0)


def draw_migration(key, part):
    devices = N_SLAB * N_RAD
    key_up, key_down, key_pick_up, key_pick_down, key_order = jax.random.split(key, 5)
    upward = jax.random.randint(key_up, (devices,), MIG // 2, MIG + 1)
    upward = upward.at[jax.random.randint(key_pick_up, (), 0, devices)].set(MIG)
    downward = jax.random.randint(key_down, (devices,), MIG // 2, MIG + 1)
    downward = downward.at[jax.random.randint(key_pick_down, (), 0, devices)].set(MIG)
    order = jax.vmap(shuffled)(jax.random.split(key_order, devices))
    result = jnp.where(order < upward[:, None], 1, jnp.where(order < (upward + downward)[:, None], -1, 0))
    return result.astype(jnp.int32).reshape(-1)


def draw_pattern(key, part):
    key_before, key_beside, key_after = jax.random.split(key, 3)
    rows = jnp.arange(BLK_TOTAL, dtype=jnp.int32)
    own = SLAB_BLK + rows % SLAB_BLK
    before = jax.random.randint(key_before, (BLK_TOTAL,), 0, SLAB_BLK).at[0].set(0)
    beside = jax.random.randint(key_beside, (BLK_TOTAL,), SLAB_BLK, 2 * SLAB_BLK)
    after = jax.random.randint(key_after, (BLK_TOTAL,), 2 * SLAB_BLK, 3 * SLAB_BLK).at[BLK_TOTAL - 1].set(3 * SLAB_BLK - 1)
    return jnp.stack([own, before, beside, after], 1).astype(jnp.int32)


def rough_part(key, shape):
    return jax.random.truncated_normal(key, -4.0, 4.0, shape, jnp.float32)


def draw_stiffness(key, part):
    shape = (BLK_TOTAL, NNZ, BLOCK, BLOCK)
    identity = jnp.eye(BLOCK, dtype=jnp.float32)
    first = (jnp.arange(NNZ) == 0).astype(jnp.float32)[:, None, None]
    return rough_part(key, shape) * (0.2 / math.sqrt(BLOCK)) + first * identity


def draw_preconditioner(key, part):
    shape = (BLK_TOTAL, BLOCK, BLOCK)
    return rough_part(key, shape) * (0.1 / math.sqrt(BLOCK)) + jnp.eye(BLOCK, dtype=jnp.float32)


def set_ends(values, own_key, smallest, high):
    extent = values.shape
    place = [jax.random.randint(jax.random.fold_in(own_key, axis), (), 0, extent[axis]) for axis in range(len(extent))]
    values = values.at[tuple(place)].set(smallest)
    longest = extent.index(max(extent))
    place[longest] = (place[longest] + 1) % extent[longest]
    return values.at[tuple(place)].set(high)


def block_levels(own_key, dims, cuts, least, top_value):
    level = 1.0
    for axis_at, shards_of in cuts:
        steps = jax.random.uniform(jax.random.fold_in(jax.random.fold_in(own_key, 6), axis_at), (shards_of,), jnp.float32, least / len(cuts), top_value / len(cuts))
        level = level * jnp.repeat(jnp.exp(steps), dims[axis_at] // shards_of).reshape((-1,) + (1,) * (len(dims) - 1 - axis_at))
    return level


def normal_values(own_key, dims, spread, bound, cuts=(), kind=jnp.bfloat16):
    drawn = jax.random.normal(own_key, dims, jnp.float32) * spread
    if len(cuts) > 0:
        drawn = block_levels(own_key, dims, cuts, -0.22, 0.18) * drawn
    return jnp.clip(drawn, min=-bound, max=bound).astype(kind)


def setup_inputs(seed: int = 0) -> dict:
    splits = jax.random.split(jax.random.key(seed), 11)
    q_state = draw_q_state(jax.random.fold_in(splits[10], 71), 0)
    increments = normal_values(splits[1], (3, DB_TOTAL), 1.0, 6.0, ((1, 32),), jnp.float32)
    velocity_grad = normal_values(splits[2], (5, E_TOTAL), 10.0, 40.0, ((1, 4),), jnp.float32)
    element = set_ends(jax.random.randint(splits[3], (DB_TOTAL,), 0, E_SLAB), jax.random.fold_in(splits[3], 1), 0, E_SLAB - 1).astype(jnp.int32)
    migration = draw_migration(jax.random.fold_in(splits[10], 71), 0)
    volume = jnp.clip(jnp.exp(math.log(128.0) - 2.1972246 * jax.random.uniform(splits[5], (E_TOTAL,), jnp.float32) ** block_levels(splits[5], (E_TOTAL,), ((0, 32),), -0.2, 0.2)), 14.222222, 128.0)
    div_map = normal_values(splits[6], (BLOCK, BLOCK), BLOCK ** -0.5, 0.4375, (), jnp.float32)
    stiffness = draw_stiffness(jax.random.fold_in(splits[10], 71), 0)
    pattern = draw_pattern(jax.random.fold_in(splits[10], 71), 0)
    preconditioner = draw_preconditioner(jax.random.fold_in(splits[10], 71), 0)
    return dict(q_state=q_state, increments=increments, velocity_grad=velocity_grad, element=element, migration=migration, volume=volume, div_map=div_map, stiffness=stiffness, pattern=pattern, preconditioner=preconditioner)


extensibility = 50.0
time_step = 0.01
noise_scale = 0.1
damping = 0.6


def update_dumbbells(q_here, inc_here, grads):
    radial = q_here[0]
    axial = q_here[1]
    azimuth = q_here[2]
    stretch = radial * radial + axial * axial + azimuth * azimuth
    spring = 1.0 / (1.0 - stretch / extensibility)
    drift = jnp.stack([grads[0] * radial + grads[1] * axial, grads[2] * radial + grads[3] * axial, grads[4] * azimuth])
    q_next = q_here + time_step * (drift - 0.5 * spring * q_here) + noise_scale * inc_here
    terms = jnp.stack([spring * radial * radial - 1.0, spring * axial * axial - 1.0, spring * radial * axial, spring * azimuth * azimuth - 1.0])
    return q_next, terms


def pack_moving(payload, chosen, capacity):
    slots = jnp.cumsum(chosen.astype(jnp.int32)) - 1
    target = jnp.where(chosen, slots, capacity).astype(jnp.int32)
    empty = jnp.zeros((payload.shape[0], capacity), payload.dtype)
    return empty.at[:, target].set(payload, mode="drop")


def absorb(partial_value, lower, upper):
    partial_value = partial_value.at[:, lower[7].astype(jnp.int32)].add(lower[3:7])
    return partial_value.at[:, upper[7].astype(jnp.int32)].add(upper[3:7])


def reference(q_state, increments, velocity_grad, element, migration, volume, div_map, stiffness, pattern, preconditioner):
    devices = N_SLAB * N_RAD
    capacity = MIG
    q_blocks = q_state.reshape(3, devices, DB_DEV).transpose(1, 0, 2)
    inc_blocks = increments.reshape(3, devices, DB_DEV).transpose(1, 0, 2)
    elem_blocks = element.reshape(devices, DB_DEV)
    move_blocks = migration.reshape(devices, DB_DEV)

    def one_device(items):
        device, q_here, inc_here, elem_here, move_here = items
        table = lax.dynamic_slice_in_dim(velocity_grad, (device // N_RAD) * E_SLAB, E_SLAB, 1)
        q_next, terms = update_dumbbells(q_here, inc_here, table[:, elem_here])
        payload = jnp.concatenate([q_next, terms, elem_here.astype(q_next.dtype)[None]], 0)
        upward = pack_moving(payload, move_here == 1, capacity)
        downward = pack_moving(payload, move_here == -1, capacity)
        staying = jnp.where(move_here == 0, terms, 0.0)
        partial_value = jnp.zeros((4, E_SLAB), terms.dtype).at[:, elem_here].add(staying)
        return q_next, upward, downward, partial_value

    q_new, upward, downward, partial_value = lax.map(one_device, (jnp.arange(devices, dtype=jnp.int32), q_blocks, inc_blocks, elem_blocks, move_blocks))
    blank = jnp.zeros((N_RAD, 8, capacity), upward.dtype)
    from_lower = jnp.concatenate([blank, upward[:devices - N_RAD]], 0)
    from_upper = jnp.concatenate([downward[N_RAD:], blank], 0)
    partial_value = jax.vmap(absorb)(partial_value, from_lower, from_upper)
    sums = partial_value.reshape(N_SLAB, N_RAD, 4, E_SLAB).sum(1).transpose(1, 0, 2).reshape(4, E_TOTAL)
    element_stress = sums / volume
    q_out = q_new.transpose(1, 0, 2).reshape(3, DB_TOTAL)
    arrivals = jnp.stack([from_lower[:, 0:3].transpose(1, 0, 2).reshape(3, devices * capacity), from_upper[:, 0:3].transpose(1, 0, 2).reshape(3, devices * capacity)])
    groups = element_stress.reshape(4, BLK_TOTAL, BLOCK // 4).transpose(1, 0, 2).reshape(BLK_TOTAL, BLOCK)
    force = jnp.dot(groups, div_map, precision=lax.Precision.HIGHEST)

    def precondition(vector):
        return jnp.einsum("bij,bj->bi", preconditioner, vector, precision=lax.Precision.HIGHEST)

    velocity = damping * precondition(force)
    owner = (jnp.arange(BLK_TOTAL, dtype=jnp.int32) // SLAB_BLK) * SLAB_BLK
    where_read = owner[:, None] + pattern
    for sweep_index in range(1, ITERS):
        border = jnp.zeros((SLAB_BLK, BLOCK), velocity.dtype)
        padded = jnp.concatenate([border, velocity, border], 0)
        neighbours = padded[where_read]
        image = jnp.einsum("bnij,bnj->bi", stiffness, neighbours, precision=lax.Precision.HIGHEST)
        velocity = velocity + damping * precondition(force - image)
    return q_out, arrivals, element_stress, velocity
```

```python
import functools

import jax
import jax.numpy as jnp
from jax import lax
from jax.experimental import pallas as pl
from jax.experimental.pallas import tpu as pltpu
from jax.sharding import PartitionSpec as P

BLOCK = 192
ITERS = 6
CHUNK = 512

extensibility = 50.0
time_step = 0.01
noise_scale = 0.1
damping = 0.6
highest = lax.Precision.HIGHEST
nt_dims = (((1,), (1,)), ((), ()))


def round_up(value, step):
    return -(-value // step) * step


def bf16_pieces(x):
    hi = x.astype(jnp.bfloat16)
    rest = x - hi.astype(jnp.float32)
    mid = rest.astype(jnp.bfloat16)
    lo = (rest - mid.astype(jnp.float32)).astype(jnp.bfloat16)
    return (hi, mid, lo)


def spring_terms(q):
    radial = q[0:1]
    axial = q[1:2]
    azimuth = q[2:3]
    stretch = radial * radial + axial * axial + azimuth * azimuth
    spring = 1.0 / (1.0 - stretch / extensibility)
    terms = (
        spring * radial * radial - 1.0,
        spring * axial * axial - 1.0,
        spring * radial * axial,
        spring * azimuth * azimuth - 1.0,
    )
    return spring, terms


def stress_kernel(q_ref, e_ref, m_ref, out_ref, *, groups, rows):
    count = q_ref.shape[1]
    out_ref[...] = jnp.zeros_like(out_ref)
    low_iota = lax.broadcasted_iota(jnp.int32, (128, CHUNK), 0)
    row_iota = lax.broadcasted_iota(jnp.int32, (rows, CHUNK), 0)
    zero = jnp.zeros((), jnp.bfloat16)

    def body(step, carry):
        cols = pl.ds(pl.multiple_of(step * CHUNK, CHUNK), CHUNK)
        q = q_ref[:, cols]
        element = e_ref[:, cols]
        move = m_ref[:, cols]
        spring, terms = spring_terms(q)
        kind = jnp.where(move == 0, 1, jnp.where(move == 1, 2, 0))
        key = kind * groups + (element >> 7)
        low = (low_iota == (element & 127)).astype(jnp.bfloat16)
        mask = row_iota == key
        pieces = [bf16_pieces(term) for term in terms]
        for p in range(3):
            spread = jnp.concatenate(
                [jnp.where(mask, pieces[c][p], zero) for c in range(4)], axis=0
            )
            out_ref[p] += lax.dot_general(
                spread, low, nt_dims, preferred_element_type=jnp.float32
            )
        return carry

    lax.fori_loop(0, count // CHUNK, body, 0)


def update_kernel(
    q_ref, inc_ref, e_ref, m_ref, tab_ref, qn_ref, up_ref, dn_ref, tri_ref, *, groups16, slots16
):
    count = q_ref.shape[1]
    up_ref[...] = jnp.zeros_like(up_ref)
    dn_ref[...] = jnp.zeros_like(dn_ref)
    before = lax.broadcasted_iota(jnp.int32, (CHUNK, CHUNK), 0)
    after = lax.broadcasted_iota(jnp.int32, (CHUNK, CHUNK), 1)
    tri_ref[...] = (before < after).astype(jnp.bfloat16)
    low_iota = lax.broadcasted_iota(jnp.int32, (128, CHUNK), 0)
    group_iota = lax.broadcasted_iota(jnp.int32, (groups16, CHUNK), 0)
    slot_iota = lax.broadcasted_iota(jnp.int32, (slots16, CHUNK), 0)
    flag_row = lax.broadcasted_iota(jnp.int32, (8, CHUNK), 0)
    zero = jnp.zeros((), jnp.bfloat16)

    def body(step, offsets):
        cols = pl.ds(pl.multiple_of(step * CHUNK, CHUNK), CHUNK)
        q = q_ref[:, cols]
        inc = inc_ref[:, cols]
        element = e_ref[:, cols]
        move = m_ref[:, cols]
        low = (low_iota == (element & 127)).astype(jnp.bfloat16)
        picked = jnp.dot(tab_ref[0], low, preferred_element_type=jnp.float32)
        picked = picked + jnp.dot(tab_ref[1], low, preferred_element_type=jnp.float32)
        picked = picked + jnp.dot(tab_ref[2], low, preferred_element_type=jnp.float32)
        hit = group_iota == (element >> 7)
        grads = [
            jnp.sum(
                jnp.where(hit, picked[c * groups16 : (c + 1) * groups16], 0.0),
                axis=0,
                keepdims=True,
            )
            for c in range(5)
        ]
        radial = q[0:1]
        axial = q[1:2]
        azimuth = q[2:3]
        spring, terms = spring_terms(q)
        drift = (
            grads[0] * radial + grads[1] * axial,
            grads[2] * radial + grads[3] * axial,
            grads[4] * azimuth,
        )
        q_next = [
            q[k : k + 1] + time_step * (drift[k] - 0.5 * spring * q[k : k + 1]) + noise_scale * inc[k : k + 1]
            for k in range(3)
        ]
        qn_ref[:, cols] = jnp.concatenate(q_next, axis=0)
        going_up = move == 1
        going_down = move == -1
        flags = jnp.where(
            flag_row == 0,
            going_up.astype(jnp.float32),
            jnp.where(flag_row == 1, going_down.astype(jnp.float32), 0.0),
        )
        ranks = jnp.dot(flags.astype(jnp.bfloat16), tri_ref[...], preferred_element_type=jnp.float32)
        slots = (ranks + offsets).astype(jnp.int32)
        pieces = [bf16_pieces(value) for value in q_next]
        for direction, chosen, out_ref in ((0, going_up, up_ref), (1, going_down, dn_ref)):
            slot = slots[direction : direction + 1]
            place = ((low_iota == (slot & 127)) & chosen).astype(jnp.bfloat16)
            which = slot_iota == (slot >> 7)
            for p in range(3):
                spread = jnp.concatenate(
                    [jnp.where(which, pieces[k][p], zero) for k in range(3)], axis=0
                )
                out_ref[p] += lax.dot_general(
                    spread, place, nt_dims, preferred_element_type=jnp.float32
                )
        return offsets + jnp.sum(flags, axis=1, keepdims=True)

    lax.fori_loop(0, count // CHUNK, body, jnp.zeros((8, 1), jnp.float32))


def stress_partials(q_state, element, migration, slab_elems):
    groups = slab_elems // 128
    rows = round_up(3 * groups, 16)
    count = q_state.shape[1]
    out = pl.pallas_call(
        functools.partial(stress_kernel, groups=groups, rows=rows),
        out_shape=jax.ShapeDtypeStruct((3, 4 * rows, 128), jnp.float32),
        cost_estimate=pl.CostEstimate(
            flops=2 * 3 * 4 * rows * 128 * count, transcendentals=0, bytes_accessed=20 * count
        ),
    )(q_state, element.reshape(1, -1), migration.reshape(1, -1))
    total = out[0] + out[1] + out[2]
    total = total.reshape(4, rows, 128)[:, : 3 * groups].reshape(4, 3 * slab_elems)
    return total


def update_and_pack(q_state, increments, element, migration, table, capacity):
    rows, slab_elems = table.shape
    groups = slab_elems // 128
    groups16 = round_up(groups, 16)
    slots = capacity // 128
    slots16 = round_up(slots, 16)
    arranged = jnp.pad(table.reshape(rows, groups, 128), ((0, 0), (0, groups16 - groups), (0, 0)))
    arranged = arranged.reshape(rows * groups16, 128)
    hi = lax.reduce_precision(arranged, exponent_bits=8, mantissa_bits=7)
    rest = arranged - hi
    mid = lax.reduce_precision(rest, exponent_bits=8, mantissa_bits=7)
    lo = rest - mid
    pieces = jnp.stack([hi, mid, lo]).astype(jnp.bfloat16)
    count = q_state.shape[1]
    q_next, up, down = pl.pallas_call(
        functools.partial(update_kernel, groups16=groups16, slots16=slots16),
        out_shape=(
            jax.ShapeDtypeStruct((3, count), jnp.float32),
            jax.ShapeDtypeStruct((3, 3 * slots16, 128), jnp.float32),
            jax.ShapeDtypeStruct((3, 3 * slots16, 128), jnp.float32),
        ),
        scratch_shapes=[pltpu.VMEM((CHUNK, CHUNK), jnp.bfloat16)],
        cost_estimate=pl.CostEstimate(
            flops=2 * 3 * (5 * groups16 + 6 * slots16) * 128 * count,
            transcendentals=0,
            bytes_accessed=40 * count,
        ),
    )(q_state, increments, element.reshape(1, -1), migration.reshape(1, -1), pieces)

    def unpack(acc):
        whole = acc[0] + acc[1] + acc[2]
        return whole.reshape(3, slots16, 128)[:, :slots].reshape(3, slots * 128)

    return q_next, unpack(up), unpack(down)


def passed_along(array, axis, by):
    size = lax.axis_size(axis)
    pairs = [(i, i + by) for i in range(size) if 0 <= i + by < size]
    return lax.ppermute(array, axis, pairs)


def body(
    q_state,
    increments,
    velocity_grad,
    element,
    migration,
    volume,
    div_map,
    stiffness,
    pattern,
    preconditioner,
):
    capacity = migration.shape[0] // 16
    slab_elems = velocity_grad.shape[1]
    n_slab = lax.axis_size("slab")
    slab = lax.axis_index("slab")

    near = stress_partials(q_state, element, migration, slab_elems)
    spread = jnp.zeros((4, (n_slab + 2) * slab_elems), jnp.float32)
    spread = lax.dynamic_update_slice(spread, near, (0, slab * slab_elems))
    spread = spread[:, slab_elems : (n_slab + 1) * slab_elems]
    sums = lax.psum_scatter(spread, ("slab", "rad"), scatter_dimension=1, tiled=True)
    element_stress = sums / volume

    q_next, upward, downward = update_and_pack(
        q_state, increments, element, migration, velocity_grad, capacity
    )
    from_lower = passed_along(upward, "slab", 1)
    from_upper = passed_along(downward, "slab", -1)
    arrivals = jnp.stack([from_lower, from_upper])

    own_blocks = stiffness.shape[0]
    groups = (
        element_stress.reshape(4, own_blocks, BLOCK // 4)
        .transpose(1, 0, 2)
        .reshape(own_blocks, BLOCK)
    )
    force = jnp.dot(groups, div_map, precision=highest)

    def precondition(vector):
        return jnp.einsum("bij,bj->bi", preconditioner, vector, precision=highest)

    slab_blocks = own_blocks * lax.axis_size("rad")
    all_blocks = slab_blocks * n_slab
    where_read = (slab - 1) * slab_blocks + pattern.reshape(-1)
    selector = (
        where_read[:, None] == jnp.arange(all_blocks, dtype=jnp.int32)[None, :]
    ).astype(jnp.float32)
    velocity = damping * precondition(force)
    for sweep_index in range(1, ITERS):
        gathered = lax.all_gather(velocity, ("slab", "rad"), axis=0, tiled=True)
        neighbours = jnp.dot(selector, gathered, precision=highest).reshape(own_blocks, -1, BLOCK)
        image = jnp.einsum("bnij,bnj->bi", stiffness, neighbours, precision=highest)
        velocity = velocity + damping * precondition(force - image)
    return (q_next, arrivals, element_stress, velocity)


def solution(mesh):
    placed = (
        P(None, ("slab", "rad")),
        P(None, ("slab", "rad")),
        P(None, "slab"),
        P(("slab", "rad")),
        P(("slab", "rad")),
        P(("slab", "rad")),
        P(),
        P(("slab", "rad"), None, None, None),
        P(("slab", "rad"), None),
        P(("slab", "rad"), None, None),
    )
    return jax.shard_map(
        body,
        mesh=mesh,
        in_specs=placed,
        out_specs=(
            P(None, ("slab", "rad")),
            P(None, None, ("slab", "rad")),
            P(None, ("slab", "rad")),
            P(("slab", "rad"), None),
        ),
        check_vma=False,
    )
```

```python
import functools

import jax
import jax.numpy as jnp
from jax import lax
from jax.experimental import pallas as pl
from jax.experimental.pallas import tpu as pltpu
from jax.sharding import PartitionSpec as P

BLOCK = 192
ITERS = 6
CHUNK = 512

extensibility = 50.0
time_step = 0.01
noise_scale = 0.1
damping = 0.6
highest = lax.Precision.HIGHEST
nt_dims = (((1,), (1,)), ((), ()))


def round_up(value, step):
    return -(-value // step) * step


def bf16_pieces(x):
    hi = x.astype(jnp.bfloat16)
    rest = x - hi.astype(jnp.float32)
    mid = rest.astype(jnp.bfloat16)
    lo = (rest - mid.astype(jnp.float32)).astype(jnp.bfloat16)
    return (hi, mid, lo)


def spring_terms(q):
    radial = q[0:1]
    axial = q[1:2]
    azimuth = q[2:3]
    stretch = radial * radial + axial * axial + azimuth * azimuth
    spring = 1.0 / (1.0 - stretch / extensibility)
    terms = (
        spring * radial * radial - 1.0,
        spring * axial * axial - 1.0,
        spring * radial * axial,
        spring * azimuth * azimuth - 1.0,
    )
    return spring, terms


def stress_kernel(q_ref, e_ref, m_ref, out_ref, *, groups, rows):
    count = q_ref.shape[1]
    out_ref[...] = jnp.zeros_like(out_ref)
    low_iota = lax.broadcasted_iota(jnp.int32, (128, CHUNK), 0)
    row_iota = lax.broadcasted_iota(jnp.int32, (rows, CHUNK), 0)
    zero = jnp.zeros((), jnp.bfloat16)

    def body(step, carry):
        cols = pl.ds(pl.multiple_of(step * CHUNK, CHUNK), CHUNK)
        q = q_ref[:, cols]
        element = e_ref[:, cols]
        move = m_ref[:, cols]
        spring, terms = spring_terms(q)
        kind = jnp.where(move == 0, 1, jnp.where(move == 1, 2, 0))
        key = kind * groups + (element >> 7)
        low = (low_iota == (element & 127)).astype(jnp.bfloat16)
        mask = row_iota == key
        pieces = [bf16_pieces(term) for term in terms]
        for p in range(3):
            spread = jnp.concatenate(
                [jnp.where(mask, pieces[c][p], zero) for c in range(4)], axis=0
            )
            out_ref[p] += lax.dot_general(
                spread, low, nt_dims, preferred_element_type=jnp.float32
            )
        return carry

    lax.fori_loop(0, count // CHUNK, body, 0)


def update_kernel(
    q_ref, inc_ref, e_ref, m_ref, tab_ref, qn_ref, up_ref, dn_ref, tri_ref, *, groups16, slots16
):
    count = q_ref.shape[1]
    up_ref[...] = jnp.zeros_like(up_ref)
    dn_ref[...] = jnp.zeros_like(dn_ref)
    before = lax.broadcasted_iota(jnp.int32, (CHUNK, CHUNK), 0)
    after = lax.broadcasted_iota(jnp.int32, (CHUNK, CHUNK), 1)
    tri_ref[...] = (before < after).astype(jnp.bfloat16)
    low_iota = lax.broadcasted_iota(jnp.int32, (128, CHUNK), 0)
    group_iota = lax.broadcasted_iota(jnp.int32, (groups16, CHUNK), 0)
    slot_iota = lax.broadcasted_iota(jnp.int32, (slots16, CHUNK), 0)
    flag_row = lax.broadcasted_iota(jnp.int32, (8, CHUNK), 0)
    zero = jnp.zeros((), jnp.bfloat16)

    def body(step, offsets):
        cols = pl.ds(pl.multiple_of(step * CHUNK, CHUNK), CHUNK)
        q = q_ref[:, cols]
        inc = inc_ref[:, cols]
        element = e_ref[:, cols]
        move = m_ref[:, cols]
        low = (low_iota == (element & 127)).astype(jnp.bfloat16)
        picked = jnp.dot(tab_ref[0], low, preferred_element_type=jnp.float32)
        picked = picked + jnp.dot(tab_ref[1], low, preferred_element_type=jnp.float32)
        picked = picked + jnp.dot(tab_ref[2], low, preferred_element_type=jnp.float32)
        hit = group_iota == (element >> 7)
        grads = [
            jnp.sum(
                jnp.where(hit, picked[c * groups16 : (c + 1) * groups16], 0.0),
                axis=0,
                keepdims=True,
            )
            for c in range(5)
        ]
        radial = q[0:1]
        axial = q[1:2]
        azimuth = q[2:3]
        spring, terms = spring_terms(q)
        drift = (
            grads[0] * radial + grads[1] * axial,
            grads[2] * radial + grads[3] * axial,
            grads[4] * azimuth,
        )
        q_next = [
            q[k : k + 1] + time_step * (drift[k] - 0.5 * spring * q[k : k + 1]) + noise_scale * inc[k : k + 1]
            for k in range(3)
        ]
        qn_ref[:, cols] = jnp.concatenate(q_next, axis=0)
        going_up = move == 1
        going_down = move == -1
        flags = jnp.where(
            flag_row == 0,
            going_up.astype(jnp.float32),
            jnp.where(flag_row == 1, going_down.astype(jnp.float32), 0.0),
        )
        ranks = jnp.dot(flags.astype(jnp.bfloat16), tri_ref[...], preferred_element_type=jnp.float32)
        slots = (ranks + offsets).astype(jnp.int32)
        pieces = [bf16_pieces(value) for value in q_next]
        for direction, chosen, out_ref in ((0, going_up, up_ref), (1, going_down, dn_ref)):
            slot = slots[direction : direction + 1]
            place = ((low_iota == (slot & 127)) & chosen).astype(jnp.bfloat16)
            which = slot_iota == (slot >> 7)
            for p in range(3):
                spread = jnp.concatenate(
                    [jnp.where(which, pieces[k][p], zero) for k in range(3)], axis=0
                )
                out_ref[p] += lax.dot_general(
                    spread, place, nt_dims, preferred_element_type=jnp.float32
                )
        return offsets + jnp.sum(flags, axis=1, keepdims=True)

    lax.fori_loop(0, count // CHUNK, body, jnp.zeros((8, 1), jnp.float32))


def stress_partials(q_state, element, migration, slab_elems):
    groups = slab_elems // 128
    rows = round_up(3 * groups, 16)
    count = q_state.shape[1]
    out = pl.pallas_call(
        functools.partial(stress_kernel, groups=groups, rows=rows),
        out_shape=jax.ShapeDtypeStruct((3, 4 * rows, 128), jnp.float32),
        cost_estimate=pl.CostEstimate(
            flops=2 * 3 * 4 * rows * 128 * count, transcendentals=0, bytes_accessed=20 * count
        ),
    )(q_state, element.reshape(1, -1), migration.reshape(1, -1))
    total = out[0] + out[1] + out[2]
    total = total.reshape(4, rows, 128)[:, : 3 * groups].reshape(4, 3 * slab_elems)
    return total


def update_and_pack(q_state, increments, element, migration, table, capacity):
    rows, slab_elems = table.shape
    groups = slab_elems // 128
    groups16 = round_up(groups, 16)
    slots = capacity // 128
    slots16 = round_up(slots, 16)
    arranged = jnp.pad(table.reshape(rows, groups, 128), ((0, 0), (0, groups16 - groups), (0, 0)))
    arranged = arranged.reshape(rows * groups16, 128)
    hi = lax.reduce_precision(arranged, exponent_bits=8, mantissa_bits=7)
    rest = arranged - hi
    mid = lax.reduce_precision(rest, exponent_bits=8, mantissa_bits=7)
    lo = rest - mid
    pieces = jnp.stack([hi, mid, lo]).astype(jnp.bfloat16)
    count = q_state.shape[1]
    q_next, up, down = pl.pallas_call(
        functools.partial(update_kernel, groups16=groups16, slots16=slots16),
        out_shape=(
            jax.ShapeDtypeStruct((3, count), jnp.float32),
            jax.ShapeDtypeStruct((3, 3 * slots16, 128), jnp.float32),
            jax.ShapeDtypeStruct((3, 3 * slots16, 128), jnp.float32),
        ),
        scratch_shapes=[pltpu.VMEM((CHUNK, CHUNK), jnp.bfloat16)],
        cost_estimate=pl.CostEstimate(
            flops=2 * 3 * (5 * groups16 + 6 * slots16) * 128 * count,
            transcendentals=0,
            bytes_accessed=40 * count,
        ),
    )(q_state, increments, element.reshape(1, -1), migration.reshape(1, -1), pieces)

    def unpack(acc):
        whole = acc[0] + acc[1] + acc[2]
        return whole.reshape(3, slots16, 128)[:, :slots].reshape(3, slots * 128)

    return q_next, unpack(up), unpack(down)


def passed_along(array, axis, by):
    size = lax.axis_size(axis)
    pairs = [(i, i + by) for i in range(size) if 0 <= i + by < size]
    return lax.ppermute(array, axis, pairs)


def body(
    q_state,
    increments,
    velocity_grad,
    element,
    migration,
    volume,
    div_map,
    stiffness,
    pattern,
    preconditioner,
):
    capacity = migration.shape[0] // 16
    slab_elems = velocity_grad.shape[1]
    n_slab = lax.axis_size("slab")
    slab = lax.axis_index("slab")

    n_rad = lax.axis_size("rad")
    near = stress_partials(q_state, element, migration, slab_elems)
    near = near.reshape(4, 3, n_rad, slab_elems // n_rad).transpose(1, 2, 0, 3)
    spread = jnp.zeros((n_slab + 2,) + near.shape[1:], jnp.float32)
    spread = lax.dynamic_update_slice(spread, near, (slab, 0, 0, 0))
    spread = spread[1 : n_slab + 1].reshape((n_slab * n_rad,) + near.shape[2:])
    received = lax.all_to_all(spread, ("slab", "rad"), 0, 0, tiled=True)
    sums = jnp.sum(received, axis=0)
    element_stress = sums / volume

    q_next, upward, downward = update_and_pack(
        q_state, increments, element, migration, velocity_grad, capacity
    )
    from_lower = passed_along(upward, "slab", 1)
    from_upper = passed_along(downward, "slab", -1)
    arrivals = jnp.stack([from_lower, from_upper])

    own_blocks = stiffness.shape[0]
    groups = (
        element_stress.reshape(4, own_blocks, BLOCK // 4)
        .transpose(1, 0, 2)
        .reshape(own_blocks, BLOCK)
    )
    force = jnp.dot(groups, div_map, precision=highest)

    def precondition(vector):
        return jnp.einsum("bij,bj->bi", preconditioner, vector, precision=highest)

    slab_blocks = own_blocks * lax.axis_size("rad")
    all_blocks = slab_blocks * n_slab
    where_read = (slab - 1) * slab_blocks + pattern.reshape(-1)
    selector = (
        where_read[:, None] == jnp.arange(all_blocks, dtype=jnp.int32)[None, :]
    ).astype(jnp.float32)
    velocity = damping * precondition(force)
    for sweep_index in range(1, ITERS):
        gathered = lax.all_to_all(
            jnp.tile(velocity, (n_slab * n_rad, 1)), ("slab", "rad"), 0, 0, tiled=True
        )
        neighbours = jnp.dot(selector, gathered, precision=highest).reshape(own_blocks, -1, BLOCK)
        image = jnp.einsum("bnij,bnj->bi", stiffness, neighbours, precision=highest)
        velocity = velocity + damping * precondition(force - image)
    return (q_next, arrivals, element_stress, velocity)


def solution(mesh):
    placed = (
        P(None, ("slab", "rad")),
        P(None, ("slab", "rad")),
        P(None, "slab"),
        P(("slab", "rad")),
        P(("slab", "rad")),
        P(("slab", "rad")),
        P(),
        P(("slab", "rad"), None, None, None),
        P(("slab", "rad"), None),
        P(("slab", "rad"), None, None),
    )
    return jax.shard_map(
        body,
        mesh=mesh,
        in_specs=placed,
        out_specs=(
            P(None, ("slab", "rad")),
            P(None, None, ("slab", "rad")),
            P(None, ("slab", "rad")),
            P(("slab", "rad"), None),
        ),
        check_vma=False,
    )
```

```python
import functools

import jax
import jax.numpy as jnp
from jax import lax
from jax.experimental import pallas as pl
from jax.experimental.pallas import tpu as pltpu
from jax.sharding import PartitionSpec as P

BLOCK = 192
ITERS = 6
CHUNK = 512

extensibility = 50.0
time_step = 0.01
noise_scale = 0.1
damping = 0.6
highest = lax.Precision.HIGHEST
nt_dims = (((1,), (1,)), ((), ()))


def round_up(value, step):
    return -(-value // step) * step


def bf16_pieces(x):
    hi = x.astype(jnp.bfloat16)
    rest = x - hi.astype(jnp.float32)
    mid = rest.astype(jnp.bfloat16)
    lo = (rest - mid.astype(jnp.float32)).astype(jnp.bfloat16)
    return (hi, mid, lo)


def spring_terms(q):
    radial = q[0:1]
    axial = q[1:2]
    azimuth = q[2:3]
    stretch = radial * radial + axial * axial + azimuth * azimuth
    spring = 1.0 / (1.0 - stretch / extensibility)
    terms = (
        spring * radial * radial - 1.0,
        spring * axial * axial - 1.0,
        spring * radial * axial,
        spring * azimuth * azimuth - 1.0,
    )
    return spring, terms


def stress_kernel(q_ref, e_ref, m_ref, out_ref, *, groups, rows):
    count = q_ref.shape[1]
    out_ref[...] = jnp.zeros_like(out_ref)
    low_iota = lax.broadcasted_iota(jnp.int32, (128, CHUNK), 0)
    row_iota = lax.broadcasted_iota(jnp.int32, (rows, CHUNK), 0)
    zero = jnp.zeros((), jnp.bfloat16)

    def body(step, carry):
        cols = pl.ds(pl.multiple_of(step * CHUNK, CHUNK), CHUNK)
        q = q_ref[:, cols]
        element = e_ref[:, cols]
        move = m_ref[:, cols]
        spring, terms = spring_terms(q)
        kind = jnp.where(move == 0, 1, jnp.where(move == 1, 2, 0))
        key = kind * groups + (element >> 7)
        low = (low_iota == (element & 127)).astype(jnp.bfloat16)
        mask = row_iota == key
        pieces = [bf16_pieces(term) for term in terms]
        for p in range(3):
            spread = jnp.concatenate(
                [jnp.where(mask, pieces[c][p], zero) for c in range(4)], axis=0
            )
            out_ref[p] += lax.dot_general(
                spread, low, nt_dims, preferred_element_type=jnp.float32
            )
        return carry

    lax.fori_loop(0, count // CHUNK, body, 0)


def update_kernel(
    q_ref, inc_ref, e_ref, m_ref, tab_ref, qn_ref, up_ref, dn_ref, tri_ref, *, groups16, slots16
):
    count = q_ref.shape[1]
    up_ref[...] = jnp.zeros_like(up_ref)
    dn_ref[...] = jnp.zeros_like(dn_ref)
    before = lax.broadcasted_iota(jnp.int32, (CHUNK, CHUNK), 0)
    after = lax.broadcasted_iota(jnp.int32, (CHUNK, CHUNK), 1)
    tri_ref[...] = (before < after).astype(jnp.bfloat16)
    low_iota = lax.broadcasted_iota(jnp.int32, (128, CHUNK), 0)
    group_iota = lax.broadcasted_iota(jnp.int32, (groups16, CHUNK), 0)
    slot_iota = lax.broadcasted_iota(jnp.int32, (slots16, CHUNK), 0)
    flag_row = lax.broadcasted_iota(jnp.int32, (8, CHUNK), 0)
    zero = jnp.zeros((), jnp.bfloat16)

    def body(step, offsets):
        cols = pl.ds(pl.multiple_of(step * CHUNK, CHUNK), CHUNK)
        q = q_ref[:, cols]
        inc = inc_ref[:, cols]
        element = e_ref[:, cols]
        move = m_ref[:, cols]
        low = (low_iota == (element & 127)).astype(jnp.bfloat16)
        picked = jnp.dot(tab_ref[0], low, preferred_element_type=jnp.float32)
        picked = picked + jnp.dot(tab_ref[1], low, preferred_element_type=jnp.float32)
        picked = picked + jnp.dot(tab_ref[2], low, preferred_element_type=jnp.float32)
        hit = group_iota == (element >> 7)
        grads = [
            jnp.sum(
                jnp.where(hit, picked[c * groups16 : (c + 1) * groups16], 0.0),
                axis=0,
                keepdims=True,
            )
            for c in range(5)
        ]
        radial = q[0:1]
        axial = q[1:2]
        azimuth = q[2:3]
        spring, terms = spring_terms(q)
        drift = (
            grads[0] * radial + grads[1] * axial,
            grads[2] * radial + grads[3] * axial,
            grads[4] * azimuth,
        )
        q_next = [
            q[k : k + 1] + time_step * (drift[k] - 0.5 * spring * q[k : k + 1]) + noise_scale * inc[k : k + 1]
            for k in range(3)
        ]
        qn_ref[:, cols] = jnp.concatenate(q_next, axis=0)
        going_up = move == 1
        going_down = move == -1
        flags = jnp.where(
            flag_row == 0,
            going_up.astype(jnp.float32),
            jnp.where(flag_row == 1, going_down.astype(jnp.float32), 0.0),
        )
        ranks = jnp.dot(flags.astype(jnp.bfloat16), tri_ref[...], preferred_element_type=jnp.float32)
        slots = (ranks + offsets).astype(jnp.int32)
        pieces = [bf16_pieces(value) for value in q_next]
        for direction, chosen, out_ref in ((0, going_up, up_ref), (1, going_down, dn_ref)):
            slot = slots[direction : direction + 1]
            place = ((low_iota == (slot & 127)) & chosen).astype(jnp.bfloat16)
            which = slot_iota == (slot >> 7)
            for p in range(3):
                spread = jnp.concatenate(
                    [jnp.where(which, pieces[k][p], zero) for k in range(3)], axis=0
                )
                out_ref[p] += lax.dot_general(
                    spread, place, nt_dims, preferred_element_type=jnp.float32
                )
        return offsets + jnp.sum(flags, axis=1, keepdims=True)

    lax.fori_loop(0, count // CHUNK, body, jnp.zeros((8, 1), jnp.float32))


def stress_partials(q_state, element, migration, slab_elems):
    groups = slab_elems // 128
    rows = round_up(3 * groups, 16)
    count = q_state.shape[1]
    out = pl.pallas_call(
        functools.partial(stress_kernel, groups=groups, rows=rows),
        out_shape=jax.ShapeDtypeStruct((3, 4 * rows, 128), jnp.float32),
        cost_estimate=pl.CostEstimate(
            flops=2 * 3 * 4 * rows * 128 * count, transcendentals=0, bytes_accessed=20 * count
        ),
    )(q_state, element.reshape(1, -1), migration.reshape(1, -1))
    total = out[0] + out[1] + out[2]
    total = total.reshape(4, rows, 128)[:, : 3 * groups].reshape(4, 3 * slab_elems)
    return total


def update_and_pack(q_state, increments, element, migration, table, capacity):
    rows, slab_elems = table.shape
    groups = slab_elems // 128
    groups16 = round_up(groups, 16)
    slots = capacity // 128
    slots16 = round_up(slots, 16)
    arranged = jnp.pad(table.reshape(rows, groups, 128), ((0, 0), (0, groups16 - groups), (0, 0)))
    arranged = arranged.reshape(rows * groups16, 128)
    hi = lax.reduce_precision(arranged, exponent_bits=8, mantissa_bits=7)
    rest = arranged - hi
    mid = lax.reduce_precision(rest, exponent_bits=8, mantissa_bits=7)
    lo = rest - mid
    pieces = jnp.stack([hi, mid, lo]).astype(jnp.bfloat16)
    count = q_state.shape[1]
    q_next, up, down = pl.pallas_call(
        functools.partial(update_kernel, groups16=groups16, slots16=slots16),
        out_shape=(
            jax.ShapeDtypeStruct((3, count), jnp.float32),
            jax.ShapeDtypeStruct((3, 3 * slots16, 128), jnp.float32),
            jax.ShapeDtypeStruct((3, 3 * slots16, 128), jnp.float32),
        ),
        scratch_shapes=[pltpu.VMEM((CHUNK, CHUNK), jnp.bfloat16)],
        cost_estimate=pl.CostEstimate(
            flops=2 * 3 * (5 * groups16 + 6 * slots16) * 128 * count,
            transcendentals=0,
            bytes_accessed=40 * count,
        ),
    )(q_state, increments, element.reshape(1, -1), migration.reshape(1, -1), pieces)

    def unpack(acc):
        whole = acc[0] + acc[1] + acc[2]
        return whole.reshape(3, slots16, 128)[:, :slots].reshape(3, slots * 128)

    return q_next, unpack(up), unpack(down)


def sweep_kernel(idx_ref, g_ref, s_ref, pt_ref, ft_ref, v_ref, vout_ref, send_ref):
    total = g_ref.shape[0]
    own = v_ref.shape[0]
    width = s_ref.shape[1]
    rows = []
    for b in range(own):
        acc = None
        for n in range(width):
            w = idx_ref[b * width + n]
            inside = jnp.logical_and(w >= 0, w < total)
            near = g_ref[pl.ds(jnp.clip(w, 0, total - 1), 1), :]
            near = jnp.where(inside, near, 0.0)
            term = s_ref[b, n] * near
            acc = term if acc is None else acc + term
        image = jnp.sum(acc, axis=1, keepdims=True)
        rest = ft_ref[:, b : b + 1] - image
        update = jnp.sum(pt_ref[b] * rest, axis=0, keepdims=True)
        rows.append(v_ref[b : b + 1, :] + damping * update)
    fresh = jnp.concatenate(rows, axis=0)
    vout_ref[...] = fresh
    for k in range(send_ref.shape[0] // own):
        send_ref[k * own : (k + 1) * own, :] = fresh


def sweep(where_read, gathered, stiffness, transposed, force_t, velocity, copies):
    own = velocity.shape[0]
    vmem = pl.BlockSpec(memory_space=pltpu.VMEM)
    return pl.pallas_call(
        sweep_kernel,
        out_shape=(
            jax.ShapeDtypeStruct(velocity.shape, jnp.float32),
            jax.ShapeDtypeStruct((copies * own, velocity.shape[1]), jnp.float32),
        ),
        in_specs=[pl.BlockSpec(memory_space=pltpu.SMEM)] + [vmem] * 5,
        out_specs=(vmem, vmem),
        cost_estimate=pl.CostEstimate(
            flops=2 * (stiffness.size + transposed.size),
            transcendentals=0,
            bytes_accessed=4 * (stiffness.size + transposed.size + gathered.size),
        ),
    )(where_read, gathered, stiffness, transposed, force_t, velocity)


def passed_along(array, axis, by):
    size = lax.axis_size(axis)
    pairs = [(i, i + by) for i in range(size) if 0 <= i + by < size]
    return lax.ppermute(array, axis, pairs)


def body(
    q_state,
    increments,
    velocity_grad,
    element,
    migration,
    volume,
    div_map,
    stiffness,
    pattern,
    preconditioner,
):
    capacity = migration.shape[0] // 16
    slab_elems = velocity_grad.shape[1]
    n_slab = lax.axis_size("slab")
    slab = lax.axis_index("slab")

    n_rad = lax.axis_size("rad")
    near = stress_partials(q_state, element, migration, slab_elems)
    near = near.reshape(4, 3, n_rad, slab_elems // n_rad).transpose(1, 2, 0, 3)
    spread = jnp.zeros((n_slab + 2,) + near.shape[1:], jnp.float32)
    spread = lax.dynamic_update_slice(spread, near, (slab, 0, 0, 0))
    spread = spread[1 : n_slab + 1].reshape((n_slab * n_rad,) + near.shape[2:])
    received = lax.all_to_all(spread, ("slab", "rad"), 0, 0, tiled=True)
    sums = jnp.sum(received, axis=0)
    element_stress = sums / volume

    q_next, upward, downward = update_and_pack(
        q_state, increments, element, migration, velocity_grad, capacity
    )
    from_lower = passed_along(upward, "slab", 1)
    from_upper = passed_along(downward, "slab", -1)
    arrivals = jnp.stack([from_lower, from_upper])

    own_blocks = stiffness.shape[0]
    groups = (
        element_stress.reshape(4, own_blocks, BLOCK // 4)
        .transpose(1, 0, 2)
        .reshape(own_blocks, BLOCK)
    )
    force = jnp.dot(groups, div_map, precision=highest)

    def precondition(vector):
        return jnp.einsum("bij,bj->bi", preconditioner, vector, precision=highest)

    slab_blocks = own_blocks * n_rad
    copies = n_slab * n_rad
    where_read = ((slab - 1) * slab_blocks + pattern).reshape(-1).astype(jnp.int32)
    transposed = jnp.swapaxes(preconditioner, 1, 2)
    force_t = force.T
    velocity = damping * precondition(force)
    send = jnp.tile(velocity, (copies, 1))
    for sweep_index in range(1, ITERS):
        gathered = lax.all_to_all(send, ("slab", "rad"), 0, 0, tiled=True)
        velocity, send = sweep(
            where_read, gathered, stiffness, transposed, force_t, velocity, copies
        )
    return (q_next, arrivals, element_stress, velocity)


def solution(mesh):
    placed = (
        P(None, ("slab", "rad")),
        P(None, ("slab", "rad")),
        P(None, "slab"),
        P(("slab", "rad")),
        P(("slab", "rad")),
        P(("slab", "rad")),
        P(),
        P(("slab", "rad"), None, None, None),
        P(("slab", "rad"), None),
        P(("slab", "rad"), None, None),
    )
    return jax.shard_map(
        body,
        mesh=mesh,
        in_specs=placed,
        out_specs=(
            P(None, ("slab", "rad")),
            P(None, None, ("slab", "rad")),
            P(None, ("slab", "rad")),
            P(("slab", "rad"), None),
        ),
        check_vma=False,
    )
```

```python
import functools

import jax
import jax.numpy as jnp
from jax import lax
from jax.experimental import pallas as pl
from jax.experimental.pallas import tpu as pltpu
from jax.sharding import PartitionSpec as P

BLOCK = 192
ITERS = 6
CHUNK = 512
UPDATE_PARTS = 4

extensibility = 50.0
time_step = 0.01
noise_scale = 0.1
damping = 0.6
highest = lax.Precision.HIGHEST
nt_dims = (((1,), (1,)), ((), ()))


def round_up(value, step):
    return -(-value // step) * step


def bf16_pieces(x):
    hi = x.astype(jnp.bfloat16)
    rest = x - hi.astype(jnp.float32)
    mid = rest.astype(jnp.bfloat16)
    lo = (rest - mid.astype(jnp.float32)).astype(jnp.bfloat16)
    return (hi, mid, lo)


def spring_terms(q):
    radial = q[0:1]
    axial = q[1:2]
    azimuth = q[2:3]
    stretch = radial * radial + axial * axial + azimuth * azimuth
    spring = 1.0 / (1.0 - stretch / extensibility)
    terms = (
        spring * radial * radial - 1.0,
        spring * axial * axial - 1.0,
        spring * radial * axial,
        spring * azimuth * azimuth - 1.0,
    )
    return spring, terms


def stress_kernel(q_ref, e_ref, m_ref, out_ref, *, groups, rows):
    count = q_ref.shape[1]
    out_ref[...] = jnp.zeros_like(out_ref)
    low_iota = lax.broadcasted_iota(jnp.int32, (128, CHUNK), 0)
    row_iota = lax.broadcasted_iota(jnp.int32, (rows, CHUNK), 0)
    zero = jnp.zeros((), jnp.bfloat16)

    def body(step, carry):
        cols = pl.ds(pl.multiple_of(step * CHUNK, CHUNK), CHUNK)
        q = q_ref[:, cols]
        element = e_ref[:, cols]
        move = m_ref[:, cols]
        spring, terms = spring_terms(q)
        kind = jnp.where(move == 0, 1, jnp.where(move == 1, 2, 0))
        key = kind * groups + (element >> 7)
        low = (low_iota == (element & 127)).astype(jnp.bfloat16)
        mask = row_iota == key
        pieces = [bf16_pieces(term) for term in terms]
        for p in range(3):
            spread = jnp.concatenate(
                [jnp.where(mask, pieces[c][p], zero) for c in range(4)], axis=0
            )
            out_ref[p] += lax.dot_general(
                spread, low, nt_dims, preferred_element_type=jnp.float32
            )
        return carry

    lax.fori_loop(0, count // CHUNK, body, 0)


def update_kernel(
    q_ref, inc_ref, e_ref, m_ref, tab_ref, start_ref, qn_ref, up_ref, dn_ref, tri_ref, *, groups16, slots16, first
):
    count = qn_ref.shape[1]
    up_ref[...] = jnp.zeros_like(up_ref)
    dn_ref[...] = jnp.zeros_like(dn_ref)
    before = lax.broadcasted_iota(jnp.int32, (CHUNK, CHUNK), 0)
    after = lax.broadcasted_iota(jnp.int32, (CHUNK, CHUNK), 1)
    tri_ref[...] = (before < after).astype(jnp.bfloat16)
    low_iota = lax.broadcasted_iota(jnp.int32, (128, CHUNK), 0)
    group_iota = lax.broadcasted_iota(jnp.int32, (groups16, CHUNK), 0)
    slot_iota = lax.broadcasted_iota(jnp.int32, (slots16, CHUNK), 0)
    flag_row = lax.broadcasted_iota(jnp.int32, (8, CHUNK), 0)
    zero = jnp.zeros((), jnp.bfloat16)

    def body(step, offsets):
        cols = pl.ds(pl.multiple_of((first + step) * CHUNK, CHUNK), CHUNK)
        q = q_ref[:, cols]
        inc = inc_ref[:, cols]
        element = e_ref[:, cols]
        move = m_ref[:, cols]
        low = (low_iota == (element & 127)).astype(jnp.bfloat16)
        picked = jnp.dot(tab_ref[0], low, preferred_element_type=jnp.float32)
        picked = picked + jnp.dot(tab_ref[1], low, preferred_element_type=jnp.float32)
        picked = picked + jnp.dot(tab_ref[2], low, preferred_element_type=jnp.float32)
        hit = group_iota == (element >> 7)
        grads = [
            jnp.sum(
                jnp.where(hit, picked[c * groups16 : (c + 1) * groups16], 0.0),
                axis=0,
                keepdims=True,
            )
            for c in range(5)
        ]
        radial = q[0:1]
        axial = q[1:2]
        azimuth = q[2:3]
        spring, terms = spring_terms(q)
        drift = (
            grads[0] * radial + grads[1] * axial,
            grads[2] * radial + grads[3] * axial,
            grads[4] * azimuth,
        )
        q_next = [
            q[k : k + 1] + time_step * (drift[k] - 0.5 * spring * q[k : k + 1]) + noise_scale * inc[k : k + 1]
            for k in range(3)
        ]
        qn_ref[:, pl.ds(pl.multiple_of(step * CHUNK, CHUNK), CHUNK)] = jnp.concatenate(q_next, axis=0)
        going_up = move == 1
        going_down = move == -1
        flags = jnp.where(
            flag_row == 0,
            going_up.astype(jnp.float32),
            jnp.where(flag_row == 1, going_down.astype(jnp.float32), 0.0),
        )
        ranks = jnp.dot(flags.astype(jnp.bfloat16), tri_ref[...], preferred_element_type=jnp.float32)
        slots = (ranks + offsets).astype(jnp.int32)
        pieces = [bf16_pieces(value) for value in q_next]
        for direction, chosen, out_ref in ((0, going_up, up_ref), (1, going_down, dn_ref)):
            slot = slots[direction : direction + 1]
            place = ((low_iota == (slot & 127)) & chosen).astype(jnp.bfloat16)
            which = slot_iota == (slot >> 7)
            for p in range(3):
                spread = jnp.concatenate(
                    [jnp.where(which, pieces[k][p], zero) for k in range(3)], axis=0
                )
                out_ref[p] += lax.dot_general(
                    spread, place, nt_dims, preferred_element_type=jnp.float32
                )
        return offsets + jnp.sum(flags, axis=1, keepdims=True)

    lax.fori_loop(0, count // CHUNK, body, start_ref[...])


def stress_partials(q_state, element, migration, slab_elems):
    groups = slab_elems // 128
    rows = round_up(3 * groups, 16)
    count = q_state.shape[1]
    out = pl.pallas_call(
        functools.partial(stress_kernel, groups=groups, rows=rows),
        out_shape=jax.ShapeDtypeStruct((3, 4 * rows, 128), jnp.float32),
        cost_estimate=pl.CostEstimate(
            flops=2 * 3 * 4 * rows * 128 * count, transcendentals=0, bytes_accessed=20 * count
        ),
    )(q_state, element.reshape(1, -1), migration.reshape(1, -1))
    total = out[0] + out[1] + out[2]
    total = total.reshape(4, rows, 128)[:, : 3 * groups].reshape(4, 3 * slab_elems)
    return total


def update_and_pack(q_state, increments, element, migration, table, capacity):
    rows, slab_elems = table.shape
    groups = slab_elems // 128
    groups16 = round_up(groups, 16)
    slots = capacity // 128
    slots16 = round_up(slots, 16)
    arranged = jnp.pad(table.reshape(rows, groups, 128), ((0, 0), (0, groups16 - groups), (0, 0)))
    arranged = arranged.reshape(rows * groups16, 128)
    hi = lax.reduce_precision(arranged, exponent_bits=8, mantissa_bits=7)
    rest = arranged - hi
    mid = lax.reduce_precision(rest, exponent_bits=8, mantissa_bits=7)
    lo = rest - mid
    pieces = jnp.stack([hi, mid, lo]).astype(jnp.bfloat16)
    count = q_state.shape[1]
    parts = UPDATE_PARTS
    share = count // parts
    flags = jnp.stack([migration == 1, migration == -1]).astype(jnp.float32)
    per_part = jnp.sum(flags.reshape(2, parts, share), axis=2)
    starts = jnp.cumsum(per_part, axis=1) - per_part
    starts = jnp.pad(starts.T, ((0, 0), (0, 6)))[:, :, None]
    q_parts, up, down = [], 0.0, 0.0
    for part in range(parts):
        q_part, up_part, down_part = pl.pallas_call(
            functools.partial(
                update_kernel, groups16=groups16, slots16=slots16, first=part * share // CHUNK
            ),
            out_shape=(
                jax.ShapeDtypeStruct((3, share), jnp.float32),
                jax.ShapeDtypeStruct((3, 3 * slots16, 128), jnp.float32),
                jax.ShapeDtypeStruct((3, 3 * slots16, 128), jnp.float32),
            ),
            scratch_shapes=[pltpu.VMEM((CHUNK, CHUNK), jnp.bfloat16)],
            cost_estimate=pl.CostEstimate(
                flops=16 * 3 * (5 * groups16 + 6 * slots16) * 128 * share,
                transcendentals=0,
                bytes_accessed=40 * share,
            ),
        )(
            q_state,
            increments,
            element.reshape(1, -1),
            migration.reshape(1, -1),
            pieces,
            starts[part],
        )
        q_parts.append(q_part)
        up = up + up_part
        down = down + down_part
    q_next = jnp.concatenate(q_parts, axis=1)

    def unpack(acc):
        whole = acc[0] + acc[1] + acc[2]
        return whole.reshape(3, slots16, 128)[:, :slots].reshape(3, slots * 128)

    return q_next, unpack(up), unpack(down)


def sweep_kernel(idx_ref, g_ref, s_ref, pt_ref, ft_ref, v_ref, vout_ref, send_ref):
    total = g_ref.shape[0]
    own = v_ref.shape[0]
    width = s_ref.shape[1]
    rows = []
    for b in range(own):
        acc = None
        for n in range(width):
            w = idx_ref[b * width + n]
            inside = jnp.logical_and(w >= 0, w < total)
            near = g_ref[pl.ds(jnp.clip(w, 0, total - 1), 1), :]
            near = jnp.where(inside, near, 0.0)
            term = s_ref[b, n] * near
            acc = term if acc is None else acc + term
        image = jnp.sum(acc, axis=1, keepdims=True)
        rest = ft_ref[:, b : b + 1] - image
        update = jnp.sum(pt_ref[b] * rest, axis=0, keepdims=True)
        rows.append(v_ref[b : b + 1, :] + damping * update)
    fresh = jnp.concatenate(rows, axis=0)
    vout_ref[...] = fresh
    for k in range(send_ref.shape[0] // own):
        send_ref[k * own : (k + 1) * own, :] = fresh


def sweep(where_read, gathered, stiffness, transposed, force_t, velocity, copies):
    own = velocity.shape[0]
    vmem = pl.BlockSpec(memory_space=pltpu.VMEM)
    return pl.pallas_call(
        sweep_kernel,
        out_shape=(
            jax.ShapeDtypeStruct(velocity.shape, jnp.float32),
            jax.ShapeDtypeStruct((copies * own, velocity.shape[1]), jnp.float32),
        ),
        in_specs=[pl.BlockSpec(memory_space=pltpu.SMEM)] + [vmem] * 5,
        out_specs=(vmem, vmem),
        cost_estimate=pl.CostEstimate(
            flops=2 * (stiffness.size + transposed.size),
            transcendentals=0,
            bytes_accessed=4 * (stiffness.size + transposed.size + gathered.size),
        ),
    )(where_read, gathered, stiffness, transposed, force_t, velocity)


def passed_along(array, axis, by):
    size = lax.axis_size(axis)
    pairs = [(i, i + by) for i in range(size) if 0 <= i + by < size]
    return lax.ppermute(array, axis, pairs)


def body(
    q_state,
    increments,
    velocity_grad,
    element,
    migration,
    volume,
    div_map,
    stiffness,
    pattern,
    preconditioner,
):
    capacity = migration.shape[0] // 16
    slab_elems = velocity_grad.shape[1]
    n_slab = lax.axis_size("slab")
    slab = lax.axis_index("slab")

    n_rad = lax.axis_size("rad")
    near = stress_partials(q_state, element, migration, slab_elems)
    near = near.reshape(4, 3, n_rad, slab_elems // n_rad).transpose(1, 2, 0, 3)
    spread = jnp.zeros((n_slab + 2,) + near.shape[1:], jnp.float32)
    spread = lax.dynamic_update_slice(spread, near, (slab, 0, 0, 0))
    spread = spread[1 : n_slab + 1].reshape((n_slab * n_rad,) + near.shape[2:])
    received = lax.all_to_all(spread, ("slab", "rad"), 0, 0, tiled=True)
    sums = jnp.sum(received, axis=0)
    element_stress = sums / volume

    q_next, upward, downward = update_and_pack(
        q_state, increments, element, migration, velocity_grad, capacity
    )
    from_lower = passed_along(upward, "slab", 1)
    from_upper = passed_along(downward, "slab", -1)
    arrivals = jnp.stack([from_lower, from_upper])

    own_blocks = stiffness.shape[0]
    groups = (
        element_stress.reshape(4, own_blocks, BLOCK // 4)
        .transpose(1, 0, 2)
        .reshape(own_blocks, BLOCK)
    )
    force = jnp.dot(groups, div_map, precision=highest)

    def precondition(vector):
        return jnp.einsum("bij,bj->bi", preconditioner, vector, precision=highest)

    slab_blocks = own_blocks * n_rad
    copies = n_slab * n_rad
    where_read = ((slab - 1) * slab_blocks + pattern).reshape(-1).astype(jnp.int32)
    transposed = jnp.swapaxes(preconditioner, 1, 2)
    force_t = force.T
    velocity = damping * precondition(force)
    send = jnp.tile(velocity, (copies, 1))
    for sweep_index in range(1, ITERS):
        gathered = lax.all_to_all(send, ("slab", "rad"), 0, 0, tiled=True)
        velocity, send = sweep(
            where_read, gathered, stiffness, transposed, force_t, velocity, copies
        )
    return (q_next, arrivals, element_stress, velocity)


def solution(mesh):
    placed = (
        P(None, ("slab", "rad")),
        P(None, ("slab", "rad")),
        P(None, "slab"),
        P(("slab", "rad")),
        P(("slab", "rad")),
        P(("slab", "rad")),
        P(),
        P(("slab", "rad"), None, None, None),
        P(("slab", "rad"), None),
        P(("slab", "rad"), None, None),
    )
    return jax.shard_map(
        body,
        mesh=mesh,
        in_specs=placed,
        out_specs=(
            P(None, ("slab", "rad")),
            P(None, None, ("slab", "rad")),
            P(None, ("slab", "rad")),
            P(("slab", "rad"), None),
        ),
        check_vma=False,
    )
```

```python
import functools

import jax
import jax.numpy as jnp
from jax import lax
from jax.experimental import pallas as pl
from jax.experimental.pallas import tpu as pltpu
from jax.sharding import PartitionSpec as P

BLOCK = 192
ITERS = 6
CHUNK = 512
STRESS_CHUNK = 1024
UPDATE_PARTS = 4

extensibility = 50.0
time_step = 0.01
noise_scale = 0.1
damping = 0.6
highest = lax.Precision.HIGHEST
nt_dims = (((1,), (1,)), ((), ()))


def round_up(value, step):
    return -(-value // step) * step


def bf16_pieces(x):
    hi = x.astype(jnp.bfloat16)
    rest = x - hi.astype(jnp.float32)
    mid = rest.astype(jnp.bfloat16)
    lo = (rest - mid.astype(jnp.float32)).astype(jnp.bfloat16)
    return (hi, mid, lo)


def spring_terms(q):
    radial = q[0:1]
    axial = q[1:2]
    azimuth = q[2:3]
    stretch = radial * radial + axial * axial + azimuth * azimuth
    spring = 1.0 / (1.0 - stretch / extensibility)
    terms = (
        spring * radial * radial - 1.0,
        spring * axial * axial - 1.0,
        spring * radial * axial,
        spring * azimuth * azimuth - 1.0,
    )
    return spring, terms


def stress_kernel(q_ref, e_ref, m_ref, out_ref, *, groups, rows):
    count = q_ref.shape[1]
    out_ref[...] = jnp.zeros_like(out_ref)
    low_iota = lax.broadcasted_iota(jnp.int32, (128, STRESS_CHUNK), 0)
    row_iota = lax.broadcasted_iota(jnp.int32, (rows, STRESS_CHUNK), 0)
    zero = jnp.zeros((), jnp.bfloat16)

    def body(step, carry):
        cols = pl.ds(pl.multiple_of(step * STRESS_CHUNK, STRESS_CHUNK), STRESS_CHUNK)
        q = q_ref[:, cols]
        element = e_ref[:, cols]
        move = m_ref[:, cols]
        spring, terms = spring_terms(q)
        kind = jnp.where(move == 0, 1, jnp.where(move == 1, 2, 0))
        key = kind * groups + (element >> 7)
        low = (low_iota == (element & 127)).astype(jnp.bfloat16)
        low = jnp.concatenate([low, low, low], axis=1)
        mask = row_iota == key
        spread = jnp.concatenate(
            [
                jnp.concatenate([jnp.where(mask, piece, zero) for piece in bf16_pieces(term)], axis=1)
                for term in terms
            ],
            axis=0,
        )
        out_ref[...] += lax.dot_general(spread, low, nt_dims, preferred_element_type=jnp.float32)
        return carry

    lax.fori_loop(0, count // STRESS_CHUNK, body, 0)


def update_kernel(
    q_ref, inc_ref, e_ref, m_ref, tab_ref, start_ref, qn_ref, up_ref, dn_ref, tri_ref, *, groups16, slots16, first
):
    count = qn_ref.shape[1]
    up_ref[...] = jnp.zeros_like(up_ref)
    dn_ref[...] = jnp.zeros_like(dn_ref)
    before = lax.broadcasted_iota(jnp.int32, (CHUNK, CHUNK), 0)
    after = lax.broadcasted_iota(jnp.int32, (CHUNK, CHUNK), 1)
    tri_ref[...] = (before < after).astype(jnp.bfloat16)
    low_iota = lax.broadcasted_iota(jnp.int32, (128, CHUNK), 0)
    group_iota = lax.broadcasted_iota(jnp.int32, (groups16, CHUNK), 0)
    slot_iota = lax.broadcasted_iota(jnp.int32, (slots16, CHUNK), 0)
    flag_row = lax.broadcasted_iota(jnp.int32, (8, CHUNK), 0)
    zero = jnp.zeros((), jnp.bfloat16)

    def body(step, offsets):
        cols = pl.ds(pl.multiple_of((first + step) * CHUNK, CHUNK), CHUNK)
        q = q_ref[:, cols]
        inc = inc_ref[:, cols]
        element = e_ref[:, cols]
        move = m_ref[:, cols]
        low = (low_iota == (element & 127)).astype(jnp.bfloat16)
        picked = jnp.dot(
            tab_ref[...], jnp.concatenate([low, low, low], axis=0), preferred_element_type=jnp.float32
        )
        hit = group_iota == (element >> 7)
        grads = [
            jnp.sum(
                jnp.where(hit, picked[c * groups16 : (c + 1) * groups16], 0.0),
                axis=0,
                keepdims=True,
            )
            for c in range(5)
        ]
        radial = q[0:1]
        axial = q[1:2]
        azimuth = q[2:3]
        spring, terms = spring_terms(q)
        drift = (
            grads[0] * radial + grads[1] * axial,
            grads[2] * radial + grads[3] * axial,
            grads[4] * azimuth,
        )
        q_next = [
            q[k : k + 1] + time_step * (drift[k] - 0.5 * spring * q[k : k + 1]) + noise_scale * inc[k : k + 1]
            for k in range(3)
        ]
        qn_ref[:, pl.ds(pl.multiple_of(step * CHUNK, CHUNK), CHUNK)] = jnp.concatenate(q_next, axis=0)
        going_up = move == 1
        going_down = move == -1
        flags = jnp.where(
            flag_row == 0,
            going_up.astype(jnp.float32),
            jnp.where(flag_row == 1, going_down.astype(jnp.float32), 0.0),
        )
        ranks = jnp.dot(flags.astype(jnp.bfloat16), tri_ref[...], preferred_element_type=jnp.float32)
        slots = (ranks + offsets).astype(jnp.int32)
        pieces = [bf16_pieces(value) for value in q_next]
        for direction, chosen, out_ref in ((0, going_up, up_ref), (1, going_down, dn_ref)):
            slot = slots[direction : direction + 1]
            place = ((low_iota == (slot & 127)) & chosen).astype(jnp.bfloat16)
            place = jnp.concatenate([place, place, place], axis=1)
            which = slot_iota == (slot >> 7)
            spread = jnp.concatenate(
                [
                    jnp.concatenate([jnp.where(which, piece, zero) for piece in pieces[k]], axis=1)
                    for k in range(3)
                ],
                axis=0,
            )
            out_ref[...] += lax.dot_general(spread, place, nt_dims, preferred_element_type=jnp.float32)
        return offsets + jnp.sum(flags, axis=1, keepdims=True)

    lax.fori_loop(0, count // CHUNK, body, start_ref[...])


def stress_partials(q_state, element, migration, slab_elems):
    groups = slab_elems // 128
    rows = round_up(3 * groups, 16)
    count = q_state.shape[1]
    out = pl.pallas_call(
        functools.partial(stress_kernel, groups=groups, rows=rows),
        out_shape=jax.ShapeDtypeStruct((4 * rows, 128), jnp.float32),
        cost_estimate=pl.CostEstimate(
            flops=2 * 3 * 4 * rows * 128 * count, transcendentals=0, bytes_accessed=20 * count
        ),
    )(q_state, element.reshape(1, -1), migration.reshape(1, -1))
    total = out.reshape(4, rows, 128)[:, : 3 * groups].reshape(4, 3 * slab_elems)
    return total


def update_and_pack(q_state, increments, element, migration, table, capacity):
    rows, slab_elems = table.shape
    groups = slab_elems // 128
    groups16 = round_up(groups, 16)
    slots = capacity // 128
    slots16 = round_up(slots, 16)
    arranged = jnp.pad(table.reshape(rows, groups, 128), ((0, 0), (0, groups16 - groups), (0, 0)))
    arranged = arranged.reshape(rows * groups16, 128)
    hi = lax.reduce_precision(arranged, exponent_bits=8, mantissa_bits=7)
    rest = arranged - hi
    mid = lax.reduce_precision(rest, exponent_bits=8, mantissa_bits=7)
    lo = rest - mid
    pieces = jnp.concatenate([hi, mid, lo], axis=1).astype(jnp.bfloat16)
    count = q_state.shape[1]
    parts = UPDATE_PARTS
    share = count // parts
    flags = jnp.stack([migration == 1, migration == -1]).astype(jnp.float32)
    per_part = jnp.sum(flags.reshape(2, parts, share), axis=2)
    starts = jnp.cumsum(per_part, axis=1) - per_part
    starts = jnp.pad(starts.T, ((0, 0), (0, 6)))[:, :, None]
    q_parts, up, down = [], 0.0, 0.0
    for part in range(parts):
        q_part, up_part, down_part = pl.pallas_call(
            functools.partial(
                update_kernel, groups16=groups16, slots16=slots16, first=part * share // CHUNK
            ),
            out_shape=(
                jax.ShapeDtypeStruct((3, share), jnp.float32),
                jax.ShapeDtypeStruct((3 * slots16, 128), jnp.float32),
                jax.ShapeDtypeStruct((3 * slots16, 128), jnp.float32),
            ),
            scratch_shapes=[pltpu.VMEM((CHUNK, CHUNK), jnp.bfloat16)],
            cost_estimate=pl.CostEstimate(
                flops=16 * 3 * (5 * groups16 + 6 * slots16) * 128 * share,
                transcendentals=0,
                bytes_accessed=40 * share,
            ),
        )(
            q_state,
            increments,
            element.reshape(1, -1),
            migration.reshape(1, -1),
            pieces,
            starts[part],
        )
        q_parts.append(q_part)
        up = up + up_part
        down = down + down_part
    q_next = jnp.concatenate(q_parts, axis=1)

    def unpack(acc):
        return acc.reshape(3, slots16, 128)[:, :slots].reshape(3, slots * 128)

    return q_next, unpack(up), unpack(down)


def sweep_kernel(idx_ref, g_ref, s_ref, pt_ref, ft_ref, v_ref, vout_ref, send_ref):
    total = g_ref.shape[0]
    own = v_ref.shape[0]
    width = s_ref.shape[1]
    rows = []
    for b in range(own):
        acc = None
        for n in range(width):
            w = idx_ref[b * width + n]
            inside = jnp.logical_and(w >= 0, w < total)
            near = g_ref[pl.ds(jnp.clip(w, 0, total - 1), 1), :]
            near = jnp.where(inside, near, 0.0)
            term = s_ref[b, n] * near
            acc = term if acc is None else acc + term
        image = jnp.sum(acc, axis=1, keepdims=True)
        rest = ft_ref[:, b : b + 1] - image
        update = jnp.sum(pt_ref[b] * rest, axis=0, keepdims=True)
        rows.append(v_ref[b : b + 1, :] + damping * update)
    fresh = jnp.concatenate(rows, axis=0)
    vout_ref[...] = fresh
    for k in range(send_ref.shape[0] // own):
        send_ref[k * own : (k + 1) * own, :] = fresh


def sweep(where_read, gathered, stiffness, transposed, force_t, velocity, copies):
    own = velocity.shape[0]
    vmem = pl.BlockSpec(memory_space=pltpu.VMEM)
    return pl.pallas_call(
        sweep_kernel,
        out_shape=(
            jax.ShapeDtypeStruct(velocity.shape, jnp.float32),
            jax.ShapeDtypeStruct((copies * own, velocity.shape[1]), jnp.float32),
        ),
        in_specs=[pl.BlockSpec(memory_space=pltpu.SMEM)] + [vmem] * 5,
        out_specs=(vmem, vmem),
        cost_estimate=pl.CostEstimate(
            flops=2 * (stiffness.size + transposed.size),
            transcendentals=0,
            bytes_accessed=4 * (stiffness.size + transposed.size + gathered.size),
        ),
    )(where_read, gathered, stiffness, transposed, force_t, velocity)


def passed_along(array, axis, by):
    size = lax.axis_size(axis)
    pairs = [(i, i + by) for i in range(size) if 0 <= i + by < size]
    return lax.ppermute(array, axis, pairs)


def body(
    q_state,
    increments,
    velocity_grad,
    element,
    migration,
    volume,
    div_map,
    stiffness,
    pattern,
    preconditioner,
):
    capacity = migration.shape[0] // 16
    slab_elems = velocity_grad.shape[1]
    n_slab = lax.axis_size("slab")
    slab = lax.axis_index("slab")

    n_rad = lax.axis_size("rad")
    near = stress_partials(q_state, element, migration, slab_elems)
    near = near.reshape(4, 3, n_rad, slab_elems // n_rad).transpose(1, 2, 0, 3)
    spread = jnp.zeros((n_slab + 2,) + near.shape[1:], jnp.float32)
    spread = lax.dynamic_update_slice(spread, near, (slab, 0, 0, 0))
    spread = spread[1 : n_slab + 1].reshape((n_slab * n_rad,) + near.shape[2:])
    received = lax.all_to_all(spread, ("slab", "rad"), 0, 0, tiled=True)
    sums = jnp.sum(received, axis=0)
    element_stress = sums / volume

    q_next, upward, downward = update_and_pack(
        q_state, increments, element, migration, velocity_grad, capacity
    )
    from_lower = passed_along(upward, "slab", 1)
    from_upper = passed_along(downward, "slab", -1)
    arrivals = jnp.stack([from_lower, from_upper])

    own_blocks = stiffness.shape[0]
    groups = (
        element_stress.reshape(4, own_blocks, BLOCK // 4)
        .transpose(1, 0, 2)
        .reshape(own_blocks, BLOCK)
    )
    force = jnp.dot(groups, div_map, precision=highest)

    def precondition(vector):
        return jnp.einsum("bij,bj->bi", preconditioner, vector, precision=highest)

    slab_blocks = own_blocks * n_rad
    copies = n_slab * n_rad
    where_read = ((slab - 1) * slab_blocks + pattern).reshape(-1).astype(jnp.int32)
    transposed = jnp.swapaxes(preconditioner, 1, 2)
    force_t = force.T
    velocity = damping * precondition(force)
    send = jnp.tile(velocity, (copies, 1))
    for sweep_index in range(1, ITERS):
        gathered = lax.all_to_all(send, ("slab", "rad"), 0, 0, tiled=True)
        velocity, send = sweep(
            where_read, gathered, stiffness, transposed, force_t, velocity, copies
        )
    return (q_next, arrivals, element_stress, velocity)


def solution(mesh):
    placed = (
        P(None, ("slab", "rad")),
        P(None, ("slab", "rad")),
        P(None, "slab"),
        P(("slab", "rad")),
        P(("slab", "rad")),
        P(("slab", "rad")),
        P(),
        P(("slab", "rad"), None, None, None),
        P(("slab", "rad"), None),
        P(("slab", "rad"), None, None),
    )
    return jax.shard_map(
        body,
        mesh=mesh,
        in_specs=placed,
        out_specs=(
            P(None, ("slab", "rad")),
            P(None, None, ("slab", "rad")),
            P(None, ("slab", "rad")),
            P(("slab", "rad"), None),
        ),
        check_vma=False,
    )
```

```python
import functools

import jax
import jax.numpy as jnp
from jax import lax
from jax.experimental import pallas as pl
from jax.experimental.pallas import tpu as pltpu
from jax.sharding import PartitionSpec as P

BLOCK = 192
ITERS = 6
CHUNK = 512
STRESS_CHUNK = 1024
UPDATE_PARTS = 4

extensibility = 50.0
time_step = 0.01
noise_scale = 0.1
damping = 0.6
highest = lax.Precision.HIGHEST
nt_dims = (((1,), (1,)), ((), ()))


def round_up(value, step):
    return -(-value // step) * step


def bf16_pieces(x):
    hi = x.astype(jnp.bfloat16)
    rest = x - hi.astype(jnp.float32)
    mid = rest.astype(jnp.bfloat16)
    lo = (rest - mid.astype(jnp.float32)).astype(jnp.bfloat16)
    return (hi, mid, lo)


def spring_terms(q):
    radial = q[0:1]
    axial = q[1:2]
    azimuth = q[2:3]
    stretch = radial * radial + axial * axial + azimuth * azimuth
    spring = 1.0 / (1.0 - stretch / extensibility)
    terms = (
        spring * radial * radial - 1.0,
        spring * axial * axial - 1.0,
        spring * radial * axial,
        spring * azimuth * azimuth - 1.0,
    )
    return spring, terms


def stress_kernel(q_ref, e_ref, m_ref, out_ref, *, groups, rows):
    count = q_ref.shape[1]
    out_ref[...] = jnp.zeros_like(out_ref)
    low_iota = lax.broadcasted_iota(jnp.int32, (128, STRESS_CHUNK), 0)
    row_iota = lax.broadcasted_iota(jnp.int32, (rows, STRESS_CHUNK), 0)
    zero = jnp.zeros((), jnp.bfloat16)

    def body(step, carry):
        cols = pl.ds(pl.multiple_of(step * STRESS_CHUNK, STRESS_CHUNK), STRESS_CHUNK)
        q = q_ref[:, cols]
        element = e_ref[:, cols]
        move = m_ref[:, cols]
        spring, terms = spring_terms(q)
        kind = jnp.where(move == 0, 1, jnp.where(move == 1, 2, 0))
        key = kind * groups + (element >> 7)
        low = (low_iota == (element & 127)).astype(jnp.bfloat16)
        low = jnp.concatenate([low, low, low], axis=1)
        mask = row_iota == key
        spread = jnp.concatenate(
            [
                jnp.concatenate([jnp.where(mask, piece, zero) for piece in bf16_pieces(term)], axis=1)
                for term in terms
            ],
            axis=0,
        )
        out_ref[...] += lax.dot_general(spread, low, nt_dims, preferred_element_type=jnp.float32)
        return carry

    lax.fori_loop(0, count // STRESS_CHUNK, body, 0)


def update_kernel(
    q_ref, inc_ref, e_ref, m_ref, tab_ref, start_ref, qn_ref, up_ref, dn_ref, tri_ref, *, groups16, slots16, first
):
    count = qn_ref.shape[1]
    up_ref[...] = jnp.zeros_like(up_ref)
    dn_ref[...] = jnp.zeros_like(dn_ref)
    before = lax.broadcasted_iota(jnp.int32, (CHUNK, CHUNK), 0)
    after = lax.broadcasted_iota(jnp.int32, (CHUNK, CHUNK), 1)
    tri_ref[...] = (before < after).astype(jnp.bfloat16)
    low_iota = lax.broadcasted_iota(jnp.int32, (128, CHUNK), 0)
    group_iota = lax.broadcasted_iota(jnp.int32, (groups16, CHUNK), 0)
    slot_iota = lax.broadcasted_iota(jnp.int32, (slots16, CHUNK), 0)
    flag_row = lax.broadcasted_iota(jnp.int32, (8, CHUNK), 0)
    zero = jnp.zeros((), jnp.bfloat16)

    def body(step, offsets):
        cols = pl.ds(pl.multiple_of((first + step) * CHUNK, CHUNK), CHUNK)
        q = q_ref[:, cols]
        inc = inc_ref[:, cols]
        element = e_ref[:, cols]
        move = m_ref[:, cols]
        low = (low_iota == (element & 127)).astype(jnp.bfloat16)
        picked = jnp.dot(
            tab_ref[...], jnp.concatenate([low, low, low], axis=0), preferred_element_type=jnp.float32
        )
        hit = group_iota == (element >> 7)
        grads = [
            jnp.sum(
                jnp.where(hit, picked[c * groups16 : (c + 1) * groups16], 0.0),
                axis=0,
                keepdims=True,
            )
            for c in range(5)
        ]
        radial = q[0:1]
        axial = q[1:2]
        azimuth = q[2:3]
        spring, terms = spring_terms(q)
        drift = (
            grads[0] * radial + grads[1] * axial,
            grads[2] * radial + grads[3] * axial,
            grads[4] * azimuth,
        )
        q_next = [
            q[k : k + 1] + time_step * (drift[k] - 0.5 * spring * q[k : k + 1]) + noise_scale * inc[k : k + 1]
            for k in range(3)
        ]
        qn_ref[:, pl.ds(pl.multiple_of(step * CHUNK, CHUNK), CHUNK)] = jnp.concatenate(q_next, axis=0)
        going_up = move == 1
        going_down = move == -1
        flags = jnp.where(
            flag_row == 0,
            going_up.astype(jnp.float32),
            jnp.where(flag_row == 1, going_down.astype(jnp.float32), 0.0),
        )
        ranks = jnp.dot(flags.astype(jnp.bfloat16), tri_ref[...], preferred_element_type=jnp.float32)
        slots = (ranks + offsets).astype(jnp.int32)
        pieces = [bf16_pieces(value) for value in q_next]
        for direction, chosen, out_ref in ((0, going_up, up_ref), (1, going_down, dn_ref)):
            slot = slots[direction : direction + 1]
            place = ((low_iota == (slot & 127)) & chosen).astype(jnp.bfloat16)
            place = jnp.concatenate([place, place, place], axis=1)
            which = slot_iota == (slot >> 7)
            spread = jnp.concatenate(
                [
                    jnp.concatenate([jnp.where(which, piece, zero) for piece in pieces[k]], axis=1)
                    for k in range(3)
                ],
                axis=0,
            )
            out_ref[...] += lax.dot_general(spread, place, nt_dims, preferred_element_type=jnp.float32)
        return offsets + jnp.sum(flags, axis=1, keepdims=True)

    lax.fori_loop(0, count // CHUNK, body, start_ref[...])


def stress_partials(q_state, element, migration, slab_elems):
    groups = slab_elems // 128
    rows = round_up(3 * groups, 16)
    count = q_state.shape[1]
    out = pl.pallas_call(
        functools.partial(stress_kernel, groups=groups, rows=rows),
        out_shape=jax.ShapeDtypeStruct((4 * rows, 128), jnp.float32),
        cost_estimate=pl.CostEstimate(
            flops=2 * 3 * 4 * rows * 128 * count, transcendentals=0, bytes_accessed=20 * count
        ),
    )(q_state, element.reshape(1, -1), migration.reshape(1, -1))
    total = out.reshape(4, rows, 128)[:, : 3 * groups].reshape(4, 3 * slab_elems)
    return total


def update_and_pack(q_state, increments, element, migration, table, capacity):
    rows, slab_elems = table.shape
    groups = slab_elems // 128
    groups16 = round_up(groups, 16)
    slots = capacity // 128
    slots16 = round_up(slots, 16)
    arranged = jnp.pad(table.reshape(rows, groups, 128), ((0, 0), (0, groups16 - groups), (0, 0)))
    arranged = arranged.reshape(rows * groups16, 128)
    hi = lax.reduce_precision(arranged, exponent_bits=8, mantissa_bits=7)
    rest = arranged - hi
    mid = lax.reduce_precision(rest, exponent_bits=8, mantissa_bits=7)
    lo = rest - mid
    pieces = jnp.concatenate([hi, mid, lo], axis=1).astype(jnp.bfloat16)
    count = q_state.shape[1]
    parts = UPDATE_PARTS
    share = count // parts
    flags = jnp.stack([migration == 1, migration == -1]).astype(jnp.float32)
    per_part = jnp.sum(flags.reshape(2, parts, share), axis=2)
    starts = jnp.cumsum(per_part, axis=1) - per_part
    starts = jnp.pad(starts.T, ((0, 0), (0, 6)))[:, :, None]
    q_parts, up, down = [], 0.0, 0.0
    for part in range(parts):
        q_part, up_part, down_part = pl.pallas_call(
            functools.partial(
                update_kernel, groups16=groups16, slots16=slots16, first=part * share // CHUNK
            ),
            out_shape=(
                jax.ShapeDtypeStruct((3, share), jnp.float32),
                jax.ShapeDtypeStruct((3 * slots16, 128), jnp.float32),
                jax.ShapeDtypeStruct((3 * slots16, 128), jnp.float32),
            ),
            scratch_shapes=[pltpu.VMEM((CHUNK, CHUNK), jnp.bfloat16)],
            cost_estimate=pl.CostEstimate(
                flops=16 * 3 * (5 * groups16 + 6 * slots16) * 128 * share,
                transcendentals=0,
                bytes_accessed=40 * share,
            ),
        )(
            q_state,
            increments,
            element.reshape(1, -1),
            migration.reshape(1, -1),
            pieces,
            starts[part],
        )
        q_parts.append(q_part)
        up = up + up_part
        down = down + down_part
    q_next = jnp.concatenate(q_parts, axis=1)

    def unpack(acc):
        return acc.reshape(3, slots16, 128)[:, :slots].reshape(3, slots * 128)

    return q_next, unpack(up), unpack(down)


def sweep_kernel(idx_ref, g_ref, s_ref, pt_ref, ft_ref, v_ref, vout_ref, send_ref):
    total = g_ref.shape[0]
    own = v_ref.shape[0]
    width = s_ref.shape[1]
    b = pl.program_id(0)
    acc = None
    for n in range(width):
        w = idx_ref[b * width + n]
        inside = jnp.logical_and(w >= 0, w < total)
        near = g_ref[pl.ds(jnp.clip(w, 0, total - 1), 1), :]
        near = jnp.where(inside, near, 0.0)
        term = s_ref[0, n] * near
        acc = term if acc is None else acc + term
    image = jnp.sum(acc, axis=1, keepdims=True)
    rest = ft_ref[0] - image
    update = jnp.sum(pt_ref[0] * rest, axis=0, keepdims=True)
    vout_ref[pl.ds(b, 1), :] = v_ref[pl.ds(b, 1), :] + damping * update

    @pl.when(b == own - 1)
    def _():
        fresh = vout_ref[...]
        for k in range(send_ref.shape[0] // own):
            send_ref[k * own : (k + 1) * own, :] = fresh


def sweep(where_read, gathered, stiffness, transposed, force_t, velocity, copies):
    own, size = velocity.shape
    width = stiffness.shape[1]
    whole = lambda shape: pl.BlockSpec(shape, lambda b, idx: (0,) * len(shape))
    return pl.pallas_call(
        sweep_kernel,
        out_shape=(
            jax.ShapeDtypeStruct(velocity.shape, jnp.float32),
            jax.ShapeDtypeStruct((copies * own, size), jnp.float32),
        ),
        grid_spec=pltpu.PrefetchScalarGridSpec(
            num_scalar_prefetch=1,
            grid=(own,),
            in_specs=[
                whole(gathered.shape),
                pl.BlockSpec((1, width, size, size), lambda b, idx: (b, 0, 0, 0)),
                pl.BlockSpec((1, size, size), lambda b, idx: (b, 0, 0)),
                pl.BlockSpec((1, size, 1), lambda b, idx: (b, 0, 0)),
                whole(velocity.shape),
            ],
            out_specs=(whole(velocity.shape), whole((copies * own, size))),
        ),
        cost_estimate=pl.CostEstimate(
            flops=2 * (stiffness.size + transposed.size),
            transcendentals=0,
            bytes_accessed=4 * (stiffness.size + transposed.size + gathered.size),
        ),
    )(where_read, gathered, stiffness, transposed, force_t, velocity)

def passed_along(array, axis, by):
    size = lax.axis_size(axis)
    pairs = [(i, i + by) for i in range(size) if 0 <= i + by < size]
    return lax.ppermute(array, axis, pairs)


def body(
    q_state,
    increments,
    velocity_grad,
    element,
    migration,
    volume,
    div_map,
    stiffness,
    pattern,
    preconditioner,
):
    capacity = migration.shape[0] // 16
    slab_elems = velocity_grad.shape[1]
    n_slab = lax.axis_size("slab")
    slab = lax.axis_index("slab")

    n_rad = lax.axis_size("rad")
    near = stress_partials(q_state, element, migration, slab_elems)
    near = near.reshape(4, 3, n_rad, slab_elems // n_rad).transpose(1, 2, 0, 3)
    spread = jnp.zeros((n_slab + 2,) + near.shape[1:], jnp.float32)
    spread = lax.dynamic_update_slice(spread, near, (slab, 0, 0, 0))
    spread = spread[1 : n_slab + 1].reshape((n_slab * n_rad,) + near.shape[2:])
    received = lax.all_to_all(spread, ("slab", "rad"), 0, 0, tiled=True)
    sums = jnp.sum(received, axis=0)
    element_stress = sums / volume

    q_next, upward, downward = update_and_pack(
        q_state, increments, element, migration, velocity_grad, capacity
    )
    from_lower = passed_along(upward, "slab", 1)
    from_upper = passed_along(downward, "slab", -1)
    arrivals = jnp.stack([from_lower, from_upper])

    own_blocks = stiffness.shape[0]
    groups = (
        element_stress.reshape(4, own_blocks, BLOCK // 4)
        .transpose(1, 0, 2)
        .reshape(own_blocks, BLOCK)
    )
    force = jnp.dot(groups, div_map, precision=highest)

    def precondition(vector):
        return jnp.einsum("bij,bj->bi", preconditioner, vector, precision=highest)

    slab_blocks = own_blocks * n_rad
    copies = n_slab * n_rad
    where_read = ((slab - 1) * slab_blocks + pattern).reshape(-1).astype(jnp.int32)
    transposed = jnp.swapaxes(preconditioner, 1, 2)
    force_t = force[:, :, None]
    velocity = damping * precondition(force)
    send = jnp.tile(velocity, (copies, 1))
    for sweep_index in range(1, ITERS):
        gathered = lax.all_to_all(send, ("slab", "rad"), 0, 0, tiled=True)
        velocity, send = sweep(
            where_read, gathered, stiffness, transposed, force_t, velocity, copies
        )
    return (q_next, arrivals, element_stress, velocity)


def solution(mesh):
    placed = (
        P(None, ("slab", "rad")),
        P(None, ("slab", "rad")),
        P(None, "slab"),
        P(("slab", "rad")),
        P(("slab", "rad")),
        P(("slab", "rad")),
        P(),
        P(("slab", "rad"), None, None, None),
        P(("slab", "rad"), None),
        P(("slab", "rad"), None, None),
    )
    return jax.shard_map(
        body,
        mesh=mesh,
        in_specs=placed,
        out_specs=(
            P(None, ("slab", "rad")),
            P(None, None, ("slab", "rad")),
            P(None, ("slab", "rad")),
            P(("slab", "rad"), None),
        ),
        check_vma=False,
    )
```

```python
import functools

import jax
import jax.numpy as jnp
from jax import lax
from jax.experimental import pallas as pl
from jax.experimental.pallas import tpu as pltpu
from jax.sharding import PartitionSpec as P

BLOCK = 192
ITERS = 6
CHUNK = 512
STRESS_CHUNK = 1024
UPDATE_PARTS = 4

extensibility = 50.0
time_step = 0.01
noise_scale = 0.1
damping = 0.6
highest = lax.Precision.HIGHEST
nt_dims = (((1,), (1,)), ((), ()))


def round_up(value, step):
    return -(-value // step) * step


def bf16_pieces(x):
    hi = x.astype(jnp.bfloat16)
    rest = x - hi.astype(jnp.float32)
    mid = rest.astype(jnp.bfloat16)
    lo = (rest - mid.astype(jnp.float32)).astype(jnp.bfloat16)
    return (hi, mid, lo)


def spring_terms(q):
    radial = q[0:1]
    axial = q[1:2]
    azimuth = q[2:3]
    stretch = radial * radial + axial * axial + azimuth * azimuth
    spring = 1.0 / (1.0 - stretch / extensibility)
    terms = (
        spring * radial * radial - 1.0,
        spring * axial * axial - 1.0,
        spring * radial * axial,
        spring * azimuth * azimuth - 1.0,
    )
    return spring, terms


def stress_kernel(slab_ref, q_ref, e_ref, m_ref, send_ref, acc_ref, *, groups, rows):
    count = q_ref.shape[1]
    n_dev = send_ref.shape[0]
    n_rad = groups // 3
    acc_ref[...] = jnp.zeros_like(acc_ref)
    low_iota = lax.broadcasted_iota(jnp.int32, (128, STRESS_CHUNK), 0)
    row_iota = lax.broadcasted_iota(jnp.int32, (rows, STRESS_CHUNK), 0)
    zero = jnp.zeros((), jnp.bfloat16)

    def body(step, carry):
        cols = pl.ds(pl.multiple_of(step * STRESS_CHUNK, STRESS_CHUNK), STRESS_CHUNK)
        q = q_ref[:, cols]
        element = e_ref[:, cols]
        move = m_ref[:, cols]
        spring, terms = spring_terms(q)
        kind = jnp.where(move == 0, 1, jnp.where(move == 1, 2, 0))
        key = kind * groups + (element >> 7)
        low = (low_iota == (element & 127)).astype(jnp.bfloat16)
        low = jnp.concatenate([low, low, low], axis=1)
        mask = row_iota == key
        spread = jnp.concatenate(
            [
                jnp.concatenate([jnp.where(mask, piece, zero) for piece in bf16_pieces(term)], axis=1)
                for term in terms
            ],
            axis=0,
        )
        acc_ref[...] += lax.dot_general(spread, low, nt_dims, preferred_element_type=jnp.float32)
        return carry

    lax.fori_loop(0, count // STRESS_CHUNK, body, 0)
    send_ref[...] = jnp.zeros_like(send_ref)
    slab = slab_ref[0]
    for kind in range(3):
        target = slab - 1 + kind

        @pl.when(jnp.logical_and(target >= 0, target * n_rad < n_dev))
        def _():
            for r in range(n_rad):
                for c in range(4):
                    start = c * rows + kind * groups + r * 3
                    send_ref[target * n_rad + r, c * 3 : c * 3 + 3, :] = acc_ref[start : start + 3, :]


def update_kernel(
    q_ref, inc_ref, e_ref, m_ref, tab_ref, start_ref, qn_ref, up_ref, dn_ref, tri_ref, *, groups16, slots16, first
):
    count = qn_ref.shape[1]
    up_ref[...] = jnp.zeros_like(up_ref)
    dn_ref[...] = jnp.zeros_like(dn_ref)
    before = lax.broadcasted_iota(jnp.int32, (CHUNK, CHUNK), 0)
    after = lax.broadcasted_iota(jnp.int32, (CHUNK, CHUNK), 1)
    tri_ref[...] = (before < after).astype(jnp.bfloat16)
    low_iota = lax.broadcasted_iota(jnp.int32, (128, CHUNK), 0)
    group_iota = lax.broadcasted_iota(jnp.int32, (groups16, CHUNK), 0)
    slot_iota = lax.broadcasted_iota(jnp.int32, (slots16, CHUNK), 0)
    flag_row = lax.broadcasted_iota(jnp.int32, (8, CHUNK), 0)
    zero = jnp.zeros((), jnp.bfloat16)

    def body(step, offsets):
        cols = pl.ds(pl.multiple_of((first + step) * CHUNK, CHUNK), CHUNK)
        q = q_ref[:, cols]
        inc = inc_ref[:, cols]
        element = e_ref[:, cols]
        move = m_ref[:, cols]
        low = (low_iota == (element & 127)).astype(jnp.bfloat16)
        picked = jnp.dot(
            tab_ref[...], jnp.concatenate([low, low, low], axis=0), preferred_element_type=jnp.float32
        )
        hit = group_iota == (element >> 7)
        grads = [
            jnp.sum(
                jnp.where(hit, picked[c * groups16 : (c + 1) * groups16], 0.0),
                axis=0,
                keepdims=True,
            )
            for c in range(5)
        ]
        radial = q[0:1]
        axial = q[1:2]
        azimuth = q[2:3]
        spring, terms = spring_terms(q)
        drift = (
            grads[0] * radial + grads[1] * axial,
            grads[2] * radial + grads[3] * axial,
            grads[4] * azimuth,
        )
        q_next = [
            q[k : k + 1] + time_step * (drift[k] - 0.5 * spring * q[k : k + 1]) + noise_scale * inc[k : k + 1]
            for k in range(3)
        ]
        qn_ref[:, pl.ds(pl.multiple_of(step * CHUNK, CHUNK), CHUNK)] = jnp.concatenate(q_next, axis=0)
        going_up = move == 1
        going_down = move == -1
        flags = jnp.where(
            flag_row == 0,
            going_up.astype(jnp.float32),
            jnp.where(flag_row == 1, going_down.astype(jnp.float32), 0.0),
        )
        ranks = jnp.dot(flags.astype(jnp.bfloat16), tri_ref[...], preferred_element_type=jnp.float32)
        slots = (ranks + offsets).astype(jnp.int32)
        pieces = [bf16_pieces(value) for value in q_next]
        for direction, chosen, out_ref in ((0, going_up, up_ref), (1, going_down, dn_ref)):
            slot = slots[direction : direction + 1]
            place = ((low_iota == (slot & 127)) & chosen).astype(jnp.bfloat16)
            place = jnp.concatenate([place, place, place], axis=1)
            which = slot_iota == (slot >> 7)
            spread = jnp.concatenate(
                [
                    jnp.concatenate([jnp.where(which, piece, zero) for piece in pieces[k]], axis=1)
                    for k in range(3)
                ],
                axis=0,
            )
            out_ref[...] += lax.dot_general(spread, place, nt_dims, preferred_element_type=jnp.float32)
        return offsets + jnp.sum(flags, axis=1, keepdims=True)

    lax.fori_loop(0, count // CHUNK, body, start_ref[...])


def stress_partials(slab, q_state, element, migration, slab_elems, n_dev):
    groups = slab_elems // 128
    rows = round_up(3 * groups, 16)
    count = q_state.shape[1]
    vmem = pl.BlockSpec(memory_space=pltpu.VMEM)
    return pl.pallas_call(
        functools.partial(stress_kernel, groups=groups, rows=rows),
        out_shape=jax.ShapeDtypeStruct((n_dev, 12, 128), jnp.float32),
        in_specs=[pl.BlockSpec(memory_space=pltpu.SMEM)] + [vmem] * 3,
        out_specs=vmem,
        scratch_shapes=[pltpu.VMEM((4 * rows, 128), jnp.float32)],
        cost_estimate=pl.CostEstimate(
            flops=2 * 3 * 4 * rows * 128 * count, transcendentals=0, bytes_accessed=20 * count
        ),
    )(slab, q_state, element.reshape(1, -1), migration.reshape(1, -1))


def first_kernel(pt_ref, ft_ref, vout_ref, send_ref):
    own = vout_ref.shape[0]
    rows = [
        damping * jnp.sum(pt_ref[b] * ft_ref[:, b : b + 1], axis=0, keepdims=True)
        for b in range(own)
    ]
    fresh = jnp.concatenate(rows, axis=0)
    vout_ref[...] = fresh
    for k in range(send_ref.shape[0] // own):
        send_ref[k * own : (k + 1) * own, :] = fresh


def first_velocity(transposed, force_t, copies):
    own, size = transposed.shape[0], transposed.shape[1]
    return pl.pallas_call(
        first_kernel,
        out_shape=(
            jax.ShapeDtypeStruct((own, size), jnp.float32),
            jax.ShapeDtypeStruct((copies * own, size), jnp.float32),
        ),
        cost_estimate=pl.CostEstimate(
            flops=2 * transposed.size, transcendentals=0, bytes_accessed=4 * transposed.size
        ),
    )(transposed, force_t)


def update_and_pack(q_state, increments, element, migration, table, capacity):
    rows, slab_elems = table.shape
    groups = slab_elems // 128
    groups16 = round_up(groups, 16)
    slots = capacity // 128
    slots16 = round_up(slots, 16)
    arranged = jnp.pad(table.reshape(rows, groups, 128), ((0, 0), (0, groups16 - groups), (0, 0)))
    arranged = arranged.reshape(rows * groups16, 128)
    hi = lax.reduce_precision(arranged, exponent_bits=8, mantissa_bits=7)
    rest = arranged - hi
    mid = lax.reduce_precision(rest, exponent_bits=8, mantissa_bits=7)
    lo = rest - mid
    pieces = jnp.concatenate([hi, mid, lo], axis=1).astype(jnp.bfloat16)
    count = q_state.shape[1]
    parts = UPDATE_PARTS
    share = count // parts
    flags = jnp.stack([migration == 1, migration == -1]).astype(jnp.float32)
    per_part = jnp.sum(flags.reshape(2, parts, share), axis=2)
    starts = jnp.cumsum(per_part, axis=1) - per_part
    starts = jnp.pad(starts.T, ((0, 0), (0, 6)))[:, :, None]
    q_parts, up, down = [], 0.0, 0.0
    for part in range(parts):
        q_part, up_part, down_part = pl.pallas_call(
            functools.partial(
                update_kernel, groups16=groups16, slots16=slots16, first=part * share // CHUNK
            ),
            out_shape=(
                jax.ShapeDtypeStruct((3, share), jnp.float32),
                jax.ShapeDtypeStruct((3 * slots16, 128), jnp.float32),
                jax.ShapeDtypeStruct((3 * slots16, 128), jnp.float32),
            ),
            scratch_shapes=[pltpu.VMEM((CHUNK, CHUNK), jnp.bfloat16)],
            cost_estimate=pl.CostEstimate(
                flops=16 * 3 * (5 * groups16 + 6 * slots16) * 128 * share,
                transcendentals=0,
                bytes_accessed=40 * share,
            ),
        )(
            q_state,
            increments,
            element.reshape(1, -1),
            migration.reshape(1, -1),
            pieces,
            starts[part],
        )
        q_parts.append(q_part)
        up = up + up_part
        down = down + down_part
    q_next = jnp.concatenate(q_parts, axis=1)

    def unpack(acc):
        return acc.reshape(3, slots16, 128)[:, :slots].reshape(3, slots * 128)

    return q_next, unpack(up), unpack(down)


def sweep_kernel(idx_ref, g_ref, s_ref, pt_ref, ft_ref, v_ref, vout_ref, send_ref):
    total = g_ref.shape[0]
    own = v_ref.shape[0]
    width = s_ref.shape[1]
    rows = []
    for b in range(own):
        acc = None
        for n in range(width):
            w = idx_ref[b * width + n]
            inside = jnp.logical_and(w >= 0, w < total)
            near = g_ref[pl.ds(jnp.clip(w, 0, total - 1), 1), :]
            near = jnp.where(inside, near, 0.0)
            term = s_ref[b, n] * near
            acc = term if acc is None else acc + term
        image = jnp.sum(acc, axis=1, keepdims=True)
        rest = ft_ref[:, b : b + 1] - image
        update = jnp.sum(pt_ref[b] * rest, axis=0, keepdims=True)
        rows.append(v_ref[b : b + 1, :] + damping * update)
    fresh = jnp.concatenate(rows, axis=0)
    vout_ref[...] = fresh
    for k in range(send_ref.shape[0] // own):
        send_ref[k * own : (k + 1) * own, :] = fresh


def sweep(where_read, gathered, stiffness, transposed, force_t, velocity, copies):
    own = velocity.shape[0]
    vmem = pl.BlockSpec(memory_space=pltpu.VMEM)
    return pl.pallas_call(
        sweep_kernel,
        out_shape=(
            jax.ShapeDtypeStruct(velocity.shape, jnp.float32),
            jax.ShapeDtypeStruct((copies * own, velocity.shape[1]), jnp.float32),
        ),
        in_specs=[pl.BlockSpec(memory_space=pltpu.SMEM)] + [vmem] * 5,
        out_specs=(vmem, vmem),
        cost_estimate=pl.CostEstimate(
            flops=2 * (stiffness.size + transposed.size),
            transcendentals=0,
            bytes_accessed=4 * (stiffness.size + transposed.size + gathered.size),
        ),
    )(where_read, gathered, stiffness, transposed, force_t, velocity)


def passed_along(array, axis, by):
    size = lax.axis_size(axis)
    pairs = [(i, i + by) for i in range(size) if 0 <= i + by < size]
    return lax.ppermute(array, axis, pairs)


def body(
    q_state,
    increments,
    velocity_grad,
    element,
    migration,
    volume,
    div_map,
    stiffness,
    pattern,
    preconditioner,
):
    capacity = migration.shape[0] // 16
    slab_elems = velocity_grad.shape[1]
    n_slab = lax.axis_size("slab")
    slab = lax.axis_index("slab")

    n_rad = lax.axis_size("rad")
    send = stress_partials(
        slab.reshape(1).astype(jnp.int32), q_state, element, migration, slab_elems, n_slab * n_rad
    )
    received = lax.all_to_all(send, ("slab", "rad"), 0, 0, tiled=True)
    sums = jnp.sum(received, axis=0).reshape(4, slab_elems // n_rad)
    element_stress = sums / volume

    q_next, upward, downward = update_and_pack(
        q_state, increments, element, migration, velocity_grad, capacity
    )
    from_lower = passed_along(upward, "slab", 1)
    from_upper = passed_along(downward, "slab", -1)
    arrivals = jnp.stack([from_lower, from_upper])

    own_blocks = stiffness.shape[0]
    groups = (
        element_stress.reshape(4, own_blocks, BLOCK // 4)
        .transpose(1, 0, 2)
        .reshape(own_blocks, BLOCK)
    )
    force = jnp.dot(groups, div_map, precision=highest)

    def precondition(vector):
        return jnp.einsum("bij,bj->bi", preconditioner, vector, precision=highest)

    slab_blocks = own_blocks * n_rad
    copies = n_slab * n_rad
    where_read = ((slab - 1) * slab_blocks + pattern).reshape(-1).astype(jnp.int32)
    transposed = jnp.swapaxes(preconditioner, 1, 2)
    force_t = force.T
    velocity, send = first_velocity(transposed, force_t, copies)
    for sweep_index in range(1, ITERS):
        gathered = lax.all_to_all(send, ("slab", "rad"), 0, 0, tiled=True)
        velocity, send = sweep(
            where_read, gathered, stiffness, transposed, force_t, velocity, copies
        )
    return (q_next, arrivals, element_stress, velocity)


def solution(mesh):
    placed = (
        P(None, ("slab", "rad")),
        P(None, ("slab", "rad")),
        P(None, "slab"),
        P(("slab", "rad")),
        P(("slab", "rad")),
        P(("slab", "rad")),
        P(),
        P(("slab", "rad"), None, None, None),
        P(("slab", "rad"), None),
        P(("slab", "rad"), None, None),
    )
    return jax.shard_map(
        body,
        mesh=mesh,
        in_specs=placed,
        out_specs=(
            P(None, ("slab", "rad")),
            P(None, None, ("slab", "rad")),
            P(None, ("slab", "rad")),
            P(("slab", "rad"), None),
        ),
        check_vma=False,
    )
```

```python
import functools

import jax
import jax.numpy as jnp
from jax import lax
from jax.experimental import pallas as pl
from jax.experimental.pallas import tpu as pltpu
from jax.sharding import PartitionSpec as P

BLOCK = 192
ITERS = 6
CHUNK = 512
STRESS_CHUNK = 1024
UPDATE_PARTS = 4

extensibility = 50.0
time_step = 0.01
noise_scale = 0.1
damping = 0.6
highest = lax.Precision.HIGHEST
nt_dims = (((1,), (1,)), ((), ()))


def round_up(value, step):
    return -(-value // step) * step


def bf16_pieces(x):
    hi = x.astype(jnp.bfloat16)
    rest = x - hi.astype(jnp.float32)
    mid = rest.astype(jnp.bfloat16)
    lo = (rest - mid.astype(jnp.float32)).astype(jnp.bfloat16)
    return (hi, mid, lo)


def spring_terms(q):
    radial = q[0:1]
    axial = q[1:2]
    azimuth = q[2:3]
    stretch = radial * radial + axial * axial + azimuth * azimuth
    spring = 1.0 / (1.0 - stretch / extensibility)
    terms = (
        spring * radial * radial - 1.0,
        spring * axial * axial - 1.0,
        spring * radial * axial,
        spring * azimuth * azimuth - 1.0,
    )
    return spring, terms


def stress_kernel(slab_ref, q_ref, e_ref, m_ref, send_ref, acc_ref, *, groups, rows):
    count = q_ref.shape[1]
    n_dev = send_ref.shape[0]
    n_rad = groups // 3
    acc_ref[...] = jnp.zeros_like(acc_ref)
    low_iota = lax.broadcasted_iota(jnp.int32, (128, STRESS_CHUNK), 0)
    row_iota = lax.broadcasted_iota(jnp.int32, (rows, STRESS_CHUNK), 0)
    zero = jnp.zeros((), jnp.bfloat16)

    def body(step, carry):
        cols = pl.ds(pl.multiple_of(step * STRESS_CHUNK, STRESS_CHUNK), STRESS_CHUNK)
        q = q_ref[:, cols]
        element = e_ref[:, cols]
        move = m_ref[:, cols]
        spring, terms = spring_terms(q)
        kind = jnp.where(move == 0, 1, jnp.where(move == 1, 2, 0))
        key = kind * groups + (element >> 7)
        low = (low_iota == (element & 127)).astype(jnp.bfloat16)
        low = jnp.concatenate([low, low, low], axis=1)
        mask = row_iota == key
        spread = jnp.concatenate(
            [
                jnp.concatenate([jnp.where(mask, piece, zero) for piece in bf16_pieces(term)], axis=1)
                for term in terms
            ],
            axis=0,
        )
        acc_ref[...] += lax.dot_general(spread, low, nt_dims, preferred_element_type=jnp.float32)
        return carry

    lax.fori_loop(0, count // STRESS_CHUNK, body, 0)
    send_ref[...] = jnp.zeros_like(send_ref)
    slab = slab_ref[0]
    for kind in range(3):
        target = slab - 1 + kind

        @pl.when(jnp.logical_and(target >= 0, target * n_rad < n_dev))
        def _():
            for r in range(n_rad):
                for c in range(4):
                    start = c * rows + kind * groups + r * 3
                    send_ref[target * n_rad + r, c * 3 : c * 3 + 3, :] = acc_ref[start : start + 3, :]


def update_kernel(
    q_ref, inc_ref, e_ref, m_ref, tab_ref, start_ref, qn_ref, up_ref, dn_ref, tri_ref, *, groups16, slots16, first
):
    count = qn_ref.shape[1]
    up_ref[...] = jnp.zeros_like(up_ref)
    dn_ref[...] = jnp.zeros_like(dn_ref)
    before = lax.broadcasted_iota(jnp.int32, (CHUNK, CHUNK), 0)
    after = lax.broadcasted_iota(jnp.int32, (CHUNK, CHUNK), 1)
    tri_ref[...] = (before < after).astype(jnp.bfloat16)
    low_iota = lax.broadcasted_iota(jnp.int32, (128, CHUNK), 0)
    group_iota = lax.broadcasted_iota(jnp.int32, (groups16, CHUNK), 0)
    slot_iota = lax.broadcasted_iota(jnp.int32, (slots16, CHUNK), 0)
    flag_row = lax.broadcasted_iota(jnp.int32, (8, CHUNK), 0)
    zero = jnp.zeros((), jnp.bfloat16)

    def body(step, offsets):
        cols = pl.ds(pl.multiple_of((first + step) * CHUNK, CHUNK), CHUNK)
        q = q_ref[:, cols]
        inc = inc_ref[:, cols]
        element = e_ref[:, cols]
        move = m_ref[:, cols]
        low = (low_iota == (element & 127)).astype(jnp.bfloat16)
        picked = jnp.dot(
            tab_ref[...], jnp.concatenate([low, low, low], axis=0), preferred_element_type=jnp.float32
        )
        hit = group_iota == (element >> 7)
        grads = [
            jnp.sum(
                jnp.where(hit, picked[c * groups16 : (c + 1) * groups16], 0.0),
                axis=0,
                keepdims=True,
            )
            for c in range(5)
        ]
        radial = q[0:1]
        axial = q[1:2]
        azimuth = q[2:3]
        spring, terms = spring_terms(q)
        drift = (
            grads[0] * radial + grads[1] * axial,
            grads[2] * radial + grads[3] * axial,
            grads[4] * azimuth,
        )
        q_next = [
            q[k : k + 1] + time_step * (drift[k] - 0.5 * spring * q[k : k + 1]) + noise_scale * inc[k : k + 1]
            for k in range(3)
        ]
        qn_ref[:, pl.ds(pl.multiple_of(step * CHUNK, CHUNK), CHUNK)] = jnp.concatenate(q_next, axis=0)
        going_up = move == 1
        going_down = move == -1
        flags = jnp.where(
            flag_row == 0,
            going_up.astype(jnp.float32),
            jnp.where(flag_row == 1, going_down.astype(jnp.float32), 0.0),
        )
        ranks = jnp.dot(flags.astype(jnp.bfloat16), tri_ref[...], preferred_element_type=jnp.float32)
        slots = (ranks + offsets).astype(jnp.int32)
        pieces = [bf16_pieces(value) for value in q_next]
        for direction, chosen, out_ref in ((0, going_up, up_ref), (1, going_down, dn_ref)):
            slot = slots[direction : direction + 1]
            place = ((low_iota == (slot & 127)) & chosen).astype(jnp.bfloat16)
            place = jnp.concatenate([place, place, place], axis=1)
            which = slot_iota == (slot >> 7)
            spread = jnp.concatenate(
                [
                    jnp.concatenate([jnp.where(which, piece, zero) for piece in pieces[k]], axis=1)
                    for k in range(3)
                ],
                axis=0,
            )
            out_ref[...] += lax.dot_general(spread, place, nt_dims, preferred_element_type=jnp.float32)
        return offsets + jnp.sum(flags, axis=1, keepdims=True)

    lax.fori_loop(0, count // CHUNK, body, start_ref[...])


def stress_partials(slab, q_state, element, migration, slab_elems, n_dev):
    groups = slab_elems // 128
    rows = round_up(3 * groups, 16)
    count = q_state.shape[1]
    vmem = pl.BlockSpec(memory_space=pltpu.VMEM)
    return pl.pallas_call(
        functools.partial(stress_kernel, groups=groups, rows=rows),
        out_shape=jax.ShapeDtypeStruct((n_dev, 12, 128), jnp.float32),
        in_specs=[pl.BlockSpec(memory_space=pltpu.SMEM)] + [vmem] * 3,
        out_specs=vmem,
        scratch_shapes=[pltpu.VMEM((4 * rows, 128), jnp.float32)],
        cost_estimate=pl.CostEstimate(
            flops=2 * 3 * 4 * rows * 128 * count, transcendentals=0, bytes_accessed=20 * count
        ),
    )(slab, q_state, element.reshape(1, -1), migration.reshape(1, -1))


def first_kernel(pt_ref, ft_ref, vout_ref, send_ref):
    own = vout_ref.shape[0]
    rows = [
        damping * jnp.sum(pt_ref[b] * ft_ref[:, b : b + 1], axis=0, keepdims=True)
        for b in range(own)
    ]
    fresh = jnp.concatenate(rows, axis=0)
    vout_ref[...] = fresh
    for k in range(send_ref.shape[0] // own):
        send_ref[k * own : (k + 1) * own, :] = fresh


def first_velocity(transposed, force_t, copies):
    own, size = transposed.shape[0], transposed.shape[1]
    return pl.pallas_call(
        first_kernel,
        out_shape=(
            jax.ShapeDtypeStruct((own, size), jnp.float32),
            jax.ShapeDtypeStruct((copies * own, size), jnp.float32),
        ),
        cost_estimate=pl.CostEstimate(
            flops=2 * transposed.size, transcendentals=0, bytes_accessed=4 * transposed.size
        ),
    )(transposed, force_t)


def update_and_pack(q_state, increments, element, migration, table, capacity):
    rows, slab_elems = table.shape
    groups = slab_elems // 128
    groups16 = round_up(groups, 16)
    slots = capacity // 128
    slots16 = round_up(slots, 16)
    arranged = jnp.pad(table.reshape(rows, groups, 128), ((0, 0), (0, groups16 - groups), (0, 0)))
    arranged = arranged.reshape(rows * groups16, 128)
    hi = lax.reduce_precision(arranged, exponent_bits=8, mantissa_bits=7)
    rest = arranged - hi
    mid = lax.reduce_precision(rest, exponent_bits=8, mantissa_bits=7)
    lo = rest - mid
    pieces = jnp.concatenate([hi, mid, lo], axis=1).astype(jnp.bfloat16)
    count = q_state.shape[1]
    parts = UPDATE_PARTS
    share = count // parts
    flags = jnp.stack([migration == 1, migration == -1]).astype(jnp.float32)
    per_part = jnp.sum(flags.reshape(2, parts, share), axis=2)
    starts = jnp.cumsum(per_part, axis=1) - per_part
    starts = jnp.pad(starts.T, ((0, 0), (0, 6)))[:, :, None]
    q_parts, up, down = [], 0.0, 0.0
    for part in range(parts):
        q_part, up_part, down_part = pl.pallas_call(
            functools.partial(
                update_kernel, groups16=groups16, slots16=slots16, first=part * share // CHUNK
            ),
            out_shape=(
                jax.ShapeDtypeStruct((3, share), jnp.float32),
                jax.ShapeDtypeStruct((3 * slots16, 128), jnp.float32),
                jax.ShapeDtypeStruct((3 * slots16, 128), jnp.float32),
            ),
            scratch_shapes=[pltpu.VMEM((CHUNK, CHUNK), jnp.bfloat16)],
            cost_estimate=pl.CostEstimate(
                flops=16 * 3 * (5 * groups16 + 6 * slots16) * 128 * share,
                transcendentals=0,
                bytes_accessed=40 * share,
            ),
        )(
            q_state,
            increments,
            element.reshape(1, -1),
            migration.reshape(1, -1),
            pieces,
            starts[part],
        )
        q_parts.append(q_part)
        up = up + up_part
        down = down + down_part
    q_next = jnp.concatenate(q_parts, axis=1)

    def unpack(acc):
        return acc.reshape(3, slots16, 128)[:, :slots].reshape(3, slots * 128)

    return q_next, unpack(up), unpack(down)


def sweep_kernel(
    idx_ref, g_hbm, s_hbm, pt_hbm, ft_ref, v_ref, vout_ref, send_ref, g_buf, s_buf, pt_buf, sems
):
    total = g_buf.shape[0]
    own = v_ref.shape[0]
    width = s_buf.shape[1]
    g_copy = pltpu.make_async_copy(g_hbm, g_buf, sems.at[0])
    g_copy.start()
    s_copies = [pltpu.make_async_copy(s_hbm.at[b], s_buf.at[b], sems.at[1 + b]) for b in range(own)]
    p_copies = [
        pltpu.make_async_copy(pt_hbm.at[b], pt_buf.at[b], sems.at[1 + own + b]) for b in range(own)
    ]
    for b in range(own):
        s_copies[b].start()
        p_copies[b].start()
    g_copy.wait()
    rows = []
    for b in range(own):
        s_copies[b].wait()
        acc = None
        for n in range(width):
            w = idx_ref[b * width + n]
            inside = jnp.logical_and(w >= 0, w < total)
            near = g_buf[pl.ds(jnp.clip(w, 0, total - 1), 1), :]
            near = jnp.where(inside, near, 0.0)
            term = s_buf[b, n] * near
            acc = term if acc is None else acc + term
        image = jnp.sum(acc, axis=1, keepdims=True)
        rest = ft_ref[:, b : b + 1] - image
        p_copies[b].wait()
        update = jnp.sum(pt_buf[b] * rest, axis=0, keepdims=True)
        rows.append(v_ref[b : b + 1, :] + damping * update)
    fresh = jnp.concatenate(rows, axis=0)
    vout_ref[...] = fresh
    for k in range(send_ref.shape[0] // own):
        send_ref[k * own : (k + 1) * own, :] = fresh


def sweep(where_read, gathered, stiffness, transposed, force_t, velocity, copies):
    own = velocity.shape[0]
    vmem = pl.BlockSpec(memory_space=pltpu.VMEM)
    anywhere = pl.BlockSpec(memory_space=pl.ANY)
    return pl.pallas_call(
        sweep_kernel,
        out_shape=(
            jax.ShapeDtypeStruct(velocity.shape, jnp.float32),
            jax.ShapeDtypeStruct((copies * own, velocity.shape[1]), jnp.float32),
        ),
        in_specs=[pl.BlockSpec(memory_space=pltpu.SMEM), anywhere, anywhere, anywhere, vmem, vmem],
        out_specs=(vmem, vmem),
        scratch_shapes=[
            pltpu.VMEM(gathered.shape, jnp.float32),
            pltpu.VMEM(stiffness.shape, jnp.float32),
            pltpu.VMEM(transposed.shape, jnp.float32),
            pltpu.SemaphoreType.DMA((1 + 2 * own,)),
        ],
        cost_estimate=pl.CostEstimate(
            flops=2 * (stiffness.size + transposed.size),
            transcendentals=0,
            bytes_accessed=4 * (stiffness.size + transposed.size + gathered.size),
        ),
    )(where_read, gathered, stiffness, transposed, force_t, velocity)

def passed_along(array, axis, by):
    size = lax.axis_size(axis)
    pairs = [(i, i + by) for i in range(size) if 0 <= i + by < size]
    return lax.ppermute(array, axis, pairs)


def body(
    q_state,
    increments,
    velocity_grad,
    element,
    migration,
    volume,
    div_map,
    stiffness,
    pattern,
    preconditioner,
):
    capacity = migration.shape[0] // 16
    slab_elems = velocity_grad.shape[1]
    n_slab = lax.axis_size("slab")
    slab = lax.axis_index("slab")

    n_rad = lax.axis_size("rad")
    send = stress_partials(
        slab.reshape(1).astype(jnp.int32), q_state, element, migration, slab_elems, n_slab * n_rad
    )
    received = lax.all_to_all(send, ("slab", "rad"), 0, 0, tiled=True)
    sums = jnp.sum(received, axis=0).reshape(4, slab_elems // n_rad)
    element_stress = sums / volume

    q_next, upward, downward = update_and_pack(
        q_state, increments, element, migration, velocity_grad, capacity
    )
    from_lower = passed_along(upward, "slab", 1)
    from_upper = passed_along(downward, "slab", -1)
    arrivals = jnp.stack([from_lower, from_upper])

    own_blocks = stiffness.shape[0]
    groups = (
        element_stress.reshape(4, own_blocks, BLOCK // 4)
        .transpose(1, 0, 2)
        .reshape(own_blocks, BLOCK)
    )
    force = jnp.dot(groups, div_map, precision=highest)

    def precondition(vector):
        return jnp.einsum("bij,bj->bi", preconditioner, vector, precision=highest)

    slab_blocks = own_blocks * n_rad
    copies = n_slab * n_rad
    where_read = ((slab - 1) * slab_blocks + pattern).reshape(-1).astype(jnp.int32)
    transposed = jnp.swapaxes(preconditioner, 1, 2)
    force_t = force.T
    velocity, send = first_velocity(transposed, force_t, copies)
    for sweep_index in range(1, ITERS):
        gathered = lax.all_to_all(send, ("slab", "rad"), 0, 0, tiled=True)
        velocity, send = sweep(
            where_read, gathered, stiffness, transposed, force_t, velocity, copies
        )
    return (q_next, arrivals, element_stress, velocity)


def solution(mesh):
    placed = (
        P(None, ("slab", "rad")),
        P(None, ("slab", "rad")),
        P(None, "slab"),
        P(("slab", "rad")),
        P(("slab", "rad")),
        P(("slab", "rad")),
        P(),
        P(("slab", "rad"), None, None, None),
        P(("slab", "rad"), None),
        P(("slab", "rad"), None, None),
    )
    return jax.shard_map(
        body,
        mesh=mesh,
        in_specs=placed,
        out_specs=(
            P(None, ("slab", "rad")),
            P(None, None, ("slab", "rad")),
            P(None, ("slab", "rad")),
            P(("slab", "rad"), None),
        ),
        check_vma=False,
    )
```

```python
import functools

import jax
import jax.numpy as jnp
from jax import lax
from jax.experimental import pallas as pl
from jax.experimental.pallas import tpu as pltpu
from jax.sharding import PartitionSpec as P

BLOCK = 192
ITERS = 6
CHUNK = 512
STRESS_CHUNK = 1024
UPDATE_PARTS = 4

extensibility = 50.0
time_step = 0.01
noise_scale = 0.1
damping = 0.6
highest = lax.Precision.HIGHEST
nt_dims = (((1,), (1,)), ((), ()))


def round_up(value, step):
    return -(-value // step) * step


def bf16_pieces(x):
    hi = x.astype(jnp.bfloat16)
    rest = x - hi.astype(jnp.float32)
    mid = rest.astype(jnp.bfloat16)
    lo = (rest - mid.astype(jnp.float32)).astype(jnp.bfloat16)
    return (hi, mid, lo)


def spring_terms(q):
    radial = q[0:1]
    axial = q[1:2]
    azimuth = q[2:3]
    stretch = radial * radial + axial * axial + azimuth * azimuth
    spring = 1.0 / (1.0 - stretch / extensibility)
    terms = (
        spring * radial * radial - 1.0,
        spring * axial * axial - 1.0,
        spring * radial * axial,
        spring * azimuth * azimuth - 1.0,
    )
    return spring, terms


def stress_kernel(slab_ref, q_ref, e_ref, m_ref, send_ref, acc_ref, *, groups, rows):
    count = q_ref.shape[1]
    n_dev = send_ref.shape[0]
    n_rad = groups // 3
    acc_ref[...] = jnp.zeros_like(acc_ref)
    low_iota = lax.broadcasted_iota(jnp.int32, (128, STRESS_CHUNK), 0)
    row_iota = lax.broadcasted_iota(jnp.int32, (rows, STRESS_CHUNK), 0)
    zero = jnp.zeros((), jnp.bfloat16)

    def body(step, carry):
        cols = pl.ds(pl.multiple_of(step * STRESS_CHUNK, STRESS_CHUNK), STRESS_CHUNK)
        q = q_ref[:, cols]
        element = e_ref[:, cols]
        move = m_ref[:, cols]
        spring, terms = spring_terms(q)
        kind = jnp.where(move == 0, 1, jnp.where(move == 1, 2, 0))
        key = kind * groups + (element >> 7)
        low = (low_iota == (element & 127)).astype(jnp.bfloat16)
        low = jnp.concatenate([low, low, low], axis=1)
        mask = row_iota == key
        spread = jnp.concatenate(
            [
                jnp.concatenate([jnp.where(mask, piece, zero) for piece in bf16_pieces(term)], axis=1)
                for term in terms
            ],
            axis=0,
        )
        acc_ref[...] += lax.dot_general(spread, low, nt_dims, preferred_element_type=jnp.float32)
        return carry

    lax.fori_loop(0, count // STRESS_CHUNK, body, 0)
    send_ref[...] = jnp.zeros_like(send_ref)
    slab = slab_ref[0]
    for kind in range(3):
        target = slab - 1 + kind

        @pl.when(jnp.logical_and(target >= 0, target * n_rad < n_dev))
        def _():
            for r in range(n_rad):
                for c in range(4):
                    start = c * rows + kind * groups + r * 3
                    send_ref[target * n_rad + r, c * 3 : c * 3 + 3, :] = acc_ref[start : start + 3, :]


def update_kernel(
    q_ref, inc_ref, e_ref, m_ref, tab_ref, start_ref, qn_ref, up_ref, dn_ref, tri_ref, *, groups16, slots16, first
):
    count = qn_ref.shape[1]
    up_ref[...] = jnp.zeros_like(up_ref)
    dn_ref[...] = jnp.zeros_like(dn_ref)
    before = lax.broadcasted_iota(jnp.int32, (CHUNK, CHUNK), 0)
    after = lax.broadcasted_iota(jnp.int32, (CHUNK, CHUNK), 1)
    tri_ref[...] = (before < after).astype(jnp.bfloat16)
    low_iota = lax.broadcasted_iota(jnp.int32, (128, CHUNK), 0)
    group_iota = lax.broadcasted_iota(jnp.int32, (groups16, CHUNK), 0)
    slot_iota = lax.broadcasted_iota(jnp.int32, (slots16, CHUNK), 0)
    flag_row = lax.broadcasted_iota(jnp.int32, (8, CHUNK), 0)
    zero = jnp.zeros((), jnp.bfloat16)

    def body(step, offsets):
        cols = pl.ds(pl.multiple_of((first + step) * CHUNK, CHUNK), CHUNK)
        q = q_ref[:, cols]
        inc = inc_ref[:, cols]
        element = e_ref[:, cols]
        move = m_ref[:, cols]
        low = (low_iota == (element & 127)).astype(jnp.bfloat16)
        picked = jnp.dot(
            tab_ref[...], jnp.concatenate([low, low, low], axis=0), preferred_element_type=jnp.float32
        )
        hit = group_iota == (element >> 7)
        grads = [
            jnp.sum(
                jnp.where(hit, picked[c * groups16 : (c + 1) * groups16], 0.0),
                axis=0,
                keepdims=True,
            )
            for c in range(5)
        ]
        radial = q[0:1]
        axial = q[1:2]
        azimuth = q[2:3]
        spring, terms = spring_terms(q)
        drift = (
            grads[0] * radial + grads[1] * axial,
            grads[2] * radial + grads[3] * axial,
            grads[4] * azimuth,
        )
        q_next = [
            q[k : k + 1] + time_step * (drift[k] - 0.5 * spring * q[k : k + 1]) + noise_scale * inc[k : k + 1]
            for k in range(3)
        ]
        qn_ref[:, pl.ds(pl.multiple_of(step * CHUNK, CHUNK), CHUNK)] = jnp.concatenate(q_next, axis=0)
        going_up = move == 1
        going_down = move == -1
        flags = jnp.where(
            flag_row == 0,
            going_up.astype(jnp.float32),
            jnp.where(flag_row == 1, going_down.astype(jnp.float32), 0.0),
        )
        ranks = jnp.dot(flags.astype(jnp.bfloat16), tri_ref[...], preferred_element_type=jnp.float32)
        slots = (ranks + offsets).astype(jnp.int32)
        pieces = [bf16_pieces(value) for value in q_next]
        for direction, chosen, out_ref in ((0, going_up, up_ref), (1, going_down, dn_ref)):
            slot = slots[direction : direction + 1]
            place = ((low_iota == (slot & 127)) & chosen).astype(jnp.bfloat16)
            place = jnp.concatenate([place, place, place], axis=1)
            which = slot_iota == (slot >> 7)
            spread = jnp.concatenate(
                [
                    jnp.concatenate([jnp.where(which, piece, zero) for piece in pieces[k]], axis=1)
                    for k in range(3)
                ],
                axis=0,
            )
            out_ref[...] += lax.dot_general(spread, place, nt_dims, preferred_element_type=jnp.float32)
        return offsets + jnp.sum(flags, axis=1, keepdims=True)

    lax.fori_loop(0, count // CHUNK, body, start_ref[...])


def stress_partials(slab, q_state, element, migration, slab_elems, n_dev):
    groups = slab_elems // 128
    rows = round_up(3 * groups, 16)
    count = q_state.shape[1]
    vmem = pl.BlockSpec(memory_space=pltpu.VMEM)
    return pl.pallas_call(
        functools.partial(stress_kernel, groups=groups, rows=rows),
        out_shape=jax.ShapeDtypeStruct((n_dev, 12, 128), jnp.float32),
        in_specs=[pl.BlockSpec(memory_space=pltpu.SMEM)] + [vmem] * 3,
        out_specs=vmem,
        scratch_shapes=[pltpu.VMEM((4 * rows, 128), jnp.float32)],
        cost_estimate=pl.CostEstimate(
            flops=2 * 3 * 4 * rows * 128 * count, transcendentals=0, bytes_accessed=20 * count
        ),
    )(slab, q_state, element.reshape(1, -1), migration.reshape(1, -1))


def first_kernel(pt_ref, ft_ref, vout_ref, send_ref):
    own = vout_ref.shape[0]
    rows = [
        damping * jnp.sum(pt_ref[b] * ft_ref[:, b : b + 1], axis=0, keepdims=True)
        for b in range(own)
    ]
    fresh = jnp.concatenate(rows, axis=0)
    vout_ref[...] = fresh
    for k in range(send_ref.shape[0] // own):
        send_ref[k * own : (k + 1) * own, :] = fresh


def first_velocity(transposed, force_t, copies):
    own, size = transposed.shape[0], transposed.shape[1]
    return pl.pallas_call(
        first_kernel,
        out_shape=(
            jax.ShapeDtypeStruct((own, size), jnp.float32),
            jax.ShapeDtypeStruct((copies * own, size), jnp.float32),
        ),
        cost_estimate=pl.CostEstimate(
            flops=2 * transposed.size, transcendentals=0, bytes_accessed=4 * transposed.size
        ),
    )(transposed, force_t)


def update_and_pack(q_state, increments, element, migration, table, capacity):
    rows, slab_elems = table.shape
    groups = slab_elems // 128
    groups16 = round_up(groups, 16)
    slots = capacity // 128
    slots16 = round_up(slots, 16)
    arranged = jnp.pad(table.reshape(rows, groups, 128), ((0, 0), (0, groups16 - groups), (0, 0)))
    arranged = arranged.reshape(rows * groups16, 128)
    hi = lax.reduce_precision(arranged, exponent_bits=8, mantissa_bits=7)
    rest = arranged - hi
    mid = lax.reduce_precision(rest, exponent_bits=8, mantissa_bits=7)
    lo = rest - mid
    pieces = jnp.concatenate([hi, mid, lo], axis=1).astype(jnp.bfloat16)
    count = q_state.shape[1]
    parts = UPDATE_PARTS
    share = count // parts
    flags = jnp.stack([migration == 1, migration == -1]).astype(jnp.float32)
    per_part = jnp.sum(flags.reshape(2, parts, share), axis=2)
    starts = jnp.cumsum(per_part, axis=1) - per_part
    starts = jnp.pad(starts.T, ((0, 0), (0, 6)))[:, :, None]
    q_parts, up, down = [], 0.0, 0.0
    for part in range(parts):
        q_part, up_part, down_part = pl.pallas_call(
            functools.partial(
                update_kernel, groups16=groups16, slots16=slots16, first=part * share // CHUNK
            ),
            out_shape=(
                jax.ShapeDtypeStruct((3, share), jnp.float32),
                jax.ShapeDtypeStruct((3 * slots16, 128), jnp.float32),
                jax.ShapeDtypeStruct((3 * slots16, 128), jnp.float32),
            ),
            scratch_shapes=[pltpu.VMEM((CHUNK, CHUNK), jnp.bfloat16)],
            cost_estimate=pl.CostEstimate(
                flops=16 * 3 * (5 * groups16 + 6 * slots16) * 128 * share,
                transcendentals=0,
                bytes_accessed=40 * share,
            ),
        )(
            q_state,
            increments,
            element.reshape(1, -1),
            migration.reshape(1, -1),
            pieces,
            starts[part],
        )
        q_parts.append(q_part)
        up = up + up_part
        down = down + down_part
    q_next = jnp.concatenate(q_parts, axis=1)

    def unpack(acc):
        return acc.reshape(3, slots16, 128)[:, :slots].reshape(3, slots * 128)

    return q_next, unpack(up), unpack(down)


def own_kernel(v_ref, ft_ref, s_hbm, rest_ref, s_buf, sems):
    own = v_ref.shape[0]
    copies = [pltpu.make_async_copy(s_hbm.at[b, 0], s_buf.at[b], sems.at[b]) for b in range(own)]
    for copy in copies:
        copy.start()
    for b in range(own):
        copies[b].wait()
        image = jnp.sum(s_buf[b] * v_ref[b : b + 1, :], axis=1, keepdims=True)
        rest_ref[:, b : b + 1] = ft_ref[:, b : b + 1] - image


def own_term(velocity, force_t, stiffness):
    own, size = velocity.shape
    vmem = pl.BlockSpec(memory_space=pltpu.VMEM)
    return pl.pallas_call(
        own_kernel,
        out_shape=jax.ShapeDtypeStruct(force_t.shape, jnp.float32),
        in_specs=[vmem, vmem, pl.BlockSpec(memory_space=pl.ANY)],
        out_specs=vmem,
        scratch_shapes=[
            pltpu.VMEM((own, size, size), jnp.float32),
            pltpu.SemaphoreType.DMA((own,)),
        ],
        cost_estimate=pl.CostEstimate(
            flops=2 * own * size * size, transcendentals=0, bytes_accessed=4 * own * size * size
        ),
    )(velocity, force_t, stiffness)


def sweep_kernel(
    idx_ref, g_ref, s_hbm, pt_hbm, rest_ref, v_ref, vout_ref, send_ref, s_buf, pt_buf, sems
):
    total = g_ref.shape[0]
    own = v_ref.shape[0]
    width = s_buf.shape[1] + 1
    s_copies = [
        pltpu.make_async_copy(s_hbm.at[b, pl.ds(1, width - 1)], s_buf.at[b], sems.at[b])
        for b in range(own)
    ]
    p_copies = [pltpu.make_async_copy(pt_hbm.at[b], pt_buf.at[b], sems.at[own + b]) for b in range(own)]
    for b in range(own):
        s_copies[b].start()
        p_copies[b].start()
    rows = []
    for b in range(own):
        s_copies[b].wait()
        acc = None
        for n in range(1, width):
            w = idx_ref[b * width + n]
            inside = jnp.logical_and(w >= 0, w < total)
            near = g_ref[pl.ds(jnp.clip(w, 0, total - 1), 1), :]
            near = jnp.where(inside, near, 0.0)
            term = s_buf[b, n - 1] * near
            acc = term if acc is None else acc + term
        image = jnp.sum(acc, axis=1, keepdims=True)
        rest = rest_ref[:, b : b + 1] - image
        p_copies[b].wait()
        update = jnp.sum(pt_buf[b] * rest, axis=0, keepdims=True)
        rows.append(v_ref[b : b + 1, :] + damping * update)
    fresh = jnp.concatenate(rows, axis=0)
    vout_ref[...] = fresh
    for k in range(send_ref.shape[0] // own):
        send_ref[k * own : (k + 1) * own, :] = fresh


def sweep(where_read, gathered, stiffness, transposed, rest_t, velocity, copies):
    own, size = velocity.shape
    width = stiffness.shape[1]
    vmem = pl.BlockSpec(memory_space=pltpu.VMEM)
    anywhere = pl.BlockSpec(memory_space=pl.ANY)
    return pl.pallas_call(
        sweep_kernel,
        out_shape=(
            jax.ShapeDtypeStruct(velocity.shape, jnp.float32),
            jax.ShapeDtypeStruct((copies * own, size), jnp.float32),
        ),
        in_specs=[pl.BlockSpec(memory_space=pltpu.SMEM), vmem, anywhere, anywhere, vmem, vmem],
        out_specs=(vmem, vmem),
        scratch_shapes=[
            pltpu.VMEM((own, width - 1, size, size), jnp.float32),
            pltpu.VMEM(transposed.shape, jnp.float32),
            pltpu.SemaphoreType.DMA((2 * own,)),
        ],
        cost_estimate=pl.CostEstimate(
            flops=2 * (stiffness.size + transposed.size),
            transcendentals=0,
            bytes_accessed=4 * (stiffness.size + transposed.size + gathered.size),
        ),
    )(where_read, gathered, stiffness, transposed, rest_t, velocity)

def passed_along(array, axis, by):
    size = lax.axis_size(axis)
    pairs = [(i, i + by) for i in range(size) if 0 <= i + by < size]
    return lax.ppermute(array, axis, pairs)


def body(
    q_state,
    increments,
    velocity_grad,
    element,
    migration,
    volume,
    div_map,
    stiffness,
    pattern,
    preconditioner,
):
    capacity = migration.shape[0] // 16
    slab_elems = velocity_grad.shape[1]
    n_slab = lax.axis_size("slab")
    slab = lax.axis_index("slab")

    n_rad = lax.axis_size("rad")
    send = stress_partials(
        slab.reshape(1).astype(jnp.int32), q_state, element, migration, slab_elems, n_slab * n_rad
    )
    received = lax.all_to_all(send, ("slab", "rad"), 0, 0, tiled=True)
    sums = jnp.sum(received, axis=0).reshape(4, slab_elems // n_rad)
    element_stress = sums / volume

    q_next, upward, downward = update_and_pack(
        q_state, increments, element, migration, velocity_grad, capacity
    )
    from_lower = passed_along(upward, "slab", 1)
    from_upper = passed_along(downward, "slab", -1)
    arrivals = jnp.stack([from_lower, from_upper])

    own_blocks = stiffness.shape[0]
    groups = (
        element_stress.reshape(4, own_blocks, BLOCK // 4)
        .transpose(1, 0, 2)
        .reshape(own_blocks, BLOCK)
    )
    force = jnp.dot(groups, div_map, precision=highest)

    def precondition(vector):
        return jnp.einsum("bij,bj->bi", preconditioner, vector, precision=highest)

    slab_blocks = own_blocks * n_rad
    copies = n_slab * n_rad
    where_read = ((slab - 1) * slab_blocks + pattern).reshape(-1).astype(jnp.int32)
    transposed = jnp.swapaxes(preconditioner, 1, 2)
    force_t = force.T
    velocity, send = first_velocity(transposed, force_t, copies)
    for sweep_index in range(1, ITERS):
        gathered = lax.all_to_all(send, ("slab", "rad"), 0, 0, tiled=True)
        rest_t = own_term(velocity, force_t, stiffness)
        velocity, send = sweep(
            where_read, gathered, stiffness, transposed, rest_t, velocity, copies
        )
    return (q_next, arrivals, element_stress, velocity)


def solution(mesh):
    placed = (
        P(None, ("slab", "rad")),
        P(None, ("slab", "rad")),
        P(None, "slab"),
        P(("slab", "rad")),
        P(("slab", "rad")),
        P(("slab", "rad")),
        P(),
        P(("slab", "rad"), None, None, None),
        P(("slab", "rad"), None),
        P(("slab", "rad"), None, None),
    )
    return jax.shard_map(
        body,
        mesh=mesh,
        in_specs=placed,
        out_specs=(
            P(None, ("slab", "rad")),
            P(None, None, ("slab", "rad")),
            P(None, ("slab", "rad")),
            P(("slab", "rad"), None),
        ),
        check_vma=False,
    )
```

```python
import functools

import jax
import jax.numpy as jnp
from jax import lax
from jax.experimental import pallas as pl
from jax.experimental.pallas import tpu as pltpu
from jax.sharding import PartitionSpec as P

BLOCK = 192
ITERS = 6
CHUNK = 512
STRESS_CHUNK = 1024
UPDATE_PARTS = 4

extensibility = 50.0
time_step = 0.01
noise_scale = 0.1
damping = 0.6
highest = lax.Precision.HIGHEST
nt_dims = (((1,), (1,)), ((), ()))


def round_up(value, step):
    return -(-value // step) * step


def bf16_pieces(x):
    hi = x.astype(jnp.bfloat16)
    rest = x - hi.astype(jnp.float32)
    mid = rest.astype(jnp.bfloat16)
    lo = (rest - mid.astype(jnp.float32)).astype(jnp.bfloat16)
    return (hi, mid, lo)


def spring_terms(q):
    radial = q[0:1]
    axial = q[1:2]
    azimuth = q[2:3]
    stretch = radial * radial + axial * axial + azimuth * azimuth
    spring = 1.0 / (1.0 - stretch / extensibility)
    terms = (
        spring * radial * radial - 1.0,
        spring * axial * axial - 1.0,
        spring * radial * axial,
        spring * azimuth * azimuth - 1.0,
    )
    return spring, terms


def stress_kernel(slab_ref, q_ref, e_ref, m_ref, send_ref, acc_ref, *, groups, rows):
    count = q_ref.shape[1]
    n_dev = send_ref.shape[0]
    n_rad = groups // 3
    acc_ref[...] = jnp.zeros_like(acc_ref)
    low_iota = lax.broadcasted_iota(jnp.int32, (128, STRESS_CHUNK), 0)
    row_iota = lax.broadcasted_iota(jnp.int32, (rows, STRESS_CHUNK), 0)
    zero = jnp.zeros((), jnp.bfloat16)

    def body(step, carry):
        cols = pl.ds(pl.multiple_of(step * STRESS_CHUNK, STRESS_CHUNK), STRESS_CHUNK)
        q = q_ref[:, cols]
        element = e_ref[:, cols]
        move = m_ref[:, cols]
        spring, terms = spring_terms(q)
        kind = jnp.where(move == 0, 1, jnp.where(move == 1, 2, 0))
        key = kind * groups + (element >> 7)
        low = (low_iota == (element & 127)).astype(jnp.bfloat16)
        low = jnp.concatenate([low, low, low], axis=1)
        mask = row_iota == key
        spread = jnp.concatenate(
            [
                jnp.concatenate([jnp.where(mask, piece, zero) for piece in bf16_pieces(term)], axis=1)
                for term in terms
            ],
            axis=0,
        )
        acc_ref[...] += lax.dot_general(spread, low, nt_dims, preferred_element_type=jnp.float32)
        return carry

    lax.fori_loop(0, count // STRESS_CHUNK, body, 0)
    send_ref[...] = jnp.zeros_like(send_ref)
    slab = slab_ref[0]
    for kind in range(3):
        target = slab - 1 + kind

        @pl.when(jnp.logical_and(target >= 0, target * n_rad < n_dev))
        def _():
            for r in range(n_rad):
                for c in range(4):
                    start = c * rows + kind * groups + r * 3
                    send_ref[target * n_rad + r, c * 3 : c * 3 + 3, :] = acc_ref[start : start + 3, :]


def update_kernel(
    q_ref, inc_ref, e_ref, m_ref, tab_ref, start_ref, after_ref, qn_ref, up_ref, dn_ref, tri_ref, *, groups16, slots16, first
):
    count = qn_ref.shape[1]
    up_ref[...] = jnp.zeros_like(up_ref)
    dn_ref[...] = jnp.zeros_like(dn_ref)
    before = lax.broadcasted_iota(jnp.int32, (CHUNK, CHUNK), 0)
    after = lax.broadcasted_iota(jnp.int32, (CHUNK, CHUNK), 1)
    tri_ref[...] = (before < after).astype(jnp.bfloat16)
    low_iota = lax.broadcasted_iota(jnp.int32, (128, CHUNK), 0)
    group_iota = lax.broadcasted_iota(jnp.int32, (groups16, CHUNK), 0)
    slot_iota = lax.broadcasted_iota(jnp.int32, (slots16, CHUNK), 0)
    flag_row = lax.broadcasted_iota(jnp.int32, (8, CHUNK), 0)
    zero = jnp.zeros((), jnp.bfloat16)

    def body(step, offsets):
        cols = pl.ds(pl.multiple_of((first + step) * CHUNK, CHUNK), CHUNK)
        q = q_ref[:, cols]
        inc = inc_ref[:, cols]
        element = e_ref[:, cols]
        move = m_ref[:, cols]
        low = (low_iota == (element & 127)).astype(jnp.bfloat16)
        picked = jnp.dot(
            tab_ref[...], jnp.concatenate([low, low, low], axis=0), preferred_element_type=jnp.float32
        )
        hit = group_iota == (element >> 7)
        grads = [
            jnp.sum(
                jnp.where(hit, picked[c * groups16 : (c + 1) * groups16], 0.0),
                axis=0,
                keepdims=True,
            )
            for c in range(5)
        ]
        radial = q[0:1]
        axial = q[1:2]
        azimuth = q[2:3]
        spring, terms = spring_terms(q)
        drift = (
            grads[0] * radial + grads[1] * axial,
            grads[2] * radial + grads[3] * axial,
            grads[4] * azimuth,
        )
        q_next = [
            q[k : k + 1] + time_step * (drift[k] - 0.5 * spring * q[k : k + 1]) + noise_scale * inc[k : k + 1]
            for k in range(3)
        ]
        qn_ref[:, pl.ds(pl.multiple_of(step * CHUNK, CHUNK), CHUNK)] = jnp.concatenate(q_next, axis=0)
        going_up = move == 1
        going_down = move == -1
        flags = jnp.where(
            flag_row == 0,
            going_up.astype(jnp.float32),
            jnp.where(flag_row == 1, going_down.astype(jnp.float32), 0.0),
        )
        ranks = jnp.dot(flags.astype(jnp.bfloat16), tri_ref[...], preferred_element_type=jnp.float32)
        slots = (ranks + offsets).astype(jnp.int32)
        pieces = [bf16_pieces(value) for value in q_next]
        for direction, chosen, out_ref in ((0, going_up, up_ref), (1, going_down, dn_ref)):
            slot = slots[direction : direction + 1]
            place = ((low_iota == (slot & 127)) & chosen).astype(jnp.bfloat16)
            place = jnp.concatenate([place, place, place], axis=1)
            which = slot_iota == (slot >> 7)
            spread = jnp.concatenate(
                [
                    jnp.concatenate([jnp.where(which, piece, zero) for piece in pieces[k]], axis=1)
                    for k in range(3)
                ],
                axis=0,
            )
            out_ref[...] += lax.dot_general(spread, place, nt_dims, preferred_element_type=jnp.float32)
        return offsets + jnp.sum(flags, axis=1, keepdims=True)

    lax.fori_loop(0, count // CHUNK, body, start_ref[...])


def stress_partials(slab, q_state, element, migration, slab_elems, n_dev):
    groups = slab_elems // 128
    rows = round_up(3 * groups, 16)
    count = q_state.shape[1]
    vmem = pl.BlockSpec(memory_space=pltpu.VMEM)
    return pl.pallas_call(
        functools.partial(stress_kernel, groups=groups, rows=rows),
        out_shape=jax.ShapeDtypeStruct((n_dev, 12, 128), jnp.float32),
        in_specs=[pl.BlockSpec(memory_space=pltpu.SMEM)] + [vmem] * 3,
        out_specs=vmem,
        scratch_shapes=[pltpu.VMEM((4 * rows, 128), jnp.float32)],
        cost_estimate=pl.CostEstimate(
            flops=2 * 3 * 4 * rows * 128 * count, transcendentals=0, bytes_accessed=20 * count
        ),
    )(slab, q_state, element.reshape(1, -1), migration.reshape(1, -1))


def first_kernel(pt_ref, ft_ref, vout_ref, send_ref):
    own = vout_ref.shape[0]
    rows = [
        damping * jnp.sum(pt_ref[b] * ft_ref[:, b : b + 1], axis=0, keepdims=True)
        for b in range(own)
    ]
    fresh = jnp.concatenate(rows, axis=0)
    vout_ref[...] = fresh
    for k in range(send_ref.shape[0] // own):
        send_ref[k * own : (k + 1) * own, :] = fresh


def first_velocity(transposed, force_t, copies):
    own, size = transposed.shape[0], transposed.shape[1]
    return pl.pallas_call(
        first_kernel,
        out_shape=(
            jax.ShapeDtypeStruct((own, size), jnp.float32),
            jax.ShapeDtypeStruct((copies * own, size), jnp.float32),
        ),
        cost_estimate=pl.CostEstimate(
            flops=2 * transposed.size, transcendentals=0, bytes_accessed=4 * transposed.size
        ),
    )(transposed, force_t)


def update_prepare(migration, table, capacity, count):
    rows, slab_elems = table.shape
    groups = slab_elems // 128
    groups16 = round_up(groups, 16)
    slots = capacity // 128
    slots16 = round_up(slots, 16)
    arranged = jnp.pad(table.reshape(rows, groups, 128), ((0, 0), (0, groups16 - groups), (0, 0)))
    arranged = arranged.reshape(rows * groups16, 128)
    hi = lax.reduce_precision(arranged, exponent_bits=8, mantissa_bits=7)
    rest = arranged - hi
    mid = lax.reduce_precision(rest, exponent_bits=8, mantissa_bits=7)
    lo = rest - mid
    pieces = jnp.concatenate([hi, mid, lo], axis=1).astype(jnp.bfloat16)
    share = count // UPDATE_PARTS
    flags = jnp.stack([migration == 1, migration == -1]).astype(jnp.float32)
    per_part = jnp.sum(flags.reshape(2, UPDATE_PARTS, share), axis=2)
    starts = jnp.cumsum(per_part, axis=1) - per_part
    starts = jnp.pad(starts.T, ((0, 0), (0, 6)))[:, :, None]
    return pieces, starts, groups16, slots16


def update_part(part, prepared, after, q_state, increments, element, migration):
    pieces, starts, groups16, slots16 = prepared
    share = q_state.shape[1] // UPDATE_PARTS
    vmem = pl.BlockSpec(memory_space=pltpu.VMEM)
    return pl.pallas_call(
        functools.partial(
            update_kernel, groups16=groups16, slots16=slots16, first=part * share // CHUNK
        ),
        out_shape=(
            jax.ShapeDtypeStruct((3, share), jnp.float32),
            jax.ShapeDtypeStruct((3 * slots16, 128), jnp.float32),
            jax.ShapeDtypeStruct((3 * slots16, 128), jnp.float32),
        ),
        in_specs=[vmem] * 6 + [pl.BlockSpec(memory_space=pl.ANY)],
        out_specs=(vmem, vmem, vmem),
        scratch_shapes=[pltpu.VMEM((CHUNK, CHUNK), jnp.bfloat16)],
        cost_estimate=pl.CostEstimate(
            flops=16 * 3 * (5 * groups16 + 6 * slots16) * 128 * share,
            transcendentals=0,
            bytes_accessed=40 * share,
        ),
    )(
        q_state,
        increments,
        element.reshape(1, -1),
        migration.reshape(1, -1),
        pieces,
        starts[part],
        after,
    )


def unpack(acc, capacity):
    slots = capacity // 128
    return acc.reshape(3, -1, 128)[:, :slots].reshape(3, slots * 128)


def sweep_kernel(idx_ref, g_ref, s_ref, pt_ref, ft_ref, v_ref, vout_ref, send_ref):
    total = g_ref.shape[0]
    own = v_ref.shape[0]
    width = s_ref.shape[1]
    rows = []
    for b in range(own):
        acc = None
        for n in range(width):
            w = idx_ref[b * width + n]
            inside = jnp.logical_and(w >= 0, w < total)
            near = g_ref[pl.ds(jnp.clip(w, 0, total - 1), 1), :]
            near = jnp.where(inside, near, 0.0)
            term = s_ref[b, n] * near
            acc = term if acc is None else acc + term
        image = jnp.sum(acc, axis=1, keepdims=True)
        rest = ft_ref[:, b : b + 1] - image
        update = jnp.sum(pt_ref[b] * rest, axis=0, keepdims=True)
        rows.append(v_ref[b : b + 1, :] + damping * update)
    fresh = jnp.concatenate(rows, axis=0)
    vout_ref[...] = fresh
    for k in range(send_ref.shape[0] // own):
        send_ref[k * own : (k + 1) * own, :] = fresh


def sweep(where_read, gathered, stiffness, transposed, force_t, velocity, copies):
    own = velocity.shape[0]
    vmem = pl.BlockSpec(memory_space=pltpu.VMEM)
    return pl.pallas_call(
        sweep_kernel,
        out_shape=(
            jax.ShapeDtypeStruct(velocity.shape, jnp.float32),
            jax.ShapeDtypeStruct((copies * own, velocity.shape[1]), jnp.float32),
        ),
        in_specs=[pl.BlockSpec(memory_space=pltpu.SMEM)] + [vmem] * 5,
        out_specs=(vmem, vmem),
        cost_estimate=pl.CostEstimate(
            flops=2 * (stiffness.size + transposed.size),
            transcendentals=0,
            bytes_accessed=4 * (stiffness.size + transposed.size + gathered.size),
        ),
    )(where_read, gathered, stiffness, transposed, force_t, velocity)


def passed_along(array, axis, by):
    size = lax.axis_size(axis)
    pairs = [(i, i + by) for i in range(size) if 0 <= i + by < size]
    return lax.ppermute(array, axis, pairs)


def body(
    q_state,
    increments,
    velocity_grad,
    element,
    migration,
    volume,
    div_map,
    stiffness,
    pattern,
    preconditioner,
):
    capacity = migration.shape[0] // 16
    slab_elems = velocity_grad.shape[1]
    n_slab = lax.axis_size("slab")
    slab = lax.axis_index("slab")

    n_rad = lax.axis_size("rad")
    send = stress_partials(
        slab.reshape(1).astype(jnp.int32), q_state, element, migration, slab_elems, n_slab * n_rad
    )
    received = lax.all_to_all(send, ("slab", "rad"), 0, 0, tiled=True)
    sums = jnp.sum(received, axis=0).reshape(4, slab_elems // n_rad)
    element_stress = sums / volume

    prepared = update_prepare(migration, velocity_grad, capacity, q_state.shape[1])

    own_blocks = stiffness.shape[0]
    groups = (
        element_stress.reshape(4, own_blocks, BLOCK // 4)
        .transpose(1, 0, 2)
        .reshape(own_blocks, BLOCK)
    )
    force = jnp.dot(groups, div_map, precision=highest)

    def precondition(vector):
        return jnp.einsum("bij,bj->bi", preconditioner, vector, precision=highest)

    slab_blocks = own_blocks * n_rad
    copies = n_slab * n_rad
    where_read = ((slab - 1) * slab_blocks + pattern).reshape(-1).astype(jnp.int32)
    transposed = jnp.swapaxes(preconditioner, 1, 2)
    force_t = force.T
    velocity, send = first_velocity(transposed, force_t, copies)
    q_parts, upward, downward = [], 0.0, 0.0
    for sweep_index in range(1, ITERS):
        if len(q_parts) < UPDATE_PARTS:
            q_part, up_part, down_part = update_part(
                len(q_parts), prepared, velocity, q_state, increments, element, migration
            )
            q_parts.append(q_part)
            upward = upward + up_part
            downward = downward + down_part
        gathered = lax.all_to_all(send, ("slab", "rad"), 0, 0, tiled=True)
        velocity, send = sweep(
            where_read, gathered, stiffness, transposed, force_t, velocity, copies
        )
    while len(q_parts) < UPDATE_PARTS:
        q_part, up_part, down_part = update_part(
            len(q_parts), prepared, velocity, q_state, increments, element, migration
        )
        q_parts.append(q_part)
        upward = upward + up_part
        downward = downward + down_part
    q_next = jnp.concatenate(q_parts, axis=1)
    from_lower = passed_along(unpack(upward, capacity), "slab", 1)
    from_upper = passed_along(unpack(downward, capacity), "slab", -1)
    arrivals = jnp.stack([from_lower, from_upper])
    return (q_next, arrivals, element_stress, velocity)


def solution(mesh):
    placed = (
        P(None, ("slab", "rad")),
        P(None, ("slab", "rad")),
        P(None, "slab"),
        P(("slab", "rad")),
        P(("slab", "rad")),
        P(("slab", "rad")),
        P(),
        P(("slab", "rad"), None, None, None),
        P(("slab", "rad"), None),
        P(("slab", "rad"), None, None),
    )
    return jax.shard_map(
        body,
        mesh=mesh,
        in_specs=placed,
        out_specs=(
            P(None, ("slab", "rad")),
            P(None, None, ("slab", "rad")),
            P(None, ("slab", "rad")),
            P(("slab", "rad"), None),
        ),
        check_vma=False,
    )
```

```python
import functools

import jax
import jax.numpy as jnp
from jax import lax
from jax.experimental import pallas as pl
from jax.experimental.pallas import tpu as pltpu
from jax.sharding import PartitionSpec as P

BLOCK = 192
ITERS = 6
CHUNK = 512
STRESS_CHUNK = 1024
UPDATE_PARTS = 4

extensibility = 50.0
time_step = 0.01
noise_scale = 0.1
damping = 0.6
highest = lax.Precision.HIGHEST
nt_dims = (((1,), (1,)), ((), ()))


def round_up(value, step):
    return -(-value // step) * step


def bf16_pieces(x):
    hi = x.astype(jnp.bfloat16)
    rest = x - hi.astype(jnp.float32)
    mid = rest.astype(jnp.bfloat16)
    lo = (rest - mid.astype(jnp.float32)).astype(jnp.bfloat16)
    return (hi, mid, lo)


def spring_terms(q):
    radial = q[0:1]
    axial = q[1:2]
    azimuth = q[2:3]
    stretch = radial * radial + axial * axial + azimuth * azimuth
    spring = 1.0 / (1.0 - stretch / extensibility)
    terms = (
        spring * radial * radial - 1.0,
        spring * axial * axial - 1.0,
        spring * radial * axial,
        spring * azimuth * azimuth - 1.0,
    )
    return spring, terms


def stress_kernel(slab_ref, q_ref, e_ref, m_ref, send_ref, acc_ref, *, groups, rows):
    count = q_ref.shape[1]
    n_dev = send_ref.shape[0]
    n_rad = groups // 3
    acc_ref[...] = jnp.zeros_like(acc_ref)
    low_iota = lax.broadcasted_iota(jnp.int32, (128, STRESS_CHUNK), 0)
    row_iota = lax.broadcasted_iota(jnp.int32, (rows, STRESS_CHUNK), 0)
    zero = jnp.zeros((), jnp.bfloat16)

    def body(step, carry):
        cols = pl.ds(pl.multiple_of(step * STRESS_CHUNK, STRESS_CHUNK), STRESS_CHUNK)
        q = q_ref[:, cols]
        element = e_ref[:, cols]
        move = m_ref[:, cols]
        spring, terms = spring_terms(q)
        kind = jnp.where(move == 0, 1, jnp.where(move == 1, 2, 0))
        key = kind * groups + (element >> 7)
        low = (low_iota == (element & 127)).astype(jnp.bfloat16)
        low = jnp.concatenate([low, low, low], axis=1)
        mask = row_iota == key
        spread = jnp.concatenate(
            [
                jnp.concatenate([jnp.where(mask, piece, zero) for piece in bf16_pieces(term)], axis=1)
                for term in terms
            ],
            axis=0,
        )
        acc_ref[...] += lax.dot_general(spread, low, nt_dims, preferred_element_type=jnp.float32)
        return carry

    lax.fori_loop(0, count // STRESS_CHUNK, body, 0)
    send_ref[...] = jnp.zeros_like(send_ref)
    slab = slab_ref[0]
    for kind in range(3):
        target = slab - 1 + kind

        @pl.when(jnp.logical_and(target >= 0, target * n_rad < n_dev))
        def _():
            for r in range(n_rad):
                for c in range(4):
                    start = c * rows + kind * groups + r * 3
                    send_ref[target * n_rad + r, c * 3 : c * 3 + 3, :] = acc_ref[start : start + 3, :]


def update_kernel(
    q_ref, inc_ref, e_ref, m_ref, tab_ref, start_ref, qn_ref, up_ref, dn_ref, tri_ref, *, groups16, slots16, first
):
    count = qn_ref.shape[1]
    up_ref[...] = jnp.zeros_like(up_ref)
    dn_ref[...] = jnp.zeros_like(dn_ref)
    before = lax.broadcasted_iota(jnp.int32, (CHUNK, CHUNK), 0)
    after = lax.broadcasted_iota(jnp.int32, (CHUNK, CHUNK), 1)
    tri_ref[...] = (before < after).astype(jnp.bfloat16)
    low_iota = lax.broadcasted_iota(jnp.int32, (128, CHUNK), 0)
    group_iota = lax.broadcasted_iota(jnp.int32, (groups16, CHUNK), 0)
    slot_iota = lax.broadcasted_iota(jnp.int32, (slots16, CHUNK), 0)
    flag_row = lax.broadcasted_iota(jnp.int32, (8, CHUNK), 0)
    zero = jnp.zeros((), jnp.bfloat16)

    def body(step, offsets):
        cols = pl.ds(pl.multiple_of((first + step) * CHUNK, CHUNK), CHUNK)
        q = q_ref[:, cols]
        inc = inc_ref[:, cols]
        element = e_ref[:, cols]
        move = m_ref[:, cols]
        low = (low_iota == (element & 127)).astype(jnp.bfloat16)
        picked = jnp.dot(
            tab_ref[...], jnp.concatenate([low, low, low], axis=0), preferred_element_type=jnp.float32
        )
        hit = group_iota == (element >> 7)
        grads = [
            jnp.sum(
                jnp.where(hit, picked[c * groups16 : (c + 1) * groups16], 0.0),
                axis=0,
                keepdims=True,
            )
            for c in range(5)
        ]
        radial = q[0:1]
        axial = q[1:2]
        azimuth = q[2:3]
        spring, terms = spring_terms(q)
        drift = (
            grads[0] * radial + grads[1] * axial,
            grads[2] * radial + grads[3] * axial,
            grads[4] * azimuth,
        )
        q_next = [
            q[k : k + 1] + time_step * (drift[k] - 0.5 * spring * q[k : k + 1]) + noise_scale * inc[k : k + 1]
            for k in range(3)
        ]
        qn_ref[:, pl.ds(pl.multiple_of(step * CHUNK, CHUNK), CHUNK)] = jnp.concatenate(q_next, axis=0)
        going_up = move == 1
        going_down = move == -1
        flags = jnp.where(
            flag_row == 0,
            going_up.astype(jnp.float32),
            jnp.where(flag_row == 1, going_down.astype(jnp.float32), 0.0),
        )
        ranks = jnp.dot(flags.astype(jnp.bfloat16), tri_ref[...], preferred_element_type=jnp.float32)
        slots = (ranks + offsets).astype(jnp.int32)
        pieces = [bf16_pieces(value) for value in q_next]
        for direction, chosen, out_ref in ((0, going_up, up_ref), (1, going_down, dn_ref)):
            slot = slots[direction : direction + 1]
            place = ((low_iota == (slot & 127)) & chosen).astype(jnp.bfloat16)
            place = jnp.concatenate([place, place, place], axis=1)
            which = slot_iota == (slot >> 7)
            spread = jnp.concatenate(
                [
                    jnp.concatenate([jnp.where(which, piece, zero) for piece in pieces[k]], axis=1)
                    for k in range(3)
                ],
                axis=0,
            )
            out_ref[...] += lax.dot_general(spread, place, nt_dims, preferred_element_type=jnp.float32)
        return offsets + jnp.sum(flags, axis=1, keepdims=True)

    lax.fori_loop(0, count // CHUNK, body, start_ref[...])


def stress_partials(slab, q_state, element, migration, slab_elems, n_dev):
    groups = slab_elems // 128
    rows = round_up(3 * groups, 16)
    count = q_state.shape[1]
    vmem = pl.BlockSpec(memory_space=pltpu.VMEM)
    return pl.pallas_call(
        functools.partial(stress_kernel, groups=groups, rows=rows),
        out_shape=jax.ShapeDtypeStruct((n_dev, 12, 128), jnp.float32),
        in_specs=[pl.BlockSpec(memory_space=pltpu.SMEM)] + [vmem] * 3,
        out_specs=vmem,
        scratch_shapes=[pltpu.VMEM((4 * rows, 128), jnp.float32)],
        cost_estimate=pl.CostEstimate(
            flops=2 * 3 * 4 * rows * 128 * count, transcendentals=0, bytes_accessed=20 * count
        ),
    )(slab, q_state, element.reshape(1, -1), migration.reshape(1, -1))


def first_kernel(pt_ref, ft_ref, vout_ref, send_ref):
    own = vout_ref.shape[0]
    rows = [
        damping * jnp.sum(pt_ref[b] * ft_ref[:, b : b + 1], axis=0, keepdims=True)
        for b in range(own)
    ]
    fresh = jnp.concatenate(rows, axis=0)
    vout_ref[...] = fresh
    for k in range(send_ref.shape[0] // own):
        send_ref[k * own : (k + 1) * own, :] = fresh


def first_velocity(transposed, force_t, copies):
    own, size = transposed.shape[0], transposed.shape[1]
    return pl.pallas_call(
        first_kernel,
        out_shape=(
            jax.ShapeDtypeStruct((own, size), jnp.float32),
            jax.ShapeDtypeStruct((copies * own, size), jnp.float32),
        ),
        cost_estimate=pl.CostEstimate(
            flops=2 * transposed.size, transcendentals=0, bytes_accessed=4 * transposed.size
        ),
    )(transposed, force_t)


def update_and_pack(q_state, increments, element, migration, table, capacity):
    rows, slab_elems = table.shape
    groups = slab_elems // 128
    groups16 = round_up(groups, 16)
    slots = capacity // 128
    slots16 = round_up(slots, 16)
    arranged = jnp.pad(table.reshape(rows, groups, 128), ((0, 0), (0, groups16 - groups), (0, 0)))
    arranged = arranged.reshape(rows * groups16, 128)
    hi = lax.reduce_precision(arranged, exponent_bits=8, mantissa_bits=7)
    rest = arranged - hi
    mid = lax.reduce_precision(rest, exponent_bits=8, mantissa_bits=7)
    lo = rest - mid
    pieces = jnp.concatenate([hi, mid, lo], axis=1).astype(jnp.bfloat16)
    count = q_state.shape[1]
    parts = UPDATE_PARTS
    share = count // parts
    flags = jnp.stack([migration == 1, migration == -1]).astype(jnp.float32)
    per_part = jnp.sum(flags.reshape(2, parts, share), axis=2)
    starts = jnp.cumsum(per_part, axis=1) - per_part
    starts = jnp.pad(starts.T, ((0, 0), (0, 6)))[:, :, None]
    q_parts, up, down = [], 0.0, 0.0
    for part in range(parts):
        q_part, up_part, down_part = pl.pallas_call(
            functools.partial(
                update_kernel, groups16=groups16, slots16=slots16, first=part * share // CHUNK
            ),
            out_shape=(
                jax.ShapeDtypeStruct((3, share), jnp.float32),
                jax.ShapeDtypeStruct((3 * slots16, 128), jnp.float32),
                jax.ShapeDtypeStruct((3 * slots16, 128), jnp.float32),
            ),
            scratch_shapes=[pltpu.VMEM((CHUNK, CHUNK), jnp.bfloat16)],
            cost_estimate=pl.CostEstimate(
                flops=16 * 3 * (5 * groups16 + 6 * slots16) * 128 * share,
                transcendentals=0,
                bytes_accessed=40 * share,
            ),
        )(
            q_state,
            increments,
            element.reshape(1, -1),
            migration.reshape(1, -1),
            pieces,
            starts[part],
        )
        q_parts.append(q_part)
        up = up + up_part
        down = down + down_part
    q_next = jnp.concatenate(q_parts, axis=1)

    def unpack(acc):
        return acc.reshape(3, slots16, 128)[:, :slots].reshape(3, slots * 128)

    return q_next, unpack(up), unpack(down)


def sweep_kernel(idx_ref, g_ref, m_ref, v1_ref, v_ref, vout_ref, send_ref):
    total = g_ref.shape[0]
    own, size = v_ref.shape
    width = m_ref.shape[1]
    near = []
    for k in range(own * width):
        w = idx_ref[k]
        inside = jnp.logical_and(w >= 0, w < total)
        row = g_ref[pl.ds(jnp.clip(w, 0, total - 1), 1), :]
        near.append(jnp.where(inside, row, 0.0))
    lanes = round_up(size, 128)
    near = jnp.concatenate(near, axis=0)
    near = jnp.pad(near, ((0, 128 - own * width), (0, lanes - size)))
    columns = near.T
    rows = []
    for b in range(own):
        acc = None
        for n in range(width):
            k = b * width + n
            term = m_ref[b, n] * columns[:size, k : k + 1]
            acc = term if acc is None else acc + term
        image = jnp.sum(acc, axis=0, keepdims=True)
        rows.append(v_ref[b : b + 1, :] + v1_ref[b : b + 1, :] - damping * image)
    fresh = jnp.concatenate(rows, axis=0)
    vout_ref[...] = fresh
    for k in range(send_ref.shape[0] // own):
        send_ref[k * own : (k + 1) * own, :] = fresh


def sweep(where_read, gathered, merged, first, velocity, copies):
    own = velocity.shape[0]
    vmem = pl.BlockSpec(memory_space=pltpu.VMEM)
    return pl.pallas_call(
        sweep_kernel,
        out_shape=(
            jax.ShapeDtypeStruct(velocity.shape, jnp.float32),
            jax.ShapeDtypeStruct((copies * own, velocity.shape[1]), jnp.float32),
        ),
        in_specs=[pl.BlockSpec(memory_space=pltpu.SMEM)] + [vmem] * 4,
        out_specs=(vmem, vmem),
        cost_estimate=pl.CostEstimate(
            flops=2 * merged.size, transcendentals=0, bytes_accessed=4 * (merged.size + gathered.size)
        ),
    )(where_read, gathered, merged, first, velocity)

def passed_along(array, axis, by):
    size = lax.axis_size(axis)
    pairs = [(i, i + by) for i in range(size) if 0 <= i + by < size]
    return lax.ppermute(array, axis, pairs)


def body(
    q_state,
    increments,
    velocity_grad,
    element,
    migration,
    volume,
    div_map,
    stiffness,
    pattern,
    preconditioner,
):
    capacity = migration.shape[0] // 16
    slab_elems = velocity_grad.shape[1]
    n_slab = lax.axis_size("slab")
    slab = lax.axis_index("slab")

    n_rad = lax.axis_size("rad")
    send = stress_partials(
        slab.reshape(1).astype(jnp.int32), q_state, element, migration, slab_elems, n_slab * n_rad
    )
    received = lax.all_to_all(send, ("slab", "rad"), 0, 0, tiled=True)
    sums = jnp.sum(received, axis=0).reshape(4, slab_elems // n_rad)
    element_stress = sums / volume

    q_next, upward, downward = update_and_pack(
        q_state, increments, element, migration, velocity_grad, capacity
    )
    from_lower = passed_along(upward, "slab", 1)
    from_upper = passed_along(downward, "slab", -1)
    arrivals = jnp.stack([from_lower, from_upper])

    own_blocks = stiffness.shape[0]
    groups = (
        element_stress.reshape(4, own_blocks, BLOCK // 4)
        .transpose(1, 0, 2)
        .reshape(own_blocks, BLOCK)
    )
    force = jnp.dot(groups, div_map, precision=highest)

    def precondition(vector):
        return jnp.einsum("bij,bj->bi", preconditioner, vector, precision=highest)

    slab_blocks = own_blocks * n_rad
    copies = n_slab * n_rad
    where_read = ((slab - 1) * slab_blocks + pattern).reshape(-1).astype(jnp.int32)
    transposed = jnp.swapaxes(preconditioner, 1, 2)
    force_t = force.T
    velocity, send = first_velocity(transposed, force_t, copies)
    first = velocity
    merged = jnp.einsum("bik,bnkj->bnji", preconditioner, stiffness, precision=highest)
    for sweep_index in range(1, ITERS):
        gathered = lax.all_to_all(send, ("slab", "rad"), 0, 0, tiled=True)
        velocity, send = sweep(where_read, gathered, merged, first, velocity, copies)
    return (q_next, arrivals, element_stress, velocity)


def solution(mesh):
    placed = (
        P(None, ("slab", "rad")),
        P(None, ("slab", "rad")),
        P(None, "slab"),
        P(("slab", "rad")),
        P(("slab", "rad")),
        P(("slab", "rad")),
        P(),
        P(("slab", "rad"), None, None, None),
        P(("slab", "rad"), None),
        P(("slab", "rad"), None, None),
    )
    return jax.shard_map(
        body,
        mesh=mesh,
        in_specs=placed,
        out_specs=(
            P(None, ("slab", "rad")),
            P(None, None, ("slab", "rad")),
            P(None, ("slab", "rad")),
            P(("slab", "rad"), None),
        ),
        check_vma=False,
    )
```

```python
import functools

import jax
import jax.numpy as jnp
from jax import lax
from jax.experimental import pallas as pl
from jax.experimental.pallas import tpu as pltpu
from jax.sharding import PartitionSpec as P

BLOCK = 192
ITERS = 6
CHUNK = 512
STRESS_CHUNK = 1024
UPDATE_PARTS = 4

extensibility = 50.0
time_step = 0.01
noise_scale = 0.1
damping = 0.6
highest = lax.Precision.HIGHEST
nt_dims = (((1,), (1,)), ((), ()))


def round_up(value, step):
    return -(-value // step) * step


def bf16_pieces(x):
    hi = x.astype(jnp.bfloat16)
    rest = x - hi.astype(jnp.float32)
    mid = rest.astype(jnp.bfloat16)
    lo = (rest - mid.astype(jnp.float32)).astype(jnp.bfloat16)
    return (hi, mid, lo)


def spring_terms(q):
    radial = q[0:1]
    axial = q[1:2]
    azimuth = q[2:3]
    stretch = radial * radial + axial * axial + azimuth * azimuth
    spring = 1.0 / (1.0 - stretch / extensibility)
    terms = (
        spring * radial * radial - 1.0,
        spring * axial * axial - 1.0,
        spring * radial * axial,
        spring * azimuth * azimuth - 1.0,
    )
    return spring, terms


def stress_kernel(slab_ref, q_ref, e_ref, m_ref, send_ref, acc_ref, *, groups, rows):
    count = q_ref.shape[1]
    n_dev = send_ref.shape[0]
    n_rad = groups // 3
    acc_ref[...] = jnp.zeros_like(acc_ref)
    low_iota = lax.broadcasted_iota(jnp.int32, (128, STRESS_CHUNK), 0)
    row_iota = lax.broadcasted_iota(jnp.int32, (rows, STRESS_CHUNK), 0)
    zero = jnp.zeros((), jnp.bfloat16)

    def body(step, carry):
        cols = pl.ds(pl.multiple_of(step * STRESS_CHUNK, STRESS_CHUNK), STRESS_CHUNK)
        q = q_ref[:, cols]
        element = e_ref[:, cols]
        move = m_ref[:, cols]
        spring, terms = spring_terms(q)
        kind = jnp.where(move == 0, 1, jnp.where(move == 1, 2, 0))
        key = kind * groups + (element >> 7)
        low = (low_iota == (element & 127)).astype(jnp.bfloat16)
        low = jnp.concatenate([low, low], axis=1)
        mask = row_iota == key
        spread = jnp.concatenate(
            [
                jnp.concatenate(
                    [jnp.where(mask, piece, zero) for piece in bf16_pieces(term)[:2]], axis=1
                )
                for term in terms
            ],
            axis=0,
        )
        acc_ref[...] += lax.dot_general(spread, low, nt_dims, preferred_element_type=jnp.float32)
        return carry

    lax.fori_loop(0, count // STRESS_CHUNK, body, 0)
    send_ref[...] = jnp.zeros_like(send_ref)
    slab = slab_ref[0]
    for kind in range(3):
        target = slab - 1 + kind

        @pl.when(jnp.logical_and(target >= 0, target * n_rad < n_dev))
        def _():
            for r in range(n_rad):
                for c in range(4):
                    start = c * rows + kind * groups + r * 3
                    send_ref[target * n_rad + r, c * 3 : c * 3 + 3, :] = acc_ref[start : start + 3, :]


def update_kernel(
    q_ref, inc_ref, e_ref, m_ref, tab_ref, start_ref, qn_ref, up_ref, dn_ref, tri_ref, *, groups16, slots16, first
):
    count = qn_ref.shape[1]
    up_ref[...] = jnp.zeros_like(up_ref)
    dn_ref[...] = jnp.zeros_like(dn_ref)
    before = lax.broadcasted_iota(jnp.int32, (CHUNK, CHUNK), 0)
    after = lax.broadcasted_iota(jnp.int32, (CHUNK, CHUNK), 1)
    tri_ref[...] = (before < after).astype(jnp.bfloat16)
    low_iota = lax.broadcasted_iota(jnp.int32, (128, CHUNK), 0)
    group_iota = lax.broadcasted_iota(jnp.int32, (groups16, CHUNK), 0)
    slot_iota = lax.broadcasted_iota(jnp.int32, (slots16, CHUNK), 0)
    flag_row = lax.broadcasted_iota(jnp.int32, (8, CHUNK), 0)
    zero = jnp.zeros((), jnp.bfloat16)

    def body(step, offsets):
        cols = pl.ds(pl.multiple_of((first + step) * CHUNK, CHUNK), CHUNK)
        q = q_ref[:, cols]
        inc = inc_ref[:, cols]
        element = e_ref[:, cols]
        move = m_ref[:, cols]
        low = (low_iota == (element & 127)).astype(jnp.bfloat16)
        picked = jnp.dot(
            tab_ref[...], jnp.concatenate([low, low, low], axis=0), preferred_element_type=jnp.float32
        )
        hit = group_iota == (element >> 7)
        grads = [
            jnp.sum(
                jnp.where(hit, picked[c * groups16 : (c + 1) * groups16], 0.0),
                axis=0,
                keepdims=True,
            )
            for c in range(5)
        ]
        radial = q[0:1]
        axial = q[1:2]
        azimuth = q[2:3]
        spring, terms = spring_terms(q)
        drift = (
            grads[0] * radial + grads[1] * axial,
            grads[2] * radial + grads[3] * axial,
            grads[4] * azimuth,
        )
        q_next = [
            q[k : k + 1] + time_step * (drift[k] - 0.5 * spring * q[k : k + 1]) + noise_scale * inc[k : k + 1]
            for k in range(3)
        ]
        qn_ref[:, pl.ds(pl.multiple_of(step * CHUNK, CHUNK), CHUNK)] = jnp.concatenate(q_next, axis=0)
        going_up = move == 1
        going_down = move == -1
        flags = jnp.where(
            flag_row == 0,
            going_up.astype(jnp.float32),
            jnp.where(flag_row == 1, going_down.astype(jnp.float32), 0.0),
        )
        ranks = jnp.dot(flags.astype(jnp.bfloat16), tri_ref[...], preferred_element_type=jnp.float32)
        slots = (ranks + offsets).astype(jnp.int32)
        pieces = [bf16_pieces(value) for value in q_next]
        for direction, chosen, out_ref in ((0, going_up, up_ref), (1, going_down, dn_ref)):
            slot = slots[direction : direction + 1]
            place = ((low_iota == (slot & 127)) & chosen).astype(jnp.bfloat16)
            place = jnp.concatenate([place, place, place], axis=1)
            which = slot_iota == (slot >> 7)
            spread = jnp.concatenate(
                [
                    jnp.concatenate([jnp.where(which, piece, zero) for piece in pieces[k]], axis=1)
                    for k in range(3)
                ],
                axis=0,
            )
            out_ref[...] += lax.dot_general(spread, place, nt_dims, preferred_element_type=jnp.float32)
        return offsets + jnp.sum(flags, axis=1, keepdims=True)

    lax.fori_loop(0, count // CHUNK, body, start_ref[...])


def stress_partials(slab, q_state, element, migration, slab_elems, n_dev):
    groups = slab_elems // 128
    rows = round_up(3 * groups, 16)
    count = q_state.shape[1]
    vmem = pl.BlockSpec(memory_space=pltpu.VMEM)
    return pl.pallas_call(
        functools.partial(stress_kernel, groups=groups, rows=rows),
        out_shape=jax.ShapeDtypeStruct((n_dev, 12, 128), jnp.float32),
        in_specs=[pl.BlockSpec(memory_space=pltpu.SMEM)] + [vmem] * 3,
        out_specs=vmem,
        scratch_shapes=[pltpu.VMEM((4 * rows, 128), jnp.float32)],
        cost_estimate=pl.CostEstimate(
            flops=2 * 3 * 4 * rows * 128 * count, transcendentals=0, bytes_accessed=20 * count
        ),
    )(slab, q_state, element.reshape(1, -1), migration.reshape(1, -1))


def first_kernel(pt_ref, ft_ref, vout_ref, send_ref):
    own = vout_ref.shape[0]
    rows = [
        damping * jnp.sum(pt_ref[b] * ft_ref[:, b : b + 1], axis=0, keepdims=True)
        for b in range(own)
    ]
    fresh = jnp.concatenate(rows, axis=0)
    vout_ref[...] = fresh
    for k in range(send_ref.shape[0] // own):
        send_ref[k * own : (k + 1) * own, :] = fresh


def first_velocity(transposed, force_t, copies):
    own, size = transposed.shape[0], transposed.shape[1]
    return pl.pallas_call(
        first_kernel,
        out_shape=(
            jax.ShapeDtypeStruct((own, size), jnp.float32),
            jax.ShapeDtypeStruct((copies * own, size), jnp.float32),
        ),
        cost_estimate=pl.CostEstimate(
            flops=2 * transposed.size, transcendentals=0, bytes_accessed=4 * transposed.size
        ),
    )(transposed, force_t)


def update_and_pack(q_state, increments, element, migration, table, capacity):
    rows, slab_elems = table.shape
    groups = slab_elems // 128
    groups16 = round_up(groups, 16)
    slots = capacity // 128
    slots16 = round_up(slots, 16)
    arranged = jnp.pad(table.reshape(rows, groups, 128), ((0, 0), (0, groups16 - groups), (0, 0)))
    arranged = arranged.reshape(rows * groups16, 128)
    hi = lax.reduce_precision(arranged, exponent_bits=8, mantissa_bits=7)
    rest = arranged - hi
    mid = lax.reduce_precision(rest, exponent_bits=8, mantissa_bits=7)
    lo = rest - mid
    pieces = jnp.concatenate([hi, mid, lo], axis=1).astype(jnp.bfloat16)
    count = q_state.shape[1]
    parts = UPDATE_PARTS
    share = count // parts
    flags = jnp.stack([migration == 1, migration == -1]).astype(jnp.float32)
    per_part = jnp.sum(flags.reshape(2, parts, share), axis=2)
    starts = jnp.cumsum(per_part, axis=1) - per_part
    starts = jnp.pad(starts.T, ((0, 0), (0, 6)))[:, :, None]
    q_parts, up, down = [], 0.0, 0.0
    for part in range(parts):
        q_part, up_part, down_part = pl.pallas_call(
            functools.partial(
                update_kernel, groups16=groups16, slots16=slots16, first=part * share // CHUNK
            ),
            out_shape=(
                jax.ShapeDtypeStruct((3, share), jnp.float32),
                jax.ShapeDtypeStruct((3 * slots16, 128), jnp.float32),
                jax.ShapeDtypeStruct((3 * slots16, 128), jnp.float32),
            ),
            scratch_shapes=[pltpu.VMEM((CHUNK, CHUNK), jnp.bfloat16)],
            cost_estimate=pl.CostEstimate(
                flops=16 * 3 * (5 * groups16 + 6 * slots16) * 128 * share,
                transcendentals=0,
                bytes_accessed=40 * share,
            ),
        )(
            q_state,
            increments,
            element.reshape(1, -1),
            migration.reshape(1, -1),
            pieces,
            starts[part],
        )
        q_parts.append(q_part)
        up = up + up_part
        down = down + down_part
    q_next = jnp.concatenate(q_parts, axis=1)

    def unpack(acc):
        return acc.reshape(3, slots16, 128)[:, :slots].reshape(3, slots * 128)

    return q_next, unpack(up), unpack(down)


def sweep_kernel(idx_ref, g_ref, s_ref, pt_ref, ft_ref, v_ref, vout_ref, send_ref):
    total = g_ref.shape[0]
    own = v_ref.shape[0]
    width = s_ref.shape[1]
    rows = []
    for b in range(own):
        acc = None
        for n in range(width):
            w = idx_ref[b * width + n]
            inside = jnp.logical_and(w >= 0, w < total)
            near = g_ref[pl.ds(jnp.clip(w, 0, total - 1), 1), :]
            near = jnp.where(inside, near, 0.0)
            term = s_ref[b, n] * near
            acc = term if acc is None else acc + term
        image = jnp.sum(acc, axis=1, keepdims=True)
        rest = ft_ref[:, b : b + 1] - image
        update = jnp.sum(pt_ref[b] * rest, axis=0, keepdims=True)
        rows.append(v_ref[b : b + 1, :] + damping * update)
    fresh = jnp.concatenate(rows, axis=0)
    vout_ref[...] = fresh
    for k in range(send_ref.shape[0] // own):
        send_ref[k * own : (k + 1) * own, :] = fresh


def sweep(where_read, gathered, stiffness, transposed, force_t, velocity, copies):
    own = velocity.shape[0]
    vmem = pl.BlockSpec(memory_space=pltpu.VMEM)
    return pl.pallas_call(
        sweep_kernel,
        out_shape=(
            jax.ShapeDtypeStruct(velocity.shape, jnp.float32),
            jax.ShapeDtypeStruct((copies * own, velocity.shape[1]), jnp.float32),
        ),
        in_specs=[pl.BlockSpec(memory_space=pltpu.SMEM)] + [vmem] * 5,
        out_specs=(vmem, vmem),
        cost_estimate=pl.CostEstimate(
            flops=2 * (stiffness.size + transposed.size),
            transcendentals=0,
            bytes_accessed=4 * (stiffness.size + transposed.size + gathered.size),
        ),
    )(where_read, gathered, stiffness, transposed, force_t, velocity)


def passed_along(array, axis, by):
    size = lax.axis_size(axis)
    pairs = [(i, i + by) for i in range(size) if 0 <= i + by < size]
    return lax.ppermute(array, axis, pairs)


def body(
    q_state,
    increments,
    velocity_grad,
    element,
    migration,
    volume,
    div_map,
    stiffness,
    pattern,
    preconditioner,
):
    capacity = migration.shape[0] // 16
    slab_elems = velocity_grad.shape[1]
    n_slab = lax.axis_size("slab")
    slab = lax.axis_index("slab")

    n_rad = lax.axis_size("rad")
    send = stress_partials(
        slab.reshape(1).astype(jnp.int32), q_state, element, migration, slab_elems, n_slab * n_rad
    )
    received = lax.all_to_all(send, ("slab", "rad"), 0, 0, tiled=True)
    sums = jnp.sum(received, axis=0).reshape(4, slab_elems // n_rad)
    element_stress = sums / volume

    q_next, upward, downward = update_and_pack(
        q_state, increments, element, migration, velocity_grad, capacity
    )
    from_lower = passed_along(upward, "slab", 1)
    from_upper = passed_along(downward, "slab", -1)
    arrivals = jnp.stack([from_lower, from_upper])

    own_blocks = stiffness.shape[0]
    groups = (
        element_stress.reshape(4, own_blocks, BLOCK // 4)
        .transpose(1, 0, 2)
        .reshape(own_blocks, BLOCK)
    )
    force = jnp.dot(groups, div_map, precision=highest)

    def precondition(vector):
        return jnp.einsum("bij,bj->bi", preconditioner, vector, precision=highest)

    slab_blocks = own_blocks * n_rad
    copies = n_slab * n_rad
    where_read = ((slab - 1) * slab_blocks + pattern).reshape(-1).astype(jnp.int32)
    transposed = jnp.swapaxes(preconditioner, 1, 2)
    force_t = force.T
    velocity, send = first_velocity(transposed, force_t, copies)
    for sweep_index in range(1, ITERS):
        gathered = lax.all_to_all(send, ("slab", "rad"), 0, 0, tiled=True)
        velocity, send = sweep(
            where_read, gathered, stiffness, transposed, force_t, velocity, copies
        )
    return (q_next, arrivals, element_stress, velocity)


def solution(mesh):
    placed = (
        P(None, ("slab", "rad")),
        P(None, ("slab", "rad")),
        P(None, "slab"),
        P(("slab", "rad")),
        P(("slab", "rad")),
        P(("slab", "rad")),
        P(),
        P(("slab", "rad"), None, None, None),
        P(("slab", "rad"), None),
        P(("slab", "rad"), None, None),
    )
    return jax.shard_map(
        body,
        mesh=mesh,
        in_specs=placed,
        out_specs=(
            P(None, ("slab", "rad")),
            P(None, None, ("slab", "rad")),
            P(None, ("slab", "rad")),
            P(("slab", "rad"), None),
        ),
        check_vma=False,
    )
```

```python
import functools

import jax
import jax.numpy as jnp
from jax import lax
from jax.experimental import pallas as pl
from jax.experimental.pallas import tpu as pltpu
from jax.sharding import PartitionSpec as P

BLOCK = 192
ITERS = 6
CHUNK = 512
STRESS_CHUNK = 2048
UPDATE_PARTS = 4

extensibility = 50.0
time_step = 0.01
noise_scale = 0.1
damping = 0.6
highest = lax.Precision.HIGHEST
nt_dims = (((1,), (1,)), ((), ()))


def round_up(value, step):
    return -(-value // step) * step


def bf16_pieces(x):
    hi = x.astype(jnp.bfloat16)
    rest = x - hi.astype(jnp.float32)
    mid = rest.astype(jnp.bfloat16)
    lo = (rest - mid.astype(jnp.float32)).astype(jnp.bfloat16)
    return (hi, mid, lo)


def spring_terms(q):
    radial = q[0:1]
    axial = q[1:2]
    azimuth = q[2:3]
    stretch = radial * radial + axial * axial + azimuth * azimuth
    spring = 1.0 / (1.0 - stretch / extensibility)
    terms = (
        spring * radial * radial - 1.0,
        spring * axial * axial - 1.0,
        spring * radial * axial,
        spring * azimuth * azimuth - 1.0,
    )
    return spring, terms


def stress_kernel(slab_ref, q_ref, e_ref, m_ref, send_ref, acc_ref, *, groups, rows):
    count = q_ref.shape[1]
    n_dev = send_ref.shape[0]
    n_rad = groups // 3
    acc_ref[...] = jnp.zeros_like(acc_ref)
    low_iota = lax.broadcasted_iota(jnp.int32, (128, STRESS_CHUNK), 0)
    row_iota = lax.broadcasted_iota(jnp.int32, (rows, STRESS_CHUNK), 0)
    zero = jnp.zeros((), jnp.bfloat16)

    def body(step, carry):
        cols = pl.ds(pl.multiple_of(step * STRESS_CHUNK, STRESS_CHUNK), STRESS_CHUNK)
        q = q_ref[:, cols]
        element = e_ref[:, cols]
        move = m_ref[:, cols]
        spring, terms = spring_terms(q)
        kind = jnp.where(move == 0, 1, jnp.where(move == 1, 2, 0))
        key = kind * groups + (element >> 7)
        low = (low_iota == (element & 127)).astype(jnp.bfloat16)
        low = jnp.concatenate([low, low], axis=1)
        mask = row_iota == key
        spread = jnp.concatenate(
            [
                jnp.concatenate(
                    [jnp.where(mask, piece, zero) for piece in bf16_pieces(term)[:2]], axis=1
                )
                for term in terms
            ],
            axis=0,
        )
        acc_ref[...] += lax.dot_general(spread, low, nt_dims, preferred_element_type=jnp.float32)
        return carry

    lax.fori_loop(0, count // STRESS_CHUNK, body, 0)
    send_ref[...] = jnp.zeros_like(send_ref)
    slab = slab_ref[0]
    for kind in range(3):
        target = slab - 1 + kind

        @pl.when(jnp.logical_and(target >= 0, target * n_rad < n_dev))
        def _():
            for r in range(n_rad):
                for c in range(4):
                    start = c * rows + kind * groups + r * 3
                    send_ref[target * n_rad + r, c * 3 : c * 3 + 3, :] = acc_ref[start : start + 3, :]


def update_kernel(
    q_ref, inc_ref, e_ref, m_ref, tab_ref, start_ref, qn_ref, up_ref, dn_ref, tri_ref, *, groups16, slots16, first
):
    count = qn_ref.shape[1]
    up_ref[...] = jnp.zeros_like(up_ref)
    dn_ref[...] = jnp.zeros_like(dn_ref)
    before = lax.broadcasted_iota(jnp.int32, (CHUNK, CHUNK), 0)
    after = lax.broadcasted_iota(jnp.int32, (CHUNK, CHUNK), 1)
    tri_ref[...] = (before < after).astype(jnp.bfloat16)
    low_iota = lax.broadcasted_iota(jnp.int32, (128, CHUNK), 0)
    group_iota = lax.broadcasted_iota(jnp.int32, (groups16, CHUNK), 0)
    slot_iota = lax.broadcasted_iota(jnp.int32, (slots16, CHUNK), 0)
    flag_row = lax.broadcasted_iota(jnp.int32, (8, CHUNK), 0)
    zero = jnp.zeros((), jnp.bfloat16)

    def body(step, offsets):
        cols = pl.ds(pl.multiple_of((first + step) * CHUNK, CHUNK), CHUNK)
        q = q_ref[:, cols]
        inc = inc_ref[:, cols]
        element = e_ref[:, cols]
        move = m_ref[:, cols]
        low = (low_iota == (element & 127)).astype(jnp.bfloat16)
        picked = jnp.dot(
            tab_ref[...], jnp.concatenate([low, low, low], axis=0), preferred_element_type=jnp.float32
        )
        hit = group_iota == (element >> 7)
        grads = [
            jnp.sum(
                jnp.where(hit, picked[c * groups16 : (c + 1) * groups16], 0.0),
                axis=0,
                keepdims=True,
            )
            for c in range(5)
        ]
        radial = q[0:1]
        axial = q[1:2]
        azimuth = q[2:3]
        spring, terms = spring_terms(q)
        drift = (
            grads[0] * radial + grads[1] * axial,
            grads[2] * radial + grads[3] * axial,
            grads[4] * azimuth,
        )
        q_next = [
            q[k : k + 1] + time_step * (drift[k] - 0.5 * spring * q[k : k + 1]) + noise_scale * inc[k : k + 1]
            for k in range(3)
        ]
        qn_ref[:, pl.ds(pl.multiple_of(step * CHUNK, CHUNK), CHUNK)] = jnp.concatenate(q_next, axis=0)
        going_up = move == 1
        going_down = move == -1
        flags = jnp.where(
            flag_row == 0,
            going_up.astype(jnp.float32),
            jnp.where(flag_row == 1, going_down.astype(jnp.float32), 0.0),
        )
        ranks = jnp.dot(flags.astype(jnp.bfloat16), tri_ref[...], preferred_element_type=jnp.float32)
        slots = (ranks + offsets).astype(jnp.int32)
        pieces = [bf16_pieces(value) for value in q_next]
        for direction, chosen, out_ref in ((0, going_up, up_ref), (1, going_down, dn_ref)):
            slot = slots[direction : direction + 1]
            place = ((low_iota == (slot & 127)) & chosen).astype(jnp.bfloat16)
            place = jnp.concatenate([place, place, place], axis=1)
            which = slot_iota == (slot >> 7)
            spread = jnp.concatenate(
                [
                    jnp.concatenate([jnp.where(which, piece, zero) for piece in pieces[k]], axis=1)
                    for k in range(3)
                ],
                axis=0,
            )
            out_ref[...] += lax.dot_general(spread, place, nt_dims, preferred_element_type=jnp.float32)
        return offsets + jnp.sum(flags, axis=1, keepdims=True)

    lax.fori_loop(0, count // CHUNK, body, start_ref[...])


def stress_partials(slab, q_state, element, migration, slab_elems, n_dev):
    groups = slab_elems // 128
    rows = round_up(3 * groups, 16)
    count = q_state.shape[1]
    vmem = pl.BlockSpec(memory_space=pltpu.VMEM)
    return pl.pallas_call(
        functools.partial(stress_kernel, groups=groups, rows=rows),
        out_shape=jax.ShapeDtypeStruct((n_dev, 12, 128), jnp.float32),
        in_specs=[pl.BlockSpec(memory_space=pltpu.SMEM)] + [vmem] * 3,
        out_specs=vmem,
        scratch_shapes=[pltpu.VMEM((4 * rows, 128), jnp.float32)],
        cost_estimate=pl.CostEstimate(
            flops=2 * 3 * 4 * rows * 128 * count, transcendentals=0, bytes_accessed=20 * count
        ),
    )(slab, q_state, element.reshape(1, -1), migration.reshape(1, -1))


def first_kernel(pt_ref, ft_ref, vout_ref, send_ref):
    own = vout_ref.shape[0]
    rows = [
        damping * jnp.sum(pt_ref[b] * ft_ref[:, b : b + 1], axis=0, keepdims=True)
        for b in range(own)
    ]
    fresh = jnp.concatenate(rows, axis=0)
    vout_ref[...] = fresh
    for k in range(send_ref.shape[0] // own):
        send_ref[k * own : (k + 1) * own, :] = fresh


def first_velocity(transposed, force_t, copies):
    own, size = transposed.shape[0], transposed.shape[1]
    return pl.pallas_call(
        first_kernel,
        out_shape=(
            jax.ShapeDtypeStruct((own, size), jnp.float32),
            jax.ShapeDtypeStruct((copies * own, size), jnp.float32),
        ),
        cost_estimate=pl.CostEstimate(
            flops=2 * transposed.size, transcendentals=0, bytes_accessed=4 * transposed.size
        ),
    )(transposed, force_t)


def update_and_pack(q_state, increments, element, migration, table, capacity):
    rows, slab_elems = table.shape
    groups = slab_elems // 128
    groups16 = round_up(groups, 16)
    slots = capacity // 128
    slots16 = round_up(slots, 16)
    arranged = jnp.pad(table.reshape(rows, groups, 128), ((0, 0), (0, groups16 - groups), (0, 0)))
    arranged = arranged.reshape(rows * groups16, 128)
    hi = lax.reduce_precision(arranged, exponent_bits=8, mantissa_bits=7)
    rest = arranged - hi
    mid = lax.reduce_precision(rest, exponent_bits=8, mantissa_bits=7)
    lo = rest - mid
    pieces = jnp.concatenate([hi, mid, lo], axis=1).astype(jnp.bfloat16)
    count = q_state.shape[1]
    parts = UPDATE_PARTS
    share = count // parts
    flags = jnp.stack([migration == 1, migration == -1]).astype(jnp.float32)
    per_part = jnp.sum(flags.reshape(2, parts, share), axis=2)
    starts = jnp.cumsum(per_part, axis=1) - per_part
    starts = jnp.pad(starts.T, ((0, 0), (0, 6)))[:, :, None]
    q_parts, up, down = [], 0.0, 0.0
    for part in range(parts):
        q_part, up_part, down_part = pl.pallas_call(
            functools.partial(
                update_kernel, groups16=groups16, slots16=slots16, first=part * share // CHUNK
            ),
            out_shape=(
                jax.ShapeDtypeStruct((3, share), jnp.float32),
                jax.ShapeDtypeStruct((3 * slots16, 128), jnp.float32),
                jax.ShapeDtypeStruct((3 * slots16, 128), jnp.float32),
            ),
            scratch_shapes=[pltpu.VMEM((CHUNK, CHUNK), jnp.bfloat16)],
            cost_estimate=pl.CostEstimate(
                flops=16 * 3 * (5 * groups16 + 6 * slots16) * 128 * share,
                transcendentals=0,
                bytes_accessed=40 * share,
            ),
        )(
            q_state,
            increments,
            element.reshape(1, -1),
            migration.reshape(1, -1),
            pieces,
            starts[part],
        )
        q_parts.append(q_part)
        up = up + up_part
        down = down + down_part
    q_next = jnp.concatenate(q_parts, axis=1)

    def unpack(acc):
        return acc.reshape(3, slots16, 128)[:, :slots].reshape(3, slots * 128)

    return q_next, unpack(up), unpack(down)


def sweep_kernel(idx_ref, g_ref, s_ref, pt_ref, ft_ref, v_ref, vout_ref, send_ref):
    total = g_ref.shape[0]
    own = v_ref.shape[0]
    width = s_ref.shape[1]
    rows = []
    for b in range(own):
        acc = None
        for n in range(width):
            w = idx_ref[b * width + n]
            inside = jnp.logical_and(w >= 0, w < total)
            near = g_ref[pl.ds(jnp.clip(w, 0, total - 1), 1), :]
            near = jnp.where(inside, near, 0.0)
            term = s_ref[b, n] * near
            acc = term if acc is None else acc + term
        image = jnp.sum(acc, axis=1, keepdims=True)
        rest = ft_ref[:, b : b + 1] - image
        update = jnp.sum(pt_ref[b] * rest, axis=0, keepdims=True)
        rows.append(v_ref[b : b + 1, :] + damping * update)
    fresh = jnp.concatenate(rows, axis=0)
    vout_ref[...] = fresh
    for k in range(send_ref.shape[0] // own):
        send_ref[k * own : (k + 1) * own, :] = fresh


def sweep(where_read, gathered, stiffness, transposed, force_t, velocity, copies):
    own = velocity.shape[0]
    vmem = pl.BlockSpec(memory_space=pltpu.VMEM)
    return pl.pallas_call(
        sweep_kernel,
        out_shape=(
            jax.ShapeDtypeStruct(velocity.shape, jnp.float32),
            jax.ShapeDtypeStruct((copies * own, velocity.shape[1]), jnp.float32),
        ),
        in_specs=[pl.BlockSpec(memory_space=pltpu.SMEM)] + [vmem] * 5,
        out_specs=(vmem, vmem),
        cost_estimate=pl.CostEstimate(
            flops=2 * (stiffness.size + transposed.size),
            transcendentals=0,
            bytes_accessed=4 * (stiffness.size + transposed.size + gathered.size),
        ),
    )(where_read, gathered, stiffness, transposed, force_t, velocity)


def passed_along(array, axis, by):
    size = lax.axis_size(axis)
    pairs = [(i, i + by) for i in range(size) if 0 <= i + by < size]
    return lax.ppermute(array, axis, pairs)


def body(
    q_state,
    increments,
    velocity_grad,
    element,
    migration,
    volume,
    div_map,
    stiffness,
    pattern,
    preconditioner,
):
    capacity = migration.shape[0] // 16
    slab_elems = velocity_grad.shape[1]
    n_slab = lax.axis_size("slab")
    slab = lax.axis_index("slab")

    n_rad = lax.axis_size("rad")
    send = stress_partials(
        slab.reshape(1).astype(jnp.int32), q_state, element, migration, slab_elems, n_slab * n_rad
    )
    received = lax.all_to_all(send, ("slab", "rad"), 0, 0, tiled=True)
    sums = jnp.sum(received, axis=0).reshape(4, slab_elems // n_rad)
    element_stress = sums / volume

    q_next, upward, downward = update_and_pack(
        q_state, increments, element, migration, velocity_grad, capacity
    )
    from_lower = passed_along(upward, "slab", 1)
    from_upper = passed_along(downward, "slab", -1)
    arrivals = jnp.stack([from_lower, from_upper])

    own_blocks = stiffness.shape[0]
    groups = (
        element_stress.reshape(4, own_blocks, BLOCK // 4)
        .transpose(1, 0, 2)
        .reshape(own_blocks, BLOCK)
    )
    force = jnp.dot(groups, div_map, precision=highest)

    def precondition(vector):
        return jnp.einsum("bij,bj->bi", preconditioner, vector, precision=highest)

    slab_blocks = own_blocks * n_rad
    copies = n_slab * n_rad
    where_read = ((slab - 1) * slab_blocks + pattern).reshape(-1).astype(jnp.int32)
    transposed = jnp.swapaxes(preconditioner, 1, 2)
    force_t = force.T
    velocity, send = first_velocity(transposed, force_t, copies)
    for sweep_index in range(1, ITERS):
        gathered = lax.all_to_all(send, ("slab", "rad"), 0, 0, tiled=True)
        velocity, send = sweep(
            where_read, gathered, stiffness, transposed, force_t, velocity, copies
        )
    return (q_next, arrivals, element_stress, velocity)


def solution(mesh):
    placed = (
        P(None, ("slab", "rad")),
        P(None, ("slab", "rad")),
        P(None, "slab"),
        P(("slab", "rad")),
        P(("slab", "rad")),
        P(("slab", "rad")),
        P(),
        P(("slab", "rad"), None, None, None),
        P(("slab", "rad"), None),
        P(("slab", "rad"), None, None),
    )
    return jax.shard_map(
        body,
        mesh=mesh,
        in_specs=placed,
        out_specs=(
            P(None, ("slab", "rad")),
            P(None, None, ("slab", "rad")),
            P(None, ("slab", "rad")),
            P(("slab", "rad"), None),
        ),
        check_vma=False,
    )
```

```python
import functools

import jax
import jax.numpy as jnp
from jax import lax
from jax.experimental import pallas as pl
from jax.experimental.pallas import tpu as pltpu
from jax.sharding import PartitionSpec as P

BLOCK = 192
ITERS = 6
CHUNK = 512
STRESS_CHUNK = 4096
UPDATE_PARTS = 4

extensibility = 50.0
time_step = 0.01
noise_scale = 0.1
damping = 0.6
highest = lax.Precision.HIGHEST
nt_dims = (((1,), (1,)), ((), ()))


def round_up(value, step):
    return -(-value // step) * step


def bf16_pieces(x):
    hi = x.astype(jnp.bfloat16)
    rest = x - hi.astype(jnp.float32)
    mid = rest.astype(jnp.bfloat16)
    lo = (rest - mid.astype(jnp.float32)).astype(jnp.bfloat16)
    return (hi, mid, lo)


def spring_terms(q):
    radial = q[0:1]
    axial = q[1:2]
    azimuth = q[2:3]
    stretch = radial * radial + axial * axial + azimuth * azimuth
    spring = 1.0 / (1.0 - stretch / extensibility)
    terms = (
        spring * radial * radial - 1.0,
        spring * axial * axial - 1.0,
        spring * radial * axial,
        spring * azimuth * azimuth - 1.0,
    )
    return spring, terms


def stress_kernel(slab_ref, q_ref, e_ref, m_ref, send_ref, acc_ref, *, groups, rows):
    count = q_ref.shape[1]
    n_dev = send_ref.shape[0]
    n_rad = groups // 3
    acc_ref[...] = jnp.zeros_like(acc_ref)
    low_iota = lax.broadcasted_iota(jnp.int32, (128, STRESS_CHUNK), 0)
    row_iota = lax.broadcasted_iota(jnp.int32, (rows, STRESS_CHUNK), 0)
    zero = jnp.zeros((), jnp.bfloat16)

    def body(step, carry):
        cols = pl.ds(pl.multiple_of(step * STRESS_CHUNK, STRESS_CHUNK), STRESS_CHUNK)
        q = q_ref[:, cols]
        element = e_ref[:, cols]
        move = m_ref[:, cols]
        spring, terms = spring_terms(q)
        kind = jnp.where(move == 0, 1, jnp.where(move == 1, 2, 0))
        key = kind * groups + (element >> 7)
        low = (low_iota == (element & 127)).astype(jnp.bfloat16)
        low = jnp.concatenate([low, low], axis=1)
        mask = row_iota == key
        spread = jnp.concatenate(
            [
                jnp.concatenate(
                    [jnp.where(mask, piece, zero) for piece in bf16_pieces(term)[:2]], axis=1
                )
                for term in terms
            ],
            axis=0,
        )
        acc_ref[...] += lax.dot_general(spread, low, nt_dims, preferred_element_type=jnp.float32)
        return carry

    lax.fori_loop(0, count // STRESS_CHUNK, body, 0)
    send_ref[...] = jnp.zeros_like(send_ref)
    slab = slab_ref[0]
    for kind in range(3):
        target = slab - 1 + kind

        @pl.when(jnp.logical_and(target >= 0, target * n_rad < n_dev))
        def _():
            for r in range(n_rad):
                for c in range(4):
                    start = c * rows + kind * groups + r * 3
                    send_ref[target * n_rad + r, c * 3 : c * 3 + 3, :] = acc_ref[start : start + 3, :]


def update_kernel(
    q_ref, inc_ref, e_ref, m_ref, tab_ref, start_ref, qn_ref, up_ref, dn_ref, tri_ref, *, groups16, slots16, first
):
    count = qn_ref.shape[1]
    up_ref[...] = jnp.zeros_like(up_ref)
    dn_ref[...] = jnp.zeros_like(dn_ref)
    before = lax.broadcasted_iota(jnp.int32, (CHUNK, CHUNK), 0)
    after = lax.broadcasted_iota(jnp.int32, (CHUNK, CHUNK), 1)
    tri_ref[...] = (before < after).astype(jnp.bfloat16)
    low_iota = lax.broadcasted_iota(jnp.int32, (128, CHUNK), 0)
    group_iota = lax.broadcasted_iota(jnp.int32, (groups16, CHUNK), 0)
    slot_iota = lax.broadcasted_iota(jnp.int32, (slots16, CHUNK), 0)
    flag_row = lax.broadcasted_iota(jnp.int32, (8, CHUNK), 0)
    zero = jnp.zeros((), jnp.bfloat16)

    def body(step, offsets):
        cols = pl.ds(pl.multiple_of((first + step) * CHUNK, CHUNK), CHUNK)
        q = q_ref[:, cols]
        inc = inc_ref[:, cols]
        element = e_ref[:, cols]
        move = m_ref[:, cols]
        low = (low_iota == (element & 127)).astype(jnp.bfloat16)
        picked = jnp.dot(
            tab_ref[...], jnp.concatenate([low, low, low], axis=0), preferred_element_type=jnp.float32
        )
        hit = group_iota == (element >> 7)
        grads = [
            jnp.sum(
                jnp.where(hit, picked[c * groups16 : (c + 1) * groups16], 0.0),
                axis=0,
                keepdims=True,
            )
            for c in range(5)
        ]
        radial = q[0:1]
        axial = q[1:2]
        azimuth = q[2:3]
        spring, terms = spring_terms(q)
        drift = (
            grads[0] * radial + grads[1] * axial,
            grads[2] * radial + grads[3] * axial,
            grads[4] * azimuth,
        )
        q_next = [
            q[k : k + 1] + time_step * (drift[k] - 0.5 * spring * q[k : k + 1]) + noise_scale * inc[k : k + 1]
            for k in range(3)
        ]
        qn_ref[:, pl.ds(pl.multiple_of(step * CHUNK, CHUNK), CHUNK)] = jnp.concatenate(q_next, axis=0)
        going_up = move == 1
        going_down = move == -1
        flags = jnp.where(
            flag_row == 0,
            going_up.astype(jnp.float32),
            jnp.where(flag_row == 1, going_down.astype(jnp.float32), 0.0),
        )
        ranks = jnp.dot(flags.astype(jnp.bfloat16), tri_ref[...], preferred_element_type=jnp.float32)
        slots = (ranks + offsets).astype(jnp.int32)
        pieces = [bf16_pieces(value) for value in q_next]
        for direction, chosen, out_ref in ((0, going_up, up_ref), (1, going_down, dn_ref)):
            slot = slots[direction : direction + 1]
            place = ((low_iota == (slot & 127)) & chosen).astype(jnp.bfloat16)
            place = jnp.concatenate([place, place, place], axis=1)
            which = slot_iota == (slot >> 7)
            spread = jnp.concatenate(
                [
                    jnp.concatenate([jnp.where(which, piece, zero) for piece in pieces[k]], axis=1)
                    for k in range(3)
                ],
                axis=0,
            )
            out_ref[...] += lax.dot_general(spread, place, nt_dims, preferred_element_type=jnp.float32)
        return offsets + jnp.sum(flags, axis=1, keepdims=True)

    lax.fori_loop(0, count // CHUNK, body, start_ref[...])


def stress_partials(slab, q_state, element, migration, slab_elems, n_dev):
    groups = slab_elems // 128
    rows = round_up(3 * groups, 16)
    count = q_state.shape[1]
    vmem = pl.BlockSpec(memory_space=pltpu.VMEM)
    return pl.pallas_call(
        functools.partial(stress_kernel, groups=groups, rows=rows),
        out_shape=jax.ShapeDtypeStruct((n_dev, 12, 128), jnp.float32),
        in_specs=[pl.BlockSpec(memory_space=pltpu.SMEM)] + [vmem] * 3,
        out_specs=vmem,
        scratch_shapes=[pltpu.VMEM((4 * rows, 128), jnp.float32)],
        cost_estimate=pl.CostEstimate(
            flops=2 * 3 * 4 * rows * 128 * count, transcendentals=0, bytes_accessed=20 * count
        ),
    )(slab, q_state, element.reshape(1, -1), migration.reshape(1, -1))


def first_kernel(pt_ref, ft_ref, vout_ref, send_ref):
    own = vout_ref.shape[0]
    rows = [
        damping * jnp.sum(pt_ref[b] * ft_ref[:, b : b + 1], axis=0, keepdims=True)
        for b in range(own)
    ]
    fresh = jnp.concatenate(rows, axis=0)
    vout_ref[...] = fresh
    for k in range(send_ref.shape[0] // own):
        send_ref[k * own : (k + 1) * own, :] = fresh


def first_velocity(transposed, force_t, copies):
    own, size = transposed.shape[0], transposed.shape[1]
    return pl.pallas_call(
        first_kernel,
        out_shape=(
            jax.ShapeDtypeStruct((own, size), jnp.float32),
            jax.ShapeDtypeStruct((copies * own, size), jnp.float32),
        ),
        cost_estimate=pl.CostEstimate(
            flops=2 * transposed.size, transcendentals=0, bytes_accessed=4 * transposed.size
        ),
    )(transposed, force_t)


def update_and_pack(q_state, increments, element, migration, table, capacity):
    rows, slab_elems = table.shape
    groups = slab_elems // 128
    groups16 = round_up(groups, 16)
    slots = capacity // 128
    slots16 = round_up(slots, 16)
    arranged = jnp.pad(table.reshape(rows, groups, 128), ((0, 0), (0, groups16 - groups), (0, 0)))
    arranged = arranged.reshape(rows * groups16, 128)
    hi = lax.reduce_precision(arranged, exponent_bits=8, mantissa_bits=7)
    rest = arranged - hi
    mid = lax.reduce_precision(rest, exponent_bits=8, mantissa_bits=7)
    lo = rest - mid
    pieces = jnp.concatenate([hi, mid, lo], axis=1).astype(jnp.bfloat16)
    count = q_state.shape[1]
    parts = UPDATE_PARTS
    share = count // parts
    flags = jnp.stack([migration == 1, migration == -1]).astype(jnp.float32)
    per_part = jnp.sum(flags.reshape(2, parts, share), axis=2)
    starts = jnp.cumsum(per_part, axis=1) - per_part
    starts = jnp.pad(starts.T, ((0, 0), (0, 6)))[:, :, None]
    q_parts, up, down = [], 0.0, 0.0
    for part in range(parts):
        q_part, up_part, down_part = pl.pallas_call(
            functools.partial(
                update_kernel, groups16=groups16, slots16=slots16, first=part * share // CHUNK
            ),
            out_shape=(
                jax.ShapeDtypeStruct((3, share), jnp.float32),
                jax.ShapeDtypeStruct((3 * slots16, 128), jnp.float32),
                jax.ShapeDtypeStruct((3 * slots16, 128), jnp.float32),
            ),
            scratch_shapes=[pltpu.VMEM((CHUNK, CHUNK), jnp.bfloat16)],
            cost_estimate=pl.CostEstimate(
                flops=16 * 3 * (5 * groups16 + 6 * slots16) * 128 * share,
                transcendentals=0,
                bytes_accessed=40 * share,
            ),
        )(
            q_state,
            increments,
            element.reshape(1, -1),
            migration.reshape(1, -1),
            pieces,
            starts[part],
        )
        q_parts.append(q_part)
        up = up + up_part
        down = down + down_part
    q_next = jnp.concatenate(q_parts, axis=1)

    def unpack(acc):
        return acc.reshape(3, slots16, 128)[:, :slots].reshape(3, slots * 128)

    return q_next, unpack(up), unpack(down)


def sweep_kernel(idx_ref, g_ref, s_ref, pt_ref, ft_ref, v_ref, vout_ref, send_ref):
    total = g_ref.shape[0]
    own = v_ref.shape[0]
    width = s_ref.shape[1]
    rows = []
    for b in range(own):
        acc = None
        for n in range(width):
            w = idx_ref[b * width + n]
            inside = jnp.logical_and(w >= 0, w < total)
            near = g_ref[pl.ds(jnp.clip(w, 0, total - 1), 1), :]
            near = jnp.where(inside, near, 0.0)
            term = s_ref[b, n] * near
            acc = term if acc is None else acc + term
        image = jnp.sum(acc, axis=1, keepdims=True)
        rest = ft_ref[:, b : b + 1] - image
        update = jnp.sum(pt_ref[b] * rest, axis=0, keepdims=True)
        rows.append(v_ref[b : b + 1, :] + damping * update)
    fresh = jnp.concatenate(rows, axis=0)
    vout_ref[...] = fresh
    for k in range(send_ref.shape[0] // own):
        send_ref[k * own : (k + 1) * own, :] = fresh


def sweep(where_read, gathered, stiffness, transposed, force_t, velocity, copies):
    own = velocity.shape[0]
    vmem = pl.BlockSpec(memory_space=pltpu.VMEM)
    return pl.pallas_call(
        sweep_kernel,
        out_shape=(
            jax.ShapeDtypeStruct(velocity.shape, jnp.float32),
            jax.ShapeDtypeStruct((copies * own, velocity.shape[1]), jnp.float32),
        ),
        in_specs=[pl.BlockSpec(memory_space=pltpu.SMEM)] + [vmem] * 5,
        out_specs=(vmem, vmem),
        cost_estimate=pl.CostEstimate(
            flops=2 * (stiffness.size + transposed.size),
            transcendentals=0,
            bytes_accessed=4 * (stiffness.size + transposed.size + gathered.size),
        ),
    )(where_read, gathered, stiffness, transposed, force_t, velocity)


def passed_along(array, axis, by):
    size = lax.axis_size(axis)
    pairs = [(i, i + by) for i in range(size) if 0 <= i + by < size]
    return lax.ppermute(array, axis, pairs)


def body(
    q_state,
    increments,
    velocity_grad,
    element,
    migration,
    volume,
    div_map,
    stiffness,
    pattern,
    preconditioner,
):
    capacity = migration.shape[0] // 16
    slab_elems = velocity_grad.shape[1]
    n_slab = lax.axis_size("slab")
    slab = lax.axis_index("slab")

    n_rad = lax.axis_size("rad")
    send = stress_partials(
        slab.reshape(1).astype(jnp.int32), q_state, element, migration, slab_elems, n_slab * n_rad
    )
    received = lax.all_to_all(send, ("slab", "rad"), 0, 0, tiled=True)
    sums = jnp.sum(received, axis=0).reshape(4, slab_elems // n_rad)
    element_stress = sums / volume

    q_next, upward, downward = update_and_pack(
        q_state, increments, element, migration, velocity_grad, capacity
    )
    from_lower = passed_along(upward, "slab", 1)
    from_upper = passed_along(downward, "slab", -1)
    arrivals = jnp.stack([from_lower, from_upper])

    own_blocks = stiffness.shape[0]
    groups = (
        element_stress.reshape(4, own_blocks, BLOCK // 4)
        .transpose(1, 0, 2)
        .reshape(own_blocks, BLOCK)
    )
    force = jnp.dot(groups, div_map, precision=highest)

    def precondition(vector):
        return jnp.einsum("bij,bj->bi", preconditioner, vector, precision=highest)

    slab_blocks = own_blocks * n_rad
    copies = n_slab * n_rad
    where_read = ((slab - 1) * slab_blocks + pattern).reshape(-1).astype(jnp.int32)
    transposed = jnp.swapaxes(preconditioner, 1, 2)
    force_t = force.T
    velocity, send = first_velocity(transposed, force_t, copies)
    for sweep_index in range(1, ITERS):
        gathered = lax.all_to_all(send, ("slab", "rad"), 0, 0, tiled=True)
        velocity, send = sweep(
            where_read, gathered, stiffness, transposed, force_t, velocity, copies
        )
    return (q_next, arrivals, element_stress, velocity)


def solution(mesh):
    placed = (
        P(None, ("slab", "rad")),
        P(None, ("slab", "rad")),
        P(None, "slab"),
        P(("slab", "rad")),
        P(("slab", "rad")),
        P(("slab", "rad")),
        P(),
        P(("slab", "rad"), None, None, None),
        P(("slab", "rad"), None),
        P(("slab", "rad"), None, None),
    )
    return jax.shard_map(
        body,
        mesh=mesh,
        in_specs=placed,
        out_specs=(
            P(None, ("slab", "rad")),
            P(None, None, ("slab", "rad")),
            P(None, ("slab", "rad")),
            P(("slab", "rad"), None),
        ),
        check_vma=False,
    )
```

```python
import functools

import jax
import jax.numpy as jnp
from jax import lax
from jax.experimental import pallas as pl
from jax.experimental.pallas import tpu as pltpu
from jax.sharding import PartitionSpec as P

BLOCK = 192
ITERS = 6
CHUNK = 512
STRESS_CHUNK = 4096
UPDATE_PARTS = 4

extensibility = 50.0
time_step = 0.01
noise_scale = 0.1
damping = 0.6
highest = lax.Precision.HIGHEST
nt_dims = (((1,), (1,)), ((), ()))


def round_up(value, step):
    return -(-value // step) * step


def bf16_pieces(x):
    hi = x.astype(jnp.bfloat16)
    rest = x - hi.astype(jnp.float32)
    mid = rest.astype(jnp.bfloat16)
    lo = (rest - mid.astype(jnp.float32)).astype(jnp.bfloat16)
    return (hi, mid, lo)


def spring_terms(q):
    radial = q[0:1]
    axial = q[1:2]
    azimuth = q[2:3]
    stretch = radial * radial + axial * axial + azimuth * azimuth
    spring = 1.0 / (1.0 - stretch / extensibility)
    terms = (
        spring * radial * radial - 1.0,
        spring * axial * axial - 1.0,
        spring * radial * axial,
        spring * azimuth * azimuth - 1.0,
    )
    return spring, terms


def stress_kernel(slab_ref, q_ref, e_ref, m_ref, send_ref, acc_ref, *, groups, rows):
    count = q_ref.shape[1]
    n_dev = send_ref.shape[0]
    n_rad = groups // 3
    acc_ref[...] = jnp.zeros_like(acc_ref)
    low_iota = lax.broadcasted_iota(jnp.int32, (128, STRESS_CHUNK), 0)
    row_iota = lax.broadcasted_iota(jnp.int32, (rows, STRESS_CHUNK), 0)
    zero = jnp.zeros((), jnp.bfloat16)

    def body(step, carry):
        cols = pl.ds(pl.multiple_of(step * STRESS_CHUNK, STRESS_CHUNK), STRESS_CHUNK)
        q = q_ref[:, cols]
        element = e_ref[:, cols]
        move = m_ref[:, cols]
        spring, terms = spring_terms(q)
        kind = jnp.where(move == 0, 1, jnp.where(move == 1, 2, 0))
        key = kind * groups + (element >> 7)
        low = (low_iota == (element & 127)).astype(jnp.bfloat16)
        low = jnp.concatenate([low, low], axis=1)
        mask = row_iota == key
        spread = jnp.concatenate(
            [
                jnp.concatenate(
                    [jnp.where(mask, piece, zero) for piece in bf16_pieces(term)[:2]], axis=1
                )
                for term in terms
            ],
            axis=0,
        )
        acc_ref[...] += lax.dot_general(spread, low, nt_dims, preferred_element_type=jnp.float32)
        return carry

    lax.fori_loop(0, count // STRESS_CHUNK, body, 0)
    send_ref[...] = jnp.zeros_like(send_ref)
    slab = slab_ref[0]
    for kind in range(3):
        target = slab - 1 + kind

        @pl.when(jnp.logical_and(target >= 0, target * n_rad < n_dev))
        def _():
            for r in range(n_rad):
                for c in range(4):
                    start = c * rows + kind * groups + r * 3
                    send_ref[target * n_rad + r, c * 3 : c * 3 + 3, :] = acc_ref[start : start + 3, :]


def update_kernel(
    q_ref, inc_ref, e_ref, m_ref, tab_ref, start_ref, qn_ref, up_ref, dn_ref, tri_ref, *, groups16, slots16, first
):
    count = qn_ref.shape[1]
    up_ref[...] = jnp.zeros_like(up_ref)
    dn_ref[...] = jnp.zeros_like(dn_ref)
    before = lax.broadcasted_iota(jnp.int32, (CHUNK, CHUNK), 0)
    after = lax.broadcasted_iota(jnp.int32, (CHUNK, CHUNK), 1)
    tri_ref[...] = (before < after).astype(jnp.bfloat16)
    low_iota = lax.broadcasted_iota(jnp.int32, (128, CHUNK), 0)
    group_iota = lax.broadcasted_iota(jnp.int32, (groups16, CHUNK), 0)
    slot_iota = lax.broadcasted_iota(jnp.int32, (slots16, CHUNK), 0)
    flag_row = lax.broadcasted_iota(jnp.int32, (8, CHUNK), 0)
    zero = jnp.zeros((), jnp.bfloat16)

    def body(step, offsets):
        cols = pl.ds(pl.multiple_of((first + step) * CHUNK, CHUNK), CHUNK)
        q = q_ref[:, cols]
        inc = inc_ref[:, cols]
        element = e_ref[:, cols]
        move = m_ref[:, cols]
        low = (low_iota == (element & 127)).astype(jnp.bfloat16)
        picked = jnp.dot(
            tab_ref[...], jnp.concatenate([low, low, low], axis=0), preferred_element_type=jnp.float32
        )
        hit = group_iota == (element >> 7)
        grads = [
            jnp.sum(
                jnp.where(hit, picked[c * groups16 : (c + 1) * groups16], 0.0),
                axis=0,
                keepdims=True,
            )
            for c in range(5)
        ]
        radial = q[0:1]
        axial = q[1:2]
        azimuth = q[2:3]
        spring, terms = spring_terms(q)
        drift = (
            grads[0] * radial + grads[1] * axial,
            grads[2] * radial + grads[3] * axial,
            grads[4] * azimuth,
        )
        q_next = [
            q[k : k + 1] + time_step * (drift[k] - 0.5 * spring * q[k : k + 1]) + noise_scale * inc[k : k + 1]
            for k in range(3)
        ]
        qn_ref[:, pl.ds(pl.multiple_of(step * CHUNK, CHUNK), CHUNK)] = jnp.concatenate(q_next, axis=0)
        going_up = move == 1
        going_down = move == -1
        flags = jnp.where(
            flag_row == 0,
            going_up.astype(jnp.float32),
            jnp.where(flag_row == 1, going_down.astype(jnp.float32), 0.0),
        )
        ranks = jnp.dot(flags.astype(jnp.bfloat16), tri_ref[...], preferred_element_type=jnp.float32)
        slots = (ranks + offsets).astype(jnp.int32)
        pieces = [bf16_pieces(value) for value in q_next]
        for direction, chosen, out_ref in ((0, going_up, up_ref), (1, going_down, dn_ref)):
            slot = slots[direction : direction + 1]
            place = ((low_iota == (slot & 127)) & chosen).astype(jnp.bfloat16)
            place = jnp.concatenate([place, place, place], axis=1)
            which = slot_iota == (slot >> 7)
            spread = jnp.concatenate(
                [
                    jnp.concatenate([jnp.where(which, piece, zero) for piece in pieces[k]], axis=1)
                    for k in range(3)
                ],
                axis=0,
            )
            out_ref[...] += lax.dot_general(spread, place, nt_dims, preferred_element_type=jnp.float32)
        return offsets + jnp.sum(flags, axis=1, keepdims=True)

    lax.fori_loop(0, count // CHUNK, body, start_ref[...])


def stress_partials(slab, q_state, element, migration, slab_elems, n_dev):
    groups = slab_elems // 128
    rows = round_up(3 * groups, 16)
    count = q_state.shape[1]
    vmem = pl.BlockSpec(memory_space=pltpu.VMEM)
    return pl.pallas_call(
        functools.partial(stress_kernel, groups=groups, rows=rows),
        out_shape=jax.ShapeDtypeStruct((n_dev, 12, 128), jnp.float32),
        in_specs=[pl.BlockSpec(memory_space=pltpu.SMEM)] + [vmem] * 3,
        out_specs=vmem,
        scratch_shapes=[pltpu.VMEM((4 * rows, 128), jnp.float32)],
        cost_estimate=pl.CostEstimate(
            flops=2 * 3 * 4 * rows * 128 * count, transcendentals=0, bytes_accessed=20 * count
        ),
    )(slab, q_state, element.reshape(1, -1), migration.reshape(1, -1))


def first_kernel(p_ref, f_ref, vout_ref, send_ref):
    own, size = vout_ref.shape
    lanes = lax.broadcasted_iota(jnp.int32, (size, 128), 1)
    block = jnp.zeros((size, 128), jnp.float32)
    for b in range(own):
        column = damping * jnp.sum(p_ref[b] * f_ref[b : b + 1, :], axis=1, keepdims=True)
        block = jnp.where(lanes == b, column, block)
    block = jnp.pad(block, ((0, round_up(size, 128) - size), (0, 0)))
    fresh = block.T[:own, :size]
    vout_ref[...] = fresh
    for k in range(send_ref.shape[0] // own):
        send_ref[k * own : (k + 1) * own, :] = fresh


def first_velocity(transposed, force_t, copies):
    own, size = transposed.shape[0], transposed.shape[1]
    return pl.pallas_call(
        first_kernel,
        out_shape=(
            jax.ShapeDtypeStruct((own, size), jnp.float32),
            jax.ShapeDtypeStruct((copies * own, size), jnp.float32),
        ),
        cost_estimate=pl.CostEstimate(
            flops=2 * transposed.size, transcendentals=0, bytes_accessed=4 * transposed.size
        ),
    )(transposed, force_t)


def update_and_pack(q_state, increments, element, migration, table, capacity):
    rows, slab_elems = table.shape
    groups = slab_elems // 128
    groups16 = round_up(groups, 16)
    slots = capacity // 128
    slots16 = round_up(slots, 16)
    arranged = jnp.pad(table.reshape(rows, groups, 128), ((0, 0), (0, groups16 - groups), (0, 0)))
    arranged = arranged.reshape(rows * groups16, 128)
    hi = lax.reduce_precision(arranged, exponent_bits=8, mantissa_bits=7)
    rest = arranged - hi
    mid = lax.reduce_precision(rest, exponent_bits=8, mantissa_bits=7)
    lo = rest - mid
    pieces = jnp.concatenate([hi, mid, lo], axis=1).astype(jnp.bfloat16)
    count = q_state.shape[1]
    parts = UPDATE_PARTS
    share = count // parts
    flags = jnp.stack([migration == 1, migration == -1]).astype(jnp.float32)
    per_part = jnp.sum(flags.reshape(2, parts, share), axis=2)
    starts = jnp.cumsum(per_part, axis=1) - per_part
    starts = jnp.pad(starts.T, ((0, 0), (0, 6)))[:, :, None]
    q_parts, up, down = [], 0.0, 0.0
    for part in range(parts):
        q_part, up_part, down_part = pl.pallas_call(
            functools.partial(
                update_kernel, groups16=groups16, slots16=slots16, first=part * share // CHUNK
            ),
            out_shape=(
                jax.ShapeDtypeStruct((3, share), jnp.float32),
                jax.ShapeDtypeStruct((3 * slots16, 128), jnp.float32),
                jax.ShapeDtypeStruct((3 * slots16, 128), jnp.float32),
            ),
            scratch_shapes=[pltpu.VMEM((CHUNK, CHUNK), jnp.bfloat16)],
            cost_estimate=pl.CostEstimate(
                flops=16 * 3 * (5 * groups16 + 6 * slots16) * 128 * share,
                transcendentals=0,
                bytes_accessed=40 * share,
            ),
        )(
            q_state,
            increments,
            element.reshape(1, -1),
            migration.reshape(1, -1),
            pieces,
            starts[part],
        )
        q_parts.append(q_part)
        up = up + up_part
        down = down + down_part
    q_next = jnp.concatenate(q_parts, axis=1)

    def unpack(acc):
        return acc.reshape(3, slots16, 128)[:, :slots].reshape(3, slots * 128)

    return q_next, unpack(up), unpack(down)


def sweep_kernel(idx_ref, g_ref, s_ref, pt_ref, ft_ref, v_ref, vout_ref, send_ref):
    total = g_ref.shape[0]
    own = v_ref.shape[0]
    width = s_ref.shape[1]
    rows = []
    for b in range(own):
        acc = None
        for n in range(width):
            w = idx_ref[b * width + n]
            inside = jnp.logical_and(w >= 0, w < total)
            near = g_ref[pl.ds(jnp.clip(w, 0, total - 1), 1), :]
            near = jnp.where(inside, near, 0.0)
            term = s_ref[b, n] * near
            acc = term if acc is None else acc + term
        image = jnp.sum(acc, axis=1, keepdims=True)
        rest = ft_ref[:, b : b + 1] - image
        update = jnp.sum(pt_ref[b] * rest, axis=0, keepdims=True)
        rows.append(v_ref[b : b + 1, :] + damping * update)
    fresh = jnp.concatenate(rows, axis=0)
    vout_ref[...] = fresh
    for k in range(send_ref.shape[0] // own):
        send_ref[k * own : (k + 1) * own, :] = fresh


def sweep(where_read, gathered, stiffness, transposed, force_t, velocity, copies):
    own = velocity.shape[0]
    vmem = pl.BlockSpec(memory_space=pltpu.VMEM)
    return pl.pallas_call(
        sweep_kernel,
        out_shape=(
            jax.ShapeDtypeStruct(velocity.shape, jnp.float32),
            jax.ShapeDtypeStruct((copies * own, velocity.shape[1]), jnp.float32),
        ),
        in_specs=[pl.BlockSpec(memory_space=pltpu.SMEM)] + [vmem] * 5,
        out_specs=(vmem, vmem),
        cost_estimate=pl.CostEstimate(
            flops=2 * (stiffness.size + transposed.size),
            transcendentals=0,
            bytes_accessed=4 * (stiffness.size + transposed.size + gathered.size),
        ),
    )(where_read, gathered, stiffness, transposed, force_t, velocity)


def passed_along(array, axis, by):
    size = lax.axis_size(axis)
    pairs = [(i, i + by) for i in range(size) if 0 <= i + by < size]
    return lax.ppermute(array, axis, pairs)


def body(
    q_state,
    increments,
    velocity_grad,
    element,
    migration,
    volume,
    div_map,
    stiffness,
    pattern,
    preconditioner,
):
    capacity = migration.shape[0] // 16
    slab_elems = velocity_grad.shape[1]
    n_slab = lax.axis_size("slab")
    slab = lax.axis_index("slab")

    n_rad = lax.axis_size("rad")
    send = stress_partials(
        slab.reshape(1).astype(jnp.int32), q_state, element, migration, slab_elems, n_slab * n_rad
    )
    received = lax.all_to_all(send, ("slab", "rad"), 0, 0, tiled=True)
    sums = jnp.sum(received, axis=0).reshape(4, slab_elems // n_rad)
    element_stress = sums / volume

    q_next, upward, downward = update_and_pack(
        q_state, increments, element, migration, velocity_grad, capacity
    )
    from_lower = passed_along(upward, "slab", 1)
    from_upper = passed_along(downward, "slab", -1)
    arrivals = jnp.stack([from_lower, from_upper])

    own_blocks = stiffness.shape[0]
    groups = (
        element_stress.reshape(4, own_blocks, BLOCK // 4)
        .transpose(1, 0, 2)
        .reshape(own_blocks, BLOCK)
    )
    force = jnp.dot(groups, div_map, precision=highest)

    def precondition(vector):
        return jnp.einsum("bij,bj->bi", preconditioner, vector, precision=highest)

    slab_blocks = own_blocks * n_rad
    copies = n_slab * n_rad
    where_read = ((slab - 1) * slab_blocks + pattern).reshape(-1).astype(jnp.int32)
    force_t = force.T
    velocity, send = first_velocity(preconditioner, force, copies)
    held, velocity = lax.optimization_barrier((preconditioner, velocity))
    transposed = jnp.swapaxes(held, 1, 2)
    for sweep_index in range(1, ITERS):
        gathered = lax.all_to_all(send, ("slab", "rad"), 0, 0, tiled=True)
        velocity, send = sweep(
            where_read, gathered, stiffness, transposed, force_t, velocity, copies
        )
    return (q_next, arrivals, element_stress, velocity)


def solution(mesh):
    placed = (
        P(None, ("slab", "rad")),
        P(None, ("slab", "rad")),
        P(None, "slab"),
        P(("slab", "rad")),
        P(("slab", "rad")),
        P(("slab", "rad")),
        P(),
        P(("slab", "rad"), None, None, None),
        P(("slab", "rad"), None),
        P(("slab", "rad"), None, None),
    )
    return jax.shard_map(
        body,
        mesh=mesh,
        in_specs=placed,
        out_specs=(
            P(None, ("slab", "rad")),
            P(None, None, ("slab", "rad")),
            P(None, ("slab", "rad")),
            P(("slab", "rad"), None),
        ),
        check_vma=False,
    )
```

```python
import functools

import jax
import jax.numpy as jnp
from jax import lax
from jax.experimental import pallas as pl
from jax.experimental.pallas import tpu as pltpu
from jax.sharding import PartitionSpec as P

BLOCK = 192
ITERS = 6
CHUNK = 512
STRESS_CHUNK = 4096
UPDATE_PARTS = 4

extensibility = 50.0
time_step = 0.01
noise_scale = 0.1
damping = 0.6
highest = lax.Precision.HIGHEST
nt_dims = (((1,), (1,)), ((), ()))


def round_up(value, step):
    return -(-value // step) * step


def bf16_pieces(x):
    hi = x.astype(jnp.bfloat16)
    rest = x - hi.astype(jnp.float32)
    mid = rest.astype(jnp.bfloat16)
    lo = (rest - mid.astype(jnp.float32)).astype(jnp.bfloat16)
    return (hi, mid, lo)


def spring_terms(q):
    radial = q[0:1]
    axial = q[1:2]
    azimuth = q[2:3]
    stretch = radial * radial + axial * axial + azimuth * azimuth
    spring = 1.0 / (1.0 - stretch / extensibility)
    terms = (
        spring * radial * radial - 1.0,
        spring * axial * axial - 1.0,
        spring * radial * axial,
        spring * azimuth * azimuth - 1.0,
    )
    return spring, terms


def stress_kernel(slab_ref, q_ref, e_ref, m_ref, send_ref, acc_ref, *, groups, rows):
    count = q_ref.shape[1]
    n_dev = send_ref.shape[0]
    n_rad = groups // 3
    acc_ref[...] = jnp.zeros_like(acc_ref)
    low_iota = lax.broadcasted_iota(jnp.int32, (128, STRESS_CHUNK), 0)
    row_iota = lax.broadcasted_iota(jnp.int32, (rows, STRESS_CHUNK), 0)
    zero = jnp.zeros((), jnp.bfloat16)

    def body(step, carry):
        cols = pl.ds(pl.multiple_of(step * STRESS_CHUNK, STRESS_CHUNK), STRESS_CHUNK)
        q = q_ref[:, cols]
        element = e_ref[:, cols]
        move = m_ref[:, cols]
        spring, terms = spring_terms(q)
        kind = jnp.where(move == 0, 1, jnp.where(move == 1, 2, 0))
        key = kind * groups + (element >> 7)
        low = (low_iota == (element & 127)).astype(jnp.bfloat16)
        low = jnp.concatenate([low, low], axis=1)
        mask = row_iota == key
        spread = jnp.concatenate(
            [
                jnp.concatenate(
                    [jnp.where(mask, piece, zero) for piece in bf16_pieces(term)[:2]], axis=1
                )
                for term in terms
            ],
            axis=0,
        )
        acc_ref[...] += lax.dot_general(spread, low, nt_dims, preferred_element_type=jnp.float32)
        return carry

    lax.fori_loop(0, count // STRESS_CHUNK, body, 0)
    send_ref[...] = jnp.zeros_like(send_ref)
    slab = slab_ref[0]
    for kind in range(3):
        target = slab - 1 + kind

        @pl.when(jnp.logical_and(target >= 0, target * n_rad < n_dev))
        def _():
            for r in range(n_rad):
                for c in range(4):
                    start = c * rows + kind * groups + r * 3
                    send_ref[target * n_rad + r, c * 3 : c * 3 + 3, :] = acc_ref[start : start + 3, :]


def update_kernel(
    q_ref, inc_ref, e_ref, m_ref, tab_ref, start_ref, qn_ref, up_ref, dn_ref, tri_ref, *, groups16, slots16, first
):
    count = qn_ref.shape[1]
    up_ref[...] = jnp.zeros_like(up_ref)
    dn_ref[...] = jnp.zeros_like(dn_ref)
    before = lax.broadcasted_iota(jnp.int32, (CHUNK, CHUNK), 0)
    after = lax.broadcasted_iota(jnp.int32, (CHUNK, CHUNK), 1)
    tri_ref[...] = (before < after).astype(jnp.bfloat16)
    low_iota = lax.broadcasted_iota(jnp.int32, (128, CHUNK), 0)
    group_iota = lax.broadcasted_iota(jnp.int32, (groups16, CHUNK), 0)
    slot_iota = lax.broadcasted_iota(jnp.int32, (slots16, CHUNK), 0)
    flag_row = lax.broadcasted_iota(jnp.int32, (8, CHUNK), 0)
    zero = jnp.zeros((), jnp.bfloat16)

    def body(step, offsets):
        cols = pl.ds(pl.multiple_of((first + step) * CHUNK, CHUNK), CHUNK)
        q = q_ref[:, cols]
        inc = inc_ref[:, cols]
        element = e_ref[:, cols]
        move = m_ref[:, cols]
        low = (low_iota == (element & 127)).astype(jnp.bfloat16)
        picked = jnp.dot(
            tab_ref[...], jnp.concatenate([low, low, low], axis=0), preferred_element_type=jnp.float32
        )
        hit = group_iota == (element >> 7)
        grads = [
            jnp.sum(
                jnp.where(hit, picked[c * groups16 : (c + 1) * groups16], 0.0),
                axis=0,
                keepdims=True,
            )
            for c in range(5)
        ]
        radial = q[0:1]
        axial = q[1:2]
        azimuth = q[2:3]
        spring, terms = spring_terms(q)
        drift = (
            grads[0] * radial + grads[1] * axial,
            grads[2] * radial + grads[3] * axial,
            grads[4] * azimuth,
        )
        q_next = [
            q[k : k + 1] + time_step * (drift[k] - 0.5 * spring * q[k : k + 1]) + noise_scale * inc[k : k + 1]
            for k in range(3)
        ]
        qn_ref[:, pl.ds(pl.multiple_of(step * CHUNK, CHUNK), CHUNK)] = jnp.concatenate(q_next, axis=0)
        going_up = move == 1
        going_down = move == -1
        flags = jnp.where(
            flag_row == 0,
            going_up.astype(jnp.float32),
            jnp.where(flag_row == 1, going_down.astype(jnp.float32), 0.0),
        )
        ranks = jnp.dot(flags.astype(jnp.bfloat16), tri_ref[...], preferred_element_type=jnp.float32)
        slots = (ranks + offsets).astype(jnp.int32)
        pieces = [bf16_pieces(value) for value in q_next]
        for direction, chosen, out_ref in ((0, going_up, up_ref), (1, going_down, dn_ref)):
            slot = slots[direction : direction + 1]
            place = ((low_iota == (slot & 127)) & chosen).astype(jnp.bfloat16)
            place = jnp.concatenate([place, place, place], axis=1)
            which = slot_iota == (slot >> 7)
            spread = jnp.concatenate(
                [
                    jnp.concatenate([jnp.where(which, piece, zero) for piece in pieces[k]], axis=1)
                    for k in range(3)
                ],
                axis=0,
            )
            out_ref[...] += lax.dot_general(spread, place, nt_dims, preferred_element_type=jnp.float32)
        return offsets + jnp.sum(flags, axis=1, keepdims=True)

    lax.fori_loop(0, count // CHUNK, body, start_ref[...])


def stress_partials(slab, q_state, element, migration, slab_elems, n_dev):
    groups = slab_elems // 128
    rows = round_up(3 * groups, 16)
    count = q_state.shape[1]
    vmem = pl.BlockSpec(memory_space=pltpu.VMEM)
    return pl.pallas_call(
        functools.partial(stress_kernel, groups=groups, rows=rows),
        out_shape=jax.ShapeDtypeStruct((n_dev, 12, 128), jnp.float32),
        in_specs=[pl.BlockSpec(memory_space=pltpu.SMEM)] + [vmem] * 3,
        out_specs=vmem,
        scratch_shapes=[pltpu.VMEM((4 * rows, 128), jnp.float32)],
        cost_estimate=pl.CostEstimate(
            flops=2 * 3 * 4 * rows * 128 * count, transcendentals=0, bytes_accessed=20 * count
        ),
    )(slab, q_state, element.reshape(1, -1), migration.reshape(1, -1))


def first_kernel(pt_ref, dt_ref, g_ref, vout_ref, send_ref, ft_ref):
    own = vout_ref.shape[0]
    rows = []
    for b in range(own):
        column = jnp.sum(dt_ref[...] * g_ref[b : b + 1, :], axis=1, keepdims=True)
        ft_ref[:, b : b + 1] = column
        rows.append(damping * jnp.sum(pt_ref[b] * column, axis=0, keepdims=True))
    fresh = jnp.concatenate(rows, axis=0)
    vout_ref[...] = fresh
    for k in range(send_ref.shape[0] // own):
        send_ref[k * own : (k + 1) * own, :] = fresh


def first_velocity(transposed, div_t, groups, copies):
    own, size = transposed.shape[0], transposed.shape[1]
    return pl.pallas_call(
        first_kernel,
        out_shape=(
            jax.ShapeDtypeStruct((own, size), jnp.float32),
            jax.ShapeDtypeStruct((copies * own, size), jnp.float32),
            jax.ShapeDtypeStruct((size, own), jnp.float32),
        ),
        cost_estimate=pl.CostEstimate(
            flops=2 * (transposed.size + own * div_t.size),
            transcendentals=0,
            bytes_accessed=4 * (transposed.size + div_t.size),
        ),
    )(transposed, div_t, groups)


def update_and_pack(q_state, increments, element, migration, table, capacity):
    rows, slab_elems = table.shape
    groups = slab_elems // 128
    groups16 = round_up(groups, 16)
    slots = capacity // 128
    slots16 = round_up(slots, 16)
    arranged = jnp.pad(table.reshape(rows, groups, 128), ((0, 0), (0, groups16 - groups), (0, 0)))
    arranged = arranged.reshape(rows * groups16, 128)
    hi = lax.reduce_precision(arranged, exponent_bits=8, mantissa_bits=7)
    rest = arranged - hi
    mid = lax.reduce_precision(rest, exponent_bits=8, mantissa_bits=7)
    lo = rest - mid
    pieces = jnp.concatenate([hi, mid, lo], axis=1).astype(jnp.bfloat16)
    count = q_state.shape[1]
    parts = UPDATE_PARTS
    share = count // parts
    flags = jnp.stack([migration == 1, migration == -1]).astype(jnp.float32)
    per_part = jnp.sum(flags.reshape(2, parts, share), axis=2)
    starts = jnp.cumsum(per_part, axis=1) - per_part
    starts = jnp.pad(starts.T, ((0, 0), (0, 6)))[:, :, None]
    q_parts, up, down = [], 0.0, 0.0
    for part in range(parts):
        q_part, up_part, down_part = pl.pallas_call(
            functools.partial(
                update_kernel, groups16=groups16, slots16=slots16, first=part * share // CHUNK
            ),
            out_shape=(
                jax.ShapeDtypeStruct((3, share), jnp.float32),
                jax.ShapeDtypeStruct((3 * slots16, 128), jnp.float32),
                jax.ShapeDtypeStruct((3 * slots16, 128), jnp.float32),
            ),
            scratch_shapes=[pltpu.VMEM((CHUNK, CHUNK), jnp.bfloat16)],
            cost_estimate=pl.CostEstimate(
                flops=16 * 3 * (5 * groups16 + 6 * slots16) * 128 * share,
                transcendentals=0,
                bytes_accessed=40 * share,
            ),
        )(
            q_state,
            increments,
            element.reshape(1, -1),
            migration.reshape(1, -1),
            pieces,
            starts[part],
        )
        q_parts.append(q_part)
        up = up + up_part
        down = down + down_part
    q_next = jnp.concatenate(q_parts, axis=1)

    def unpack(acc):
        return acc.reshape(3, slots16, 128)[:, :slots].reshape(3, slots * 128)

    return q_next, unpack(up), unpack(down)


def sweep_kernel(idx_ref, g_ref, s_ref, pt_ref, ft_ref, v_ref, vout_ref, send_ref):
    total = g_ref.shape[0]
    own = v_ref.shape[0]
    width = s_ref.shape[1]
    rows = []
    for b in range(own):
        acc = None
        for n in range(width):
            w = idx_ref[b * width + n]
            inside = jnp.logical_and(w >= 0, w < total)
            near = g_ref[pl.ds(jnp.clip(w, 0, total - 1), 1), :]
            near = jnp.where(inside, near, 0.0)
            term = s_ref[b, n] * near
            acc = term if acc is None else acc + term
        image = jnp.sum(acc, axis=1, keepdims=True)
        rest = ft_ref[:, b : b + 1] - image
        update = jnp.sum(pt_ref[b] * rest, axis=0, keepdims=True)
        rows.append(v_ref[b : b + 1, :] + damping * update)
    fresh = jnp.concatenate(rows, axis=0)
    vout_ref[...] = fresh
    for k in range(send_ref.shape[0] // own):
        send_ref[k * own : (k + 1) * own, :] = fresh


def sweep(where_read, gathered, stiffness, transposed, force_t, velocity, copies):
    own = velocity.shape[0]
    vmem = pl.BlockSpec(memory_space=pltpu.VMEM)
    return pl.pallas_call(
        sweep_kernel,
        out_shape=(
            jax.ShapeDtypeStruct(velocity.shape, jnp.float32),
            jax.ShapeDtypeStruct((copies * own, velocity.shape[1]), jnp.float32),
        ),
        in_specs=[pl.BlockSpec(memory_space=pltpu.SMEM)] + [vmem] * 5,
        out_specs=(vmem, vmem),
        cost_estimate=pl.CostEstimate(
            flops=2 * (stiffness.size + transposed.size),
            transcendentals=0,
            bytes_accessed=4 * (stiffness.size + transposed.size + gathered.size),
        ),
    )(where_read, gathered, stiffness, transposed, force_t, velocity)


def passed_along(array, axis, by):
    size = lax.axis_size(axis)
    pairs = [(i, i + by) for i in range(size) if 0 <= i + by < size]
    return lax.ppermute(array, axis, pairs)


def body(
    q_state,
    increments,
    velocity_grad,
    element,
    migration,
    volume,
    div_map,
    stiffness,
    pattern,
    preconditioner,
):
    capacity = migration.shape[0] // 16
    slab_elems = velocity_grad.shape[1]
    n_slab = lax.axis_size("slab")
    slab = lax.axis_index("slab")

    n_rad = lax.axis_size("rad")
    send = stress_partials(
        slab.reshape(1).astype(jnp.int32), q_state, element, migration, slab_elems, n_slab * n_rad
    )
    received = lax.all_to_all(send, ("slab", "rad"), 0, 0, tiled=True)
    sums = jnp.sum(received, axis=0).reshape(4, slab_elems // n_rad)
    element_stress = sums / volume

    q_next, upward, downward = update_and_pack(
        q_state, increments, element, migration, velocity_grad, capacity
    )
    from_lower = passed_along(upward, "slab", 1)
    from_upper = passed_along(downward, "slab", -1)
    arrivals = jnp.stack([from_lower, from_upper])

    own_blocks = stiffness.shape[0]
    groups = (
        element_stress.reshape(4, own_blocks, BLOCK // 4)
        .transpose(1, 0, 2)
        .reshape(own_blocks, BLOCK)
    )

    def precondition(vector):
        return jnp.einsum("bij,bj->bi", preconditioner, vector, precision=highest)

    slab_blocks = own_blocks * n_rad
    copies = n_slab * n_rad
    where_read = ((slab - 1) * slab_blocks + pattern).reshape(-1).astype(jnp.int32)
    transposed = jnp.swapaxes(preconditioner, 1, 2)
    velocity, send, force_t = first_velocity(transposed, div_map.T, groups, copies)
    for sweep_index in range(1, ITERS):
        gathered = lax.all_to_all(send, ("slab", "rad"), 0, 0, tiled=True)
        velocity, send = sweep(
            where_read, gathered, stiffness, transposed, force_t, velocity, copies
        )
    return (q_next, arrivals, element_stress, velocity)


def solution(mesh):
    placed = (
        P(None, ("slab", "rad")),
        P(None, ("slab", "rad")),
        P(None, "slab"),
        P(("slab", "rad")),
        P(("slab", "rad")),
        P(("slab", "rad")),
        P(),
        P(("slab", "rad"), None, None, None),
        P(("slab", "rad"), None),
        P(("slab", "rad"), None, None),
    )
    return jax.shard_map(
        body,
        mesh=mesh,
        in_specs=placed,
        out_specs=(
            P(None, ("slab", "rad")),
            P(None, None, ("slab", "rad")),
            P(None, ("slab", "rad")),
            P(("slab", "rad"), None),
        ),
        check_vma=False,
    )
```

```python
import functools

import jax
import jax.numpy as jnp
from jax import lax
from jax.experimental import pallas as pl
from jax.experimental.pallas import tpu as pltpu
from jax.sharding import PartitionSpec as P

BLOCK = 192
ITERS = 6
CHUNK = 512
STRESS_CHUNK = 4096
UPDATE_PARTS = 8

extensibility = 50.0
time_step = 0.01
noise_scale = 0.1
damping = 0.6
highest = lax.Precision.HIGHEST
nt_dims = (((1,), (1,)), ((), ()))


def round_up(value, step):
    return -(-value // step) * step


def bf16_pieces(x):
    hi = x.astype(jnp.bfloat16)
    rest = x - hi.astype(jnp.float32)
    mid = rest.astype(jnp.bfloat16)
    lo = (rest - mid.astype(jnp.float32)).astype(jnp.bfloat16)
    return (hi, mid, lo)


def spring_terms(q):
    radial = q[0:1]
    axial = q[1:2]
    azimuth = q[2:3]
    stretch = radial * radial + axial * axial + azimuth * azimuth
    spring = 1.0 / (1.0 - stretch / extensibility)
    terms = (
        spring * radial * radial - 1.0,
        spring * axial * axial - 1.0,
        spring * radial * axial,
        spring * azimuth * azimuth - 1.0,
    )
    return spring, terms


def stress_kernel(slab_ref, q_ref, e_ref, m_ref, send_ref, acc_ref, *, groups, rows):
    count = q_ref.shape[1]
    n_dev = send_ref.shape[0]
    n_rad = groups // 3
    acc_ref[...] = jnp.zeros_like(acc_ref)
    low_iota = lax.broadcasted_iota(jnp.int32, (128, STRESS_CHUNK), 0)
    row_iota = lax.broadcasted_iota(jnp.int32, (rows, STRESS_CHUNK), 0)
    zero = jnp.zeros((), jnp.bfloat16)

    def body(step, carry):
        cols = pl.ds(pl.multiple_of(step * STRESS_CHUNK, STRESS_CHUNK), STRESS_CHUNK)
        q = q_ref[:, cols]
        element = e_ref[:, cols]
        move = m_ref[:, cols]
        spring, terms = spring_terms(q)
        kind = jnp.where(move == 0, 1, jnp.where(move == 1, 2, 0))
        key = kind * groups + (element >> 7)
        low = (low_iota == (element & 127)).astype(jnp.bfloat16)
        low = jnp.concatenate([low, low], axis=1)
        mask = row_iota == key
        spread = jnp.concatenate(
            [
                jnp.concatenate(
                    [jnp.where(mask, piece, zero) for piece in bf16_pieces(term)[:2]], axis=1
                )
                for term in terms
            ],
            axis=0,
        )
        acc_ref[...] += lax.dot_general(spread, low, nt_dims, preferred_element_type=jnp.float32)
        return carry

    lax.fori_loop(0, count // STRESS_CHUNK, body, 0)
    send_ref[...] = jnp.zeros_like(send_ref)
    slab = slab_ref[0]
    for kind in range(3):
        target = slab - 1 + kind

        @pl.when(jnp.logical_and(target >= 0, target * n_rad < n_dev))
        def _():
            for r in range(n_rad):
                for c in range(4):
                    start = c * rows + kind * groups + r * 3
                    send_ref[target * n_rad + r, c * 3 : c * 3 + 3, :] = acc_ref[start : start + 3, :]


def update_kernel(
    q_ref, inc_ref, e_ref, m_ref, tab_ref, start_ref, after_ref, qn_ref, up_ref, dn_ref, tri_ref, *, groups16, slots16, first
):
    count = qn_ref.shape[1]
    up_ref[...] = jnp.zeros_like(up_ref)
    dn_ref[...] = jnp.zeros_like(dn_ref)
    before = lax.broadcasted_iota(jnp.int32, (CHUNK, CHUNK), 0)
    after = lax.broadcasted_iota(jnp.int32, (CHUNK, CHUNK), 1)
    tri_ref[...] = (before < after).astype(jnp.bfloat16)
    low_iota = lax.broadcasted_iota(jnp.int32, (128, CHUNK), 0)
    group_iota = lax.broadcasted_iota(jnp.int32, (groups16, CHUNK), 0)
    slot_iota = lax.broadcasted_iota(jnp.int32, (slots16, CHUNK), 0)
    flag_row = lax.broadcasted_iota(jnp.int32, (8, CHUNK), 0)
    zero = jnp.zeros((), jnp.bfloat16)

    def body(step, offsets):
        cols = pl.ds(pl.multiple_of((first + step) * CHUNK, CHUNK), CHUNK)
        q = q_ref[:, cols]
        inc = inc_ref[:, cols]
        element = e_ref[:, cols]
        move = m_ref[:, cols]
        low = (low_iota == (element & 127)).astype(jnp.bfloat16)
        picked = jnp.dot(
            tab_ref[...], jnp.concatenate([low, low, low], axis=0), preferred_element_type=jnp.float32
        )
        hit = group_iota == (element >> 7)
        grads = [
            jnp.sum(
                jnp.where(hit, picked[c * groups16 : (c + 1) * groups16], 0.0),
                axis=0,
                keepdims=True,
            )
            for c in range(5)
        ]
        radial = q[0:1]
        axial = q[1:2]
        azimuth = q[2:3]
        spring, terms = spring_terms(q)
        drift = (
            grads[0] * radial + grads[1] * axial,
            grads[2] * radial + grads[3] * axial,
            grads[4] * azimuth,
        )
        q_next = [
            q[k : k + 1] + time_step * (drift[k] - 0.5 * spring * q[k : k + 1]) + noise_scale * inc[k : k + 1]
            for k in range(3)
        ]
        qn_ref[:, pl.ds(pl.multiple_of(step * CHUNK, CHUNK), CHUNK)] = jnp.concatenate(q_next, axis=0)
        going_up = move == 1
        going_down = move == -1
        flags = jnp.where(
            flag_row == 0,
            going_up.astype(jnp.float32),
            jnp.where(flag_row == 1, going_down.astype(jnp.float32), 0.0),
        )
        ranks = jnp.dot(flags.astype(jnp.bfloat16), tri_ref[...], preferred_element_type=jnp.float32)
        slots = (ranks + offsets).astype(jnp.int32)
        pieces = [bf16_pieces(value) for value in q_next]
        for direction, chosen, out_ref in ((0, going_up, up_ref), (1, going_down, dn_ref)):
            slot = slots[direction : direction + 1]
            place = ((low_iota == (slot & 127)) & chosen).astype(jnp.bfloat16)
            place = jnp.concatenate([place, place, place], axis=1)
            which = slot_iota == (slot >> 7)
            spread = jnp.concatenate(
                [
                    jnp.concatenate([jnp.where(which, piece, zero) for piece in pieces[k]], axis=1)
                    for k in range(3)
                ],
                axis=0,
            )
            out_ref[...] += lax.dot_general(spread, place, nt_dims, preferred_element_type=jnp.float32)
        return offsets + jnp.sum(flags, axis=1, keepdims=True)

    lax.fori_loop(0, count // CHUNK, body, start_ref[...])


def stress_partials(slab, q_state, element, migration, slab_elems, n_dev):
    groups = slab_elems // 128
    rows = round_up(3 * groups, 16)
    count = q_state.shape[1]
    vmem = pl.BlockSpec(memory_space=pltpu.VMEM)
    return pl.pallas_call(
        functools.partial(stress_kernel, groups=groups, rows=rows),
        out_shape=jax.ShapeDtypeStruct((n_dev, 12, 128), jnp.float32),
        in_specs=[pl.BlockSpec(memory_space=pltpu.SMEM)] + [vmem] * 3,
        out_specs=vmem,
        scratch_shapes=[pltpu.VMEM((4 * rows, 128), jnp.float32)],
        cost_estimate=pl.CostEstimate(
            flops=2 * 3 * 4 * rows * 128 * count, transcendentals=0, bytes_accessed=20 * count
        ),
    )(slab, q_state, element.reshape(1, -1), migration.reshape(1, -1))


def first_kernel(pt_ref, ft_ref, vout_ref, send_ref):
    own = vout_ref.shape[0]
    rows = [
        damping * jnp.sum(pt_ref[b] * ft_ref[:, b : b + 1], axis=0, keepdims=True)
        for b in range(own)
    ]
    fresh = jnp.concatenate(rows, axis=0)
    vout_ref[...] = fresh
    for k in range(send_ref.shape[0] // own):
        send_ref[k * own : (k + 1) * own, :] = fresh


def first_velocity(transposed, force_t, copies):
    own, size = transposed.shape[0], transposed.shape[1]
    return pl.pallas_call(
        first_kernel,
        out_shape=(
            jax.ShapeDtypeStruct((own, size), jnp.float32),
            jax.ShapeDtypeStruct((copies * own, size), jnp.float32),
        ),
        cost_estimate=pl.CostEstimate(
            flops=2 * transposed.size, transcendentals=0, bytes_accessed=4 * transposed.size
        ),
    )(transposed, force_t)


def update_prepare(migration, table, capacity, count):
    rows, slab_elems = table.shape
    groups = slab_elems // 128
    groups16 = round_up(groups, 16)
    slots = capacity // 128
    slots16 = round_up(slots, 16)
    arranged = jnp.pad(table.reshape(rows, groups, 128), ((0, 0), (0, groups16 - groups), (0, 0)))
    arranged = arranged.reshape(rows * groups16, 128)
    hi = lax.reduce_precision(arranged, exponent_bits=8, mantissa_bits=7)
    rest = arranged - hi
    mid = lax.reduce_precision(rest, exponent_bits=8, mantissa_bits=7)
    lo = rest - mid
    pieces = jnp.concatenate([hi, mid, lo], axis=1).astype(jnp.bfloat16)
    share = count // UPDATE_PARTS
    flags = jnp.stack([migration == 1, migration == -1]).astype(jnp.float32)
    per_part = jnp.sum(flags.reshape(2, UPDATE_PARTS, share), axis=2)
    starts = jnp.cumsum(per_part, axis=1) - per_part
    starts = jnp.pad(starts.T, ((0, 0), (0, 6)))[:, :, None]
    return pieces, starts, groups16, slots16


def update_part(part, prepared, after, q_state, increments, element, migration):
    pieces, starts, groups16, slots16 = prepared
    share = q_state.shape[1] // UPDATE_PARTS
    vmem = pl.BlockSpec(memory_space=pltpu.VMEM)
    return pl.pallas_call(
        functools.partial(
            update_kernel, groups16=groups16, slots16=slots16, first=part * share // CHUNK
        ),
        out_shape=(
            jax.ShapeDtypeStruct((3, share), jnp.float32),
            jax.ShapeDtypeStruct((3 * slots16, 128), jnp.float32),
            jax.ShapeDtypeStruct((3 * slots16, 128), jnp.float32),
        ),
        in_specs=[vmem] * 6 + [pl.BlockSpec(memory_space=pl.ANY)],
        out_specs=(vmem, vmem, vmem),
        scratch_shapes=[pltpu.VMEM((CHUNK, CHUNK), jnp.bfloat16)],
        cost_estimate=pl.CostEstimate(
            flops=16 * 3 * (5 * groups16 + 6 * slots16) * 128 * share,
            transcendentals=0,
            bytes_accessed=40 * share,
        ),
    )(
        q_state,
        increments,
        element.reshape(1, -1),
        migration.reshape(1, -1),
        pieces,
        starts[part],
        after,
    )


def unpack(acc, capacity):
    slots = capacity // 128
    return acc.reshape(3, -1, 128)[:, :slots].reshape(3, slots * 128)


def sweep_kernel(idx_ref, g_ref, s_ref, pt_ref, ft_ref, v_ref, vout_ref, send_ref):
    total = g_ref.shape[0]
    own = v_ref.shape[0]
    width = s_ref.shape[1]
    rows = []
    for b in range(own):
        acc = None
        for n in range(width):
            w = idx_ref[b * width + n]
            inside = jnp.logical_and(w >= 0, w < total)
            near = g_ref[pl.ds(jnp.clip(w, 0, total - 1), 1), :]
            near = jnp.where(inside, near, 0.0)
            term = s_ref[b, n] * near
            acc = term if acc is None else acc + term
        image = jnp.sum(acc, axis=1, keepdims=True)
        rest = ft_ref[:, b : b + 1] - image
        update = jnp.sum(pt_ref[b] * rest, axis=0, keepdims=True)
        rows.append(v_ref[b : b + 1, :] + damping * update)
    fresh = jnp.concatenate(rows, axis=0)
    vout_ref[...] = fresh
    for k in range(send_ref.shape[0] // own):
        send_ref[k * own : (k + 1) * own, :] = fresh


def sweep(where_read, gathered, stiffness, transposed, force_t, velocity, copies):
    own = velocity.shape[0]
    vmem = pl.BlockSpec(memory_space=pltpu.VMEM)
    return pl.pallas_call(
        sweep_kernel,
        out_shape=(
            jax.ShapeDtypeStruct(velocity.shape, jnp.float32),
            jax.ShapeDtypeStruct((copies * own, velocity.shape[1]), jnp.float32),
        ),
        in_specs=[pl.BlockSpec(memory_space=pltpu.SMEM)] + [vmem] * 5,
        out_specs=(vmem, vmem),
        cost_estimate=pl.CostEstimate(
            flops=2 * (stiffness.size + transposed.size),
            transcendentals=0,
            bytes_accessed=4 * (stiffness.size + transposed.size + gathered.size),
        ),
    )(where_read, gathered, stiffness, transposed, force_t, velocity)


def passed_along(array, axis, by):
    size = lax.axis_size(axis)
    pairs = [(i, i + by) for i in range(size) if 0 <= i + by < size]
    return lax.ppermute(array, axis, pairs)


def body(
    q_state,
    increments,
    velocity_grad,
    element,
    migration,
    volume,
    div_map,
    stiffness,
    pattern,
    preconditioner,
):
    capacity = migration.shape[0] // 16
    slab_elems = velocity_grad.shape[1]
    n_slab = lax.axis_size("slab")
    slab = lax.axis_index("slab")

    n_rad = lax.axis_size("rad")
    send = stress_partials(
        slab.reshape(1).astype(jnp.int32), q_state, element, migration, slab_elems, n_slab * n_rad
    )
    received = lax.all_to_all(send, ("slab", "rad"), 0, 0, tiled=True)
    sums = jnp.sum(received, axis=0).reshape(4, slab_elems // n_rad)
    element_stress = sums / volume

    prepared = update_prepare(migration, velocity_grad, capacity, q_state.shape[1])

    own_blocks = stiffness.shape[0]
    groups = (
        element_stress.reshape(4, own_blocks, BLOCK // 4)
        .transpose(1, 0, 2)
        .reshape(own_blocks, BLOCK)
    )
    force = jnp.dot(groups, div_map, precision=highest)

    def precondition(vector):
        return jnp.einsum("bij,bj->bi", preconditioner, vector, precision=highest)

    slab_blocks = own_blocks * n_rad
    copies = n_slab * n_rad
    where_read = ((slab - 1) * slab_blocks + pattern).reshape(-1).astype(jnp.int32)
    transposed = jnp.swapaxes(preconditioner, 1, 2)
    force_t = force.T
    q_parts, upward, downward = [], 0.0, 0.0
    q_part, upward, downward = update_part(0, prepared, element, q_state, increments, element, migration)
    q_parts.append(q_part)
    velocity, send = first_velocity(transposed, force_t, copies)
    for sweep_index in range(1, ITERS):
        for repeat in range(2):
            if len(q_parts) < UPDATE_PARTS:
                q_part, up_part, down_part = update_part(
                    len(q_parts), prepared, velocity, q_state, increments, element, migration
                )
                q_parts.append(q_part)
                upward = upward + up_part
                downward = downward + down_part
        gathered = lax.all_to_all(send, ("slab", "rad"), 0, 0, tiled=True)
        velocity, send = sweep(
            where_read, gathered, stiffness, transposed, force_t, velocity, copies
        )
    while len(q_parts) < UPDATE_PARTS:
        q_part, up_part, down_part = update_part(
            len(q_parts), prepared, velocity, q_state, increments, element, migration
        )
        q_parts.append(q_part)
        upward = upward + up_part
        downward = downward + down_part
    q_next = jnp.concatenate(q_parts, axis=1)
    from_lower = passed_along(unpack(upward, capacity), "slab", 1)
    from_upper = passed_along(unpack(downward, capacity), "slab", -1)
    arrivals = jnp.stack([from_lower, from_upper])
    return (q_next, arrivals, element_stress, velocity)


def solution(mesh):
    placed = (
        P(None, ("slab", "rad")),
        P(None, ("slab", "rad")),
        P(None, "slab"),
        P(("slab", "rad")),
        P(("slab", "rad")),
        P(("slab", "rad")),
        P(),
        P(("slab", "rad"), None, None, None),
        P(("slab", "rad"), None),
        P(("slab", "rad"), None, None),
    )
    return jax.shard_map(
        body,
        mesh=mesh,
        in_specs=placed,
        out_specs=(
            P(None, ("slab", "rad")),
            P(None, None, ("slab", "rad")),
            P(None, ("slab", "rad")),
            P(("slab", "rad"), None),
        ),
        check_vma=False,
    )
```

```python
import functools

import jax
import jax.numpy as jnp
from jax import lax
from jax.experimental import pallas as pl
from jax.experimental.pallas import tpu as pltpu
from jax.sharding import PartitionSpec as P

BLOCK = 192
ITERS = 6
CHUNK = 512
STRESS_CHUNK = 8192
UPDATE_PARTS = 4

extensibility = 50.0
time_step = 0.01
noise_scale = 0.1
damping = 0.6
highest = lax.Precision.HIGHEST
nt_dims = (((1,), (1,)), ((), ()))


def round_up(value, step):
    return -(-value // step) * step


def bf16_pieces(x):
    hi = x.astype(jnp.bfloat16)
    rest = x - hi.astype(jnp.float32)
    mid = rest.astype(jnp.bfloat16)
    lo = (rest - mid.astype(jnp.float32)).astype(jnp.bfloat16)
    return (hi, mid, lo)


def spring_terms(q):
    radial = q[0:1]
    axial = q[1:2]
    azimuth = q[2:3]
    stretch = radial * radial + axial * axial + azimuth * azimuth
    spring = 1.0 / (1.0 - stretch / extensibility)
    terms = (
        spring * radial * radial - 1.0,
        spring * axial * axial - 1.0,
        spring * radial * axial,
        spring * azimuth * azimuth - 1.0,
    )
    return spring, terms


def stress_kernel(slab_ref, q_ref, e_ref, m_ref, send_ref, acc_ref, *, groups, rows):
    count = q_ref.shape[1]
    n_dev = send_ref.shape[0]
    n_rad = groups // 3
    acc_ref[...] = jnp.zeros_like(acc_ref)
    low_iota = lax.broadcasted_iota(jnp.int32, (128, STRESS_CHUNK), 0)
    row_iota = lax.broadcasted_iota(jnp.int32, (rows, STRESS_CHUNK), 0)
    zero = jnp.zeros((), jnp.bfloat16)

    def body(step, carry):
        cols = pl.ds(pl.multiple_of(step * STRESS_CHUNK, STRESS_CHUNK), STRESS_CHUNK)
        q = q_ref[:, cols]
        element = e_ref[:, cols]
        move = m_ref[:, cols]
        spring, terms = spring_terms(q)
        kind = jnp.where(move == 0, 1, jnp.where(move == 1, 2, 0))
        key = kind * groups + (element >> 7)
        low = (low_iota == (element & 127)).astype(jnp.bfloat16)
        low = jnp.concatenate([low, low], axis=1)
        mask = row_iota == key
        spread = jnp.concatenate(
            [
                jnp.concatenate(
                    [jnp.where(mask, piece, zero) for piece in bf16_pieces(term)[:2]], axis=1
                )
                for term in terms
            ],
            axis=0,
        )
        acc_ref[...] += lax.dot_general(spread, low, nt_dims, preferred_element_type=jnp.float32)
        return carry

    lax.fori_loop(0, count // STRESS_CHUNK, body, 0)
    send_ref[...] = jnp.zeros_like(send_ref)
    slab = slab_ref[0]
    for kind in range(3):
        target = slab - 1 + kind

        @pl.when(jnp.logical_and(target >= 0, target * n_rad < n_dev))
        def _():
            for r in range(n_rad):
                for c in range(4):
                    start = c * rows + kind * groups + r * 3
                    send_ref[target * n_rad + r, c * 3 : c * 3 + 3, :] = acc_ref[start : start + 3, :]


def update_kernel(
    q_ref, inc_ref, e_ref, m_ref, tab_ref, start_ref, qn_ref, up_ref, dn_ref, tri_ref, *, groups16, slots16, first
):
    count = qn_ref.shape[1]
    up_ref[...] = jnp.zeros_like(up_ref)
    dn_ref[...] = jnp.zeros_like(dn_ref)
    before = lax.broadcasted_iota(jnp.int32, (CHUNK, CHUNK), 0)
    after = lax.broadcasted_iota(jnp.int32, (CHUNK, CHUNK), 1)
    tri_ref[...] = (before < after).astype(jnp.bfloat16)
    low_iota = lax.broadcasted_iota(jnp.int32, (128, CHUNK), 0)
    group_iota = lax.broadcasted_iota(jnp.int32, (groups16, CHUNK), 0)
    slot_iota = lax.broadcasted_iota(jnp.int32, (slots16, CHUNK), 0)
    flag_row = lax.broadcasted_iota(jnp.int32, (8, CHUNK), 0)
    zero = jnp.zeros((), jnp.bfloat16)

    def body(step, offsets):
        cols = pl.ds(pl.multiple_of((first + step) * CHUNK, CHUNK), CHUNK)
        q = q_ref[:, cols]
        inc = inc_ref[:, cols]
        element = e_ref[:, cols]
        move = m_ref[:, cols]
        low = (low_iota == (element & 127)).astype(jnp.bfloat16)
        picked = jnp.dot(
            tab_ref[...], jnp.concatenate([low, low, low], axis=0), preferred_element_type=jnp.float32
        )
        hit = group_iota == (element >> 7)
        grads = [
            jnp.sum(
                jnp.where(hit, picked[c * groups16 : (c + 1) * groups16], 0.0),
                axis=0,
                keepdims=True,
            )
            for c in range(5)
        ]
        radial = q[0:1]
        axial = q[1:2]
        azimuth = q[2:3]
        spring, terms = spring_terms(q)
        drift = (
            grads[0] * radial + grads[1] * axial,
            grads[2] * radial + grads[3] * axial,
            grads[4] * azimuth,
        )
        q_next = [
            q[k : k + 1] + time_step * (drift[k] - 0.5 * spring * q[k : k + 1]) + noise_scale * inc[k : k + 1]
            for k in range(3)
        ]
        qn_ref[:, pl.ds(pl.multiple_of(step * CHUNK, CHUNK), CHUNK)] = jnp.concatenate(q_next, axis=0)
        going_up = move == 1
        going_down = move == -1
        flags = jnp.where(
            flag_row == 0,
            going_up.astype(jnp.float32),
            jnp.where(flag_row == 1, going_down.astype(jnp.float32), 0.0),
        )
        ranks = jnp.dot(flags.astype(jnp.bfloat16), tri_ref[...], preferred_element_type=jnp.float32)
        slots = (ranks + offsets).astype(jnp.int32)
        pieces = [bf16_pieces(value) for value in q_next]
        for direction, chosen, out_ref in ((0, going_up, up_ref), (1, going_down, dn_ref)):
            slot = slots[direction : direction + 1]
            place = ((low_iota == (slot & 127)) & chosen).astype(jnp.bfloat16)
            place = jnp.concatenate([place, place, place], axis=1)
            which = slot_iota == (slot >> 7)
            spread = jnp.concatenate(
                [
                    jnp.concatenate([jnp.where(which, piece, zero) for piece in pieces[k]], axis=1)
                    for k in range(3)
                ],
                axis=0,
            )
            out_ref[...] += lax.dot_general(spread, place, nt_dims, preferred_element_type=jnp.float32)
        return offsets + jnp.sum(flags, axis=1, keepdims=True)

    lax.fori_loop(0, count // CHUNK, body, start_ref[...])


def stress_partials(slab, q_state, element, migration, slab_elems, n_dev):
    groups = slab_elems // 128
    rows = round_up(3 * groups, 16)
    count = q_state.shape[1]
    vmem = pl.BlockSpec(memory_space=pltpu.VMEM)
    return pl.pallas_call(
        functools.partial(stress_kernel, groups=groups, rows=rows),
        out_shape=jax.ShapeDtypeStruct((n_dev, 12, 128), jnp.float32),
        in_specs=[pl.BlockSpec(memory_space=pltpu.SMEM)] + [vmem] * 3,
        out_specs=vmem,
        scratch_shapes=[pltpu.VMEM((4 * rows, 128), jnp.float32)],
        cost_estimate=pl.CostEstimate(
            flops=2 * 3 * 4 * rows * 128 * count, transcendentals=0, bytes_accessed=20 * count
        ),
    )(slab, q_state, element.reshape(1, -1), migration.reshape(1, -1))


def first_kernel(pt_ref, ft_ref, vout_ref, send_ref):
    own = vout_ref.shape[0]
    rows = [
        damping * jnp.sum(pt_ref[b] * ft_ref[:, b : b + 1], axis=0, keepdims=True)
        for b in range(own)
    ]
    fresh = jnp.concatenate(rows, axis=0)
    vout_ref[...] = fresh
    for k in range(send_ref.shape[0] // own):
        send_ref[k * own : (k + 1) * own, :] = fresh


def first_velocity(transposed, force_t, copies):
    own, size = transposed.shape[0], transposed.shape[1]
    return pl.pallas_call(
        first_kernel,
        out_shape=(
            jax.ShapeDtypeStruct((own, size), jnp.float32),
            jax.ShapeDtypeStruct((copies * own, size), jnp.float32),
        ),
        cost_estimate=pl.CostEstimate(
            flops=2 * transposed.size, transcendentals=0, bytes_accessed=4 * transposed.size
        ),
    )(transposed, force_t)


def update_and_pack(q_state, increments, element, migration, table, capacity):
    rows, slab_elems = table.shape
    groups = slab_elems // 128
    groups16 = round_up(groups, 16)
    slots = capacity // 128
    slots16 = round_up(slots, 16)
    arranged = jnp.pad(table.reshape(rows, groups, 128), ((0, 0), (0, groups16 - groups), (0, 0)))
    arranged = arranged.reshape(rows * groups16, 128)
    hi = lax.reduce_precision(arranged, exponent_bits=8, mantissa_bits=7)
    rest = arranged - hi
    mid = lax.reduce_precision(rest, exponent_bits=8, mantissa_bits=7)
    lo = rest - mid
    pieces = jnp.concatenate([hi, mid, lo], axis=1).astype(jnp.bfloat16)
    count = q_state.shape[1]
    parts = UPDATE_PARTS
    share = count // parts
    flags = jnp.stack([migration == 1, migration == -1]).astype(jnp.float32)
    per_part = jnp.sum(flags.reshape(2, parts, share), axis=2)
    starts = jnp.cumsum(per_part, axis=1) - per_part
    starts = jnp.pad(starts.T, ((0, 0), (0, 6)))[:, :, None]
    q_parts, up, down = [], 0.0, 0.0
    for part in range(parts):
        q_part, up_part, down_part = pl.pallas_call(
            functools.partial(
                update_kernel, groups16=groups16, slots16=slots16, first=part * share // CHUNK
            ),
            out_shape=(
                jax.ShapeDtypeStruct((3, share), jnp.float32),
                jax.ShapeDtypeStruct((3 * slots16, 128), jnp.float32),
                jax.ShapeDtypeStruct((3 * slots16, 128), jnp.float32),
            ),
            scratch_shapes=[pltpu.VMEM((CHUNK, CHUNK), jnp.bfloat16)],
            cost_estimate=pl.CostEstimate(
                flops=16 * 3 * (5 * groups16 + 6 * slots16) * 128 * share,
                transcendentals=0,
                bytes_accessed=40 * share,
            ),
        )(
            q_state,
            increments,
            element.reshape(1, -1),
            migration.reshape(1, -1),
            pieces,
            starts[part],
        )
        q_parts.append(q_part)
        up = up + up_part
        down = down + down_part
    q_next = jnp.concatenate(q_parts, axis=1)

    def unpack(acc):
        return acc.reshape(3, slots16, 128)[:, :slots].reshape(3, slots * 128)

    return q_next, unpack(up), unpack(down)


def sweep_kernel(idx_ref, g_ref, s_ref, pt_ref, ft_ref, v_ref, vout_ref, send_ref):
    total = g_ref.shape[0]
    own = v_ref.shape[0]
    width = s_ref.shape[1]
    rows = []
    for b in range(own):
        acc = None
        for n in range(width):
            w = idx_ref[b * width + n]
            inside = jnp.logical_and(w >= 0, w < total)
            near = g_ref[pl.ds(jnp.clip(w, 0, total - 1), 1), :]
            near = jnp.where(inside, near, 0.0)
            term = s_ref[b, n] * near
            acc = term if acc is None else acc + term
        image = jnp.sum(acc, axis=1, keepdims=True)
        rest = ft_ref[:, b : b + 1] - image
        update = jnp.sum(pt_ref[b] * rest, axis=0, keepdims=True)
        rows.append(v_ref[b : b + 1, :] + damping * update)
    fresh = jnp.concatenate(rows, axis=0)
    vout_ref[...] = fresh
    for k in range(send_ref.shape[0] // own):
        send_ref[k * own : (k + 1) * own, :] = fresh


def sweep(where_read, gathered, stiffness, transposed, force_t, velocity, copies):
    own = velocity.shape[0]
    vmem = pl.BlockSpec(memory_space=pltpu.VMEM)
    return pl.pallas_call(
        sweep_kernel,
        out_shape=(
            jax.ShapeDtypeStruct(velocity.shape, jnp.float32),
            jax.ShapeDtypeStruct((copies * own, velocity.shape[1]), jnp.float32),
        ),
        in_specs=[pl.BlockSpec(memory_space=pltpu.SMEM)] + [vmem] * 5,
        out_specs=(vmem, vmem),
        cost_estimate=pl.CostEstimate(
            flops=2 * (stiffness.size + transposed.size),
            transcendentals=0,
            bytes_accessed=4 * (stiffness.size + transposed.size + gathered.size),
        ),
    )(where_read, gathered, stiffness, transposed, force_t, velocity)


def passed_along(array, axis, by):
    size = lax.axis_size(axis)
    pairs = [(i, i + by) for i in range(size) if 0 <= i + by < size]
    return lax.ppermute(array, axis, pairs)


def body(
    q_state,
    increments,
    velocity_grad,
    element,
    migration,
    volume,
    div_map,
    stiffness,
    pattern,
    preconditioner,
):
    capacity = migration.shape[0] // 16
    slab_elems = velocity_grad.shape[1]
    n_slab = lax.axis_size("slab")
    slab = lax.axis_index("slab")

    n_rad = lax.axis_size("rad")
    send = stress_partials(
        slab.reshape(1).astype(jnp.int32), q_state, element, migration, slab_elems, n_slab * n_rad
    )
    received = lax.all_to_all(send, ("slab", "rad"), 0, 0, tiled=True)
    sums = jnp.sum(received, axis=0).reshape(4, slab_elems // n_rad)
    element_stress = sums / volume

    q_next, upward, downward = update_and_pack(
        q_state, increments, element, migration, velocity_grad, capacity
    )
    from_lower = passed_along(upward, "slab", 1)
    from_upper = passed_along(downward, "slab", -1)
    arrivals = jnp.stack([from_lower, from_upper])

    own_blocks = stiffness.shape[0]
    groups = (
        element_stress.reshape(4, own_blocks, BLOCK // 4)
        .transpose(1, 0, 2)
        .reshape(own_blocks, BLOCK)
    )
    force = jnp.dot(groups, div_map, precision=highest)

    def precondition(vector):
        return jnp.einsum("bij,bj->bi", preconditioner, vector, precision=highest)

    slab_blocks = own_blocks * n_rad
    copies = n_slab * n_rad
    where_read = ((slab - 1) * slab_blocks + pattern).reshape(-1).astype(jnp.int32)
    transposed = jnp.swapaxes(preconditioner, 1, 2)
    force_t = force.T
    velocity, send = first_velocity(transposed, force_t, copies)
    for sweep_index in range(1, ITERS):
        gathered = lax.all_to_all(send, ("slab", "rad"), 0, 0, tiled=True)
        velocity, send = sweep(
            where_read, gathered, stiffness, transposed, force_t, velocity, copies
        )
    return (q_next, arrivals, element_stress, velocity)


def solution(mesh):
    placed = (
        P(None, ("slab", "rad")),
        P(None, ("slab", "rad")),
        P(None, "slab"),
        P(("slab", "rad")),
        P(("slab", "rad")),
        P(("slab", "rad")),
        P(),
        P(("slab", "rad"), None, None, None),
        P(("slab", "rad"), None),
        P(("slab", "rad"), None, None),
    )
    return jax.shard_map(
        body,
        mesh=mesh,
        in_specs=placed,
        out_specs=(
            P(None, ("slab", "rad")),
            P(None, None, ("slab", "rad")),
            P(None, ("slab", "rad")),
            P(("slab", "rad"), None),
        ),
        check_vma=False,
    )
```

```python
import functools

import jax
import jax.numpy as jnp
from jax import lax
from jax.experimental import pallas as pl
from jax.experimental.pallas import tpu as pltpu
from jax.sharding import PartitionSpec as P

BLOCK = 192
ITERS = 6
CHUNK = 1024
STRESS_CHUNK = 8192
UPDATE_PARTS = 4

extensibility = 50.0
time_step = 0.01
noise_scale = 0.1
damping = 0.6
highest = lax.Precision.HIGHEST
nt_dims = (((1,), (1,)), ((), ()))


def round_up(value, step):
    return -(-value // step) * step


def bf16_pieces(x):
    hi = x.astype(jnp.bfloat16)
    rest = x - hi.astype(jnp.float32)
    mid = rest.astype(jnp.bfloat16)
    lo = (rest - mid.astype(jnp.float32)).astype(jnp.bfloat16)
    return (hi, mid, lo)


def spring_terms(q):
    radial = q[0:1]
    axial = q[1:2]
    azimuth = q[2:3]
    stretch = radial * radial + axial * axial + azimuth * azimuth
    spring = 1.0 / (1.0 - stretch / extensibility)
    terms = (
        spring * radial * radial - 1.0,
        spring * axial * axial - 1.0,
        spring * radial * axial,
        spring * azimuth * azimuth - 1.0,
    )
    return spring, terms


def stress_kernel(slab_ref, q_ref, e_ref, m_ref, send_ref, acc_ref, *, groups, rows):
    count = q_ref.shape[1]
    n_dev = send_ref.shape[0]
    n_rad = groups // 3
    acc_ref[...] = jnp.zeros_like(acc_ref)
    low_iota = lax.broadcasted_iota(jnp.int32, (128, STRESS_CHUNK), 0)
    row_iota = lax.broadcasted_iota(jnp.int32, (rows, STRESS_CHUNK), 0)
    zero = jnp.zeros((), jnp.bfloat16)

    def body(step, carry):
        cols = pl.ds(pl.multiple_of(step * STRESS_CHUNK, STRESS_CHUNK), STRESS_CHUNK)
        q = q_ref[:, cols]
        element = e_ref[:, cols]
        move = m_ref[:, cols]
        spring, terms = spring_terms(q)
        kind = jnp.where(move == 0, 1, jnp.where(move == 1, 2, 0))
        key = kind * groups + (element >> 7)
        low = (low_iota == (element & 127)).astype(jnp.bfloat16)
        low = jnp.concatenate([low, low], axis=1)
        mask = row_iota == key
        spread = jnp.concatenate(
            [
                jnp.concatenate(
                    [jnp.where(mask, piece, zero) for piece in bf16_pieces(term)[:2]], axis=1
                )
                for term in terms
            ],
            axis=0,
        )
        acc_ref[...] += lax.dot_general(spread, low, nt_dims, preferred_element_type=jnp.float32)
        return carry

    lax.fori_loop(0, count // STRESS_CHUNK, body, 0)
    send_ref[...] = jnp.zeros_like(send_ref)
    slab = slab_ref[0]
    for kind in range(3):
        target = slab - 1 + kind

        @pl.when(jnp.logical_and(target >= 0, target * n_rad < n_dev))
        def _():
            for r in range(n_rad):
                for c in range(4):
                    start = c * rows + kind * groups + r * 3
                    send_ref[target * n_rad + r, c * 3 : c * 3 + 3, :] = acc_ref[start : start + 3, :]


def update_kernel(
    q_ref, inc_ref, e_ref, m_ref, tab_ref, start_ref, qn_ref, up_ref, dn_ref, tri_ref, *, groups16, slots16, first
):
    count = qn_ref.shape[1]
    up_ref[...] = jnp.zeros_like(up_ref)
    dn_ref[...] = jnp.zeros_like(dn_ref)
    before = lax.broadcasted_iota(jnp.int32, (CHUNK, CHUNK), 0)
    after = lax.broadcasted_iota(jnp.int32, (CHUNK, CHUNK), 1)
    tri_ref[...] = (before < after).astype(jnp.bfloat16)
    low_iota = lax.broadcasted_iota(jnp.int32, (128, CHUNK), 0)
    group_iota = lax.broadcasted_iota(jnp.int32, (groups16, CHUNK), 0)
    slot_iota = lax.broadcasted_iota(jnp.int32, (slots16, CHUNK), 0)
    flag_row = lax.broadcasted_iota(jnp.int32, (8, CHUNK), 0)
    zero = jnp.zeros((), jnp.bfloat16)

    def body(step, offsets):
        cols = pl.ds(pl.multiple_of((first + step) * CHUNK, CHUNK), CHUNK)
        q = q_ref[:, cols]
        inc = inc_ref[:, cols]
        element = e_ref[:, cols]
        move = m_ref[:, cols]
        low = (low_iota == (element & 127)).astype(jnp.bfloat16)
        picked = jnp.dot(
            tab_ref[...], jnp.concatenate([low, low, low], axis=0), preferred_element_type=jnp.float32
        )
        hit = group_iota == (element >> 7)
        grads = [
            jnp.sum(
                jnp.where(hit, picked[c * groups16 : (c + 1) * groups16], 0.0),
                axis=0,
                keepdims=True,
            )
            for c in range(5)
        ]
        radial = q[0:1]
        axial = q[1:2]
        azimuth = q[2:3]
        spring, terms = spring_terms(q)
        drift = (
            grads[0] * radial + grads[1] * axial,
            grads[2] * radial + grads[3] * axial,
            grads[4] * azimuth,
        )
        q_next = [
            q[k : k + 1] + time_step * (drift[k] - 0.5 * spring * q[k : k + 1]) + noise_scale * inc[k : k + 1]
            for k in range(3)
        ]
        qn_ref[:, pl.ds(pl.multiple_of(step * CHUNK, CHUNK), CHUNK)] = jnp.concatenate(q_next, axis=0)
        going_up = move == 1
        going_down = move == -1
        flags = jnp.where(
            flag_row == 0,
            going_up.astype(jnp.float32),
            jnp.where(flag_row == 1, going_down.astype(jnp.float32), 0.0),
        )
        ranks = jnp.dot(flags.astype(jnp.bfloat16), tri_ref[...], preferred_element_type=jnp.float32)
        slots = (ranks + offsets).astype(jnp.int32)
        pieces = [bf16_pieces(value) for value in q_next]
        for direction, chosen, out_ref in ((0, going_up, up_ref), (1, going_down, dn_ref)):
            slot = slots[direction : direction + 1]
            place = ((low_iota == (slot & 127)) & chosen).astype(jnp.bfloat16)
            place = jnp.concatenate([place, place, place], axis=1)
            which = slot_iota == (slot >> 7)
            spread = jnp.concatenate(
                [
                    jnp.concatenate([jnp.where(which, piece, zero) for piece in pieces[k]], axis=1)
                    for k in range(3)
                ],
                axis=0,
            )
            out_ref[...] += lax.dot_general(spread, place, nt_dims, preferred_element_type=jnp.float32)
        return offsets + jnp.sum(flags, axis=1, keepdims=True)

    lax.fori_loop(0, count // CHUNK, body, start_ref[...])


def stress_partials(slab, q_state, element, migration, slab_elems, n_dev):
    groups = slab_elems // 128
    rows = round_up(3 * groups, 16)
    count = q_state.shape[1]
    vmem = pl.BlockSpec(memory_space=pltpu.VMEM)
    return pl.pallas_call(
        functools.partial(stress_kernel, groups=groups, rows=rows),
        out_shape=jax.ShapeDtypeStruct((n_dev, 12, 128), jnp.float32),
        in_specs=[pl.BlockSpec(memory_space=pltpu.SMEM)] + [vmem] * 3,
        out_specs=vmem,
        scratch_shapes=[pltpu.VMEM((4 * rows, 128), jnp.float32)],
        cost_estimate=pl.CostEstimate(
            flops=2 * 3 * 4 * rows * 128 * count, transcendentals=0, bytes_accessed=20 * count
        ),
    )(slab, q_state, element.reshape(1, -1), migration.reshape(1, -1))


def first_kernel(pt_ref, ft_ref, vout_ref, send_ref):
    own = vout_ref.shape[0]
    rows = [
        damping * jnp.sum(pt_ref[b] * ft_ref[:, b : b + 1], axis=0, keepdims=True)
        for b in range(own)
    ]
    fresh = jnp.concatenate(rows, axis=0)
    vout_ref[...] = fresh
    for k in range(send_ref.shape[0] // own):
        send_ref[k * own : (k + 1) * own, :] = fresh


def first_velocity(transposed, force_t, copies):
    own, size = transposed.shape[0], transposed.shape[1]
    return pl.pallas_call(
        first_kernel,
        out_shape=(
            jax.ShapeDtypeStruct((own, size), jnp.float32),
            jax.ShapeDtypeStruct((copies * own, size), jnp.float32),
        ),
        cost_estimate=pl.CostEstimate(
            flops=2 * transposed.size, transcendentals=0, bytes_accessed=4 * transposed.size
        ),
    )(transposed, force_t)


def update_and_pack(q_state, increments, element, migration, table, capacity):
    rows, slab_elems = table.shape
    groups = slab_elems // 128
    groups16 = round_up(groups, 16)
    slots = capacity // 128
    slots16 = round_up(slots, 16)
    arranged = jnp.pad(table.reshape(rows, groups, 128), ((0, 0), (0, groups16 - groups), (0, 0)))
    arranged = arranged.reshape(rows * groups16, 128)
    hi = lax.reduce_precision(arranged, exponent_bits=8, mantissa_bits=7)
    rest = arranged - hi
    mid = lax.reduce_precision(rest, exponent_bits=8, mantissa_bits=7)
    lo = rest - mid
    pieces = jnp.concatenate([hi, mid, lo], axis=1).astype(jnp.bfloat16)
    count = q_state.shape[1]
    parts = UPDATE_PARTS
    share = count // parts
    flags = jnp.stack([migration == 1, migration == -1]).astype(jnp.float32)
    per_part = jnp.sum(flags.reshape(2, parts, share), axis=2)
    starts = jnp.cumsum(per_part, axis=1) - per_part
    starts = jnp.pad(starts.T, ((0, 0), (0, 6)))[:, :, None]
    q_parts, up, down = [], 0.0, 0.0
    for part in range(parts):
        q_part, up_part, down_part = pl.pallas_call(
            functools.partial(
                update_kernel, groups16=groups16, slots16=slots16, first=part * share // CHUNK
            ),
            out_shape=(
                jax.ShapeDtypeStruct((3, share), jnp.float32),
                jax.ShapeDtypeStruct((3 * slots16, 128), jnp.float32),
                jax.ShapeDtypeStruct((3 * slots16, 128), jnp.float32),
            ),
            scratch_shapes=[pltpu.VMEM((CHUNK, CHUNK), jnp.bfloat16)],
            cost_estimate=pl.CostEstimate(
                flops=16 * 3 * (5 * groups16 + 6 * slots16) * 128 * share,
                transcendentals=0,
                bytes_accessed=40 * share,
            ),
        )(
            q_state,
            increments,
            element.reshape(1, -1),
            migration.reshape(1, -1),
            pieces,
            starts[part],
        )
        q_parts.append(q_part)
        up = up + up_part
        down = down + down_part
    q_next = jnp.concatenate(q_parts, axis=1)

    def unpack(acc):
        return acc.reshape(3, slots16, 128)[:, :slots].reshape(3, slots * 128)

    return q_next, unpack(up), unpack(down)


def sweep_kernel(idx_ref, g_ref, s_ref, pt_ref, ft_ref, v_ref, vout_ref, send_ref):
    total = g_ref.shape[0]
    own = v_ref.shape[0]
    width = s_ref.shape[1]
    rows = []
    for b in range(own):
        acc = None
        for n in range(width):
            w = idx_ref[b * width + n]
            inside = jnp.logical_and(w >= 0, w < total)
            near = g_ref[pl.ds(jnp.clip(w, 0, total - 1), 1), :]
            near = jnp.where(inside, near, 0.0)
            term = s_ref[b, n] * near
            acc = term if acc is None else acc + term
        image = jnp.sum(acc, axis=1, keepdims=True)
        rest = ft_ref[:, b : b + 1] - image
        update = jnp.sum(pt_ref[b] * rest, axis=0, keepdims=True)
        rows.append(v_ref[b : b + 1, :] + damping * update)
    fresh = jnp.concatenate(rows, axis=0)
    vout_ref[...] = fresh
    for k in range(send_ref.shape[0] // own):
        send_ref[k * own : (k + 1) * own, :] = fresh


def sweep(where_read, gathered, stiffness, transposed, force_t, velocity, copies):
    own = velocity.shape[0]
    vmem = pl.BlockSpec(memory_space=pltpu.VMEM)
    return pl.pallas_call(
        sweep_kernel,
        out_shape=(
            jax.ShapeDtypeStruct(velocity.shape, jnp.float32),
            jax.ShapeDtypeStruct((copies * own, velocity.shape[1]), jnp.float32),
        ),
        in_specs=[pl.BlockSpec(memory_space=pltpu.SMEM)] + [vmem] * 5,
        out_specs=(vmem, vmem),
        cost_estimate=pl.CostEstimate(
            flops=2 * (stiffness.size + transposed.size),
            transcendentals=0,
            bytes_accessed=4 * (stiffness.size + transposed.size + gathered.size),
        ),
    )(where_read, gathered, stiffness, transposed, force_t, velocity)


def passed_along(array, axis, by):
    size = lax.axis_size(axis)
    pairs = [(i, i + by) for i in range(size) if 0 <= i + by < size]
    return lax.ppermute(array, axis, pairs)


def body(
    q_state,
    increments,
    velocity_grad,
    element,
    migration,
    volume,
    div_map,
    stiffness,
    pattern,
    preconditioner,
):
    capacity = migration.shape[0] // 16
    slab_elems = velocity_grad.shape[1]
    n_slab = lax.axis_size("slab")
    slab = lax.axis_index("slab")

    n_rad = lax.axis_size("rad")
    send = stress_partials(
        slab.reshape(1).astype(jnp.int32), q_state, element, migration, slab_elems, n_slab * n_rad
    )
    received = lax.all_to_all(send, ("slab", "rad"), 0, 0, tiled=True)
    sums = jnp.sum(received, axis=0).reshape(4, slab_elems // n_rad)
    element_stress = sums / volume

    q_next, upward, downward = update_and_pack(
        q_state, increments, element, migration, velocity_grad, capacity
    )
    from_lower = passed_along(upward, "slab", 1)
    from_upper = passed_along(downward, "slab", -1)
    arrivals = jnp.stack([from_lower, from_upper])

    own_blocks = stiffness.shape[0]
    groups = (
        element_stress.reshape(4, own_blocks, BLOCK // 4)
        .transpose(1, 0, 2)
        .reshape(own_blocks, BLOCK)
    )
    force = jnp.dot(groups, div_map, precision=highest)

    def precondition(vector):
        return jnp.einsum("bij,bj->bi", preconditioner, vector, precision=highest)

    slab_blocks = own_blocks * n_rad
    copies = n_slab * n_rad
    where_read = ((slab - 1) * slab_blocks + pattern).reshape(-1).astype(jnp.int32)
    transposed = jnp.swapaxes(preconditioner, 1, 2)
    force_t = force.T
    velocity, send = first_velocity(transposed, force_t, copies)
    for sweep_index in range(1, ITERS):
        gathered = lax.all_to_all(send, ("slab", "rad"), 0, 0, tiled=True)
        velocity, send = sweep(
            where_read, gathered, stiffness, transposed, force_t, velocity, copies
        )
    return (q_next, arrivals, element_stress, velocity)


def solution(mesh):
    placed = (
        P(None, ("slab", "rad")),
        P(None, ("slab", "rad")),
        P(None, "slab"),
        P(("slab", "rad")),
        P(("slab", "rad")),
        P(("slab", "rad")),
        P(),
        P(("slab", "rad"), None, None, None),
        P(("slab", "rad"), None),
        P(("slab", "rad"), None, None),
    )
    return jax.shard_map(
        body,
        mesh=mesh,
        in_specs=placed,
        out_specs=(
            P(None, ("slab", "rad")),
            P(None, None, ("slab", "rad")),
            P(None, ("slab", "rad")),
            P(("slab", "rad"), None),
        ),
        check_vma=False,
    )
```

```python
import functools

import jax
import jax.numpy as jnp
from jax import lax
from jax.experimental import pallas as pl
from jax.experimental.pallas import tpu as pltpu
from jax.sharding import PartitionSpec as P

BLOCK = 192
ITERS = 6
CHUNK = 2048
STRESS_CHUNK = 8192
UPDATE_PARTS = 4

extensibility = 50.0
time_step = 0.01
noise_scale = 0.1
damping = 0.6
highest = lax.Precision.HIGHEST
nt_dims = (((1,), (1,)), ((), ()))


def round_up(value, step):
    return -(-value // step) * step


def bf16_pieces(x):
    hi = x.astype(jnp.bfloat16)
    rest = x - hi.astype(jnp.float32)
    mid = rest.astype(jnp.bfloat16)
    lo = (rest - mid.astype(jnp.float32)).astype(jnp.bfloat16)
    return (hi, mid, lo)


def spring_terms(q):
    radial = q[0:1]
    axial = q[1:2]
    azimuth = q[2:3]
    stretch = radial * radial + axial * axial + azimuth * azimuth
    spring = 1.0 / (1.0 - stretch / extensibility)
    terms = (
        spring * radial * radial - 1.0,
        spring * axial * axial - 1.0,
        spring * radial * axial,
        spring * azimuth * azimuth - 1.0,
    )
    return spring, terms


def stress_kernel(slab_ref, q_ref, e_ref, m_ref, send_ref, acc_ref, *, groups, rows):
    count = q_ref.shape[1]
    n_dev = send_ref.shape[0]
    n_rad = groups // 3
    acc_ref[...] = jnp.zeros_like(acc_ref)
    low_iota = lax.broadcasted_iota(jnp.int32, (128, STRESS_CHUNK), 0)
    row_iota = lax.broadcasted_iota(jnp.int32, (rows, STRESS_CHUNK), 0)
    zero = jnp.zeros((), jnp.bfloat16)

    def body(step, carry):
        cols = pl.ds(pl.multiple_of(step * STRESS_CHUNK, STRESS_CHUNK), STRESS_CHUNK)
        q = q_ref[:, cols]
        element = e_ref[:, cols]
        move = m_ref[:, cols]
        spring, terms = spring_terms(q)
        kind = jnp.where(move == 0, 1, jnp.where(move == 1, 2, 0))
        key = kind * groups + (element >> 7)
        low = (low_iota == (element & 127)).astype(jnp.bfloat16)
        low = jnp.concatenate([low, low], axis=1)
        mask = row_iota == key
        spread = jnp.concatenate(
            [
                jnp.concatenate(
                    [jnp.where(mask, piece, zero) for piece in bf16_pieces(term)[:2]], axis=1
                )
                for term in terms
            ],
            axis=0,
        )
        acc_ref[...] += lax.dot_general(spread, low, nt_dims, preferred_element_type=jnp.float32)
        return carry

    lax.fori_loop(0, count // STRESS_CHUNK, body, 0)
    send_ref[...] = jnp.zeros_like(send_ref)
    slab = slab_ref[0]
    for kind in range(3):
        target = slab - 1 + kind

        @pl.when(jnp.logical_and(target >= 0, target * n_rad < n_dev))
        def _():
            for r in range(n_rad):
                for c in range(4):
                    start = c * rows + kind * groups + r * 3
                    send_ref[target * n_rad + r, c * 3 : c * 3 + 3, :] = acc_ref[start : start + 3, :]


def update_kernel(
    q_ref, inc_ref, e_ref, m_ref, tab_ref, start_ref, qn_ref, up_ref, dn_ref, tri_ref, *, groups16, slots16, first
):
    count = qn_ref.shape[1]
    up_ref[...] = jnp.zeros_like(up_ref)
    dn_ref[...] = jnp.zeros_like(dn_ref)
    before = lax.broadcasted_iota(jnp.int32, (CHUNK, CHUNK), 0)
    after = lax.broadcasted_iota(jnp.int32, (CHUNK, CHUNK), 1)
    tri_ref[...] = (before < after).astype(jnp.bfloat16)
    low_iota = lax.broadcasted_iota(jnp.int32, (128, CHUNK), 0)
    group_iota = lax.broadcasted_iota(jnp.int32, (groups16, CHUNK), 0)
    slot_iota = lax.broadcasted_iota(jnp.int32, (slots16, CHUNK), 0)
    flag_row = lax.broadcasted_iota(jnp.int32, (8, CHUNK), 0)
    zero = jnp.zeros((), jnp.bfloat16)

    def body(step, offsets):
        cols = pl.ds(pl.multiple_of((first + step) * CHUNK, CHUNK), CHUNK)
        q = q_ref[:, cols]
        inc = inc_ref[:, cols]
        element = e_ref[:, cols]
        move = m_ref[:, cols]
        low = (low_iota == (element & 127)).astype(jnp.bfloat16)
        picked = jnp.dot(
            tab_ref[...], jnp.concatenate([low, low, low], axis=0), preferred_element_type=jnp.float32
        )
        hit = group_iota == (element >> 7)
        grads = [
            jnp.sum(
                jnp.where(hit, picked[c * groups16 : (c + 1) * groups16], 0.0),
                axis=0,
                keepdims=True,
            )
            for c in range(5)
        ]
        radial = q[0:1]
        axial = q[1:2]
        azimuth = q[2:3]
        spring, terms = spring_terms(q)
        drift = (
            grads[0] * radial + grads[1] * axial,
            grads[2] * radial + grads[3] * axial,
            grads[4] * azimuth,
        )
        q_next = [
            q[k : k + 1] + time_step * (drift[k] - 0.5 * spring * q[k : k + 1]) + noise_scale * inc[k : k + 1]
            for k in range(3)
        ]
        qn_ref[:, pl.ds(pl.multiple_of(step * CHUNK, CHUNK), CHUNK)] = jnp.concatenate(q_next, axis=0)
        going_up = move == 1
        going_down = move == -1
        flags = jnp.where(
            flag_row == 0,
            going_up.astype(jnp.float32),
            jnp.where(flag_row == 1, going_down.astype(jnp.float32), 0.0),
        )
        ranks = jnp.dot(flags.astype(jnp.bfloat16), tri_ref[...], preferred_element_type=jnp.float32)
        slots = (ranks + offsets).astype(jnp.int32)
        pieces = [bf16_pieces(value) for value in q_next]
        for direction, chosen, out_ref in ((0, going_up, up_ref), (1, going_down, dn_ref)):
            slot = slots[direction : direction + 1]
            place = ((low_iota == (slot & 127)) & chosen).astype(jnp.bfloat16)
            place = jnp.concatenate([place, place, place], axis=1)
            which = slot_iota == (slot >> 7)
            spread = jnp.concatenate(
                [
                    jnp.concatenate([jnp.where(which, piece, zero) for piece in pieces[k]], axis=1)
                    for k in range(3)
                ],
                axis=0,
            )
            out_ref[...] += lax.dot_general(spread, place, nt_dims, preferred_element_type=jnp.float32)
        return offsets + jnp.sum(flags, axis=1, keepdims=True)

    lax.fori_loop(0, count // CHUNK, body, start_ref[...])


def stress_partials(slab, q_state, element, migration, slab_elems, n_dev):
    groups = slab_elems // 128
    rows = round_up(3 * groups, 16)
    count = q_state.shape[1]
    vmem = pl.BlockSpec(memory_space=pltpu.VMEM)
    return pl.pallas_call(
        functools.partial(stress_kernel, groups=groups, rows=rows),
        out_shape=jax.ShapeDtypeStruct((n_dev, 12, 128), jnp.float32),
        in_specs=[pl.BlockSpec(memory_space=pltpu.SMEM)] + [vmem] * 3,
        out_specs=vmem,
        scratch_shapes=[pltpu.VMEM((4 * rows, 128), jnp.float32)],
        cost_estimate=pl.CostEstimate(
            flops=2 * 3 * 4 * rows * 128 * count, transcendentals=0, bytes_accessed=20 * count
        ),
    )(slab, q_state, element.reshape(1, -1), migration.reshape(1, -1))


def first_kernel(pt_ref, ft_ref, vout_ref, send_ref):
    own = vout_ref.shape[0]
    rows = [
        damping * jnp.sum(pt_ref[b] * ft_ref[:, b : b + 1], axis=0, keepdims=True)
        for b in range(own)
    ]
    fresh = jnp.concatenate(rows, axis=0)
    vout_ref[...] = fresh
    for k in range(send_ref.shape[0] // own):
        send_ref[k * own : (k + 1) * own, :] = fresh


def first_velocity(transposed, force_t, copies):
    own, size = transposed.shape[0], transposed.shape[1]
    return pl.pallas_call(
        first_kernel,
        out_shape=(
            jax.ShapeDtypeStruct((own, size), jnp.float32),
            jax.ShapeDtypeStruct((copies * own, size), jnp.float32),
        ),
        cost_estimate=pl.CostEstimate(
            flops=2 * transposed.size, transcendentals=0, bytes_accessed=4 * transposed.size
        ),
    )(transposed, force_t)


def update_and_pack(q_state, increments, element, migration, table, capacity):
    rows, slab_elems = table.shape
    groups = slab_elems // 128
    groups16 = round_up(groups, 16)
    slots = capacity // 128
    slots16 = round_up(slots, 16)
    arranged = jnp.pad(table.reshape(rows, groups, 128), ((0, 0), (0, groups16 - groups), (0, 0)))
    arranged = arranged.reshape(rows * groups16, 128)
    hi = lax.reduce_precision(arranged, exponent_bits=8, mantissa_bits=7)
    rest = arranged - hi
    mid = lax.reduce_precision(rest, exponent_bits=8, mantissa_bits=7)
    lo = rest - mid
    pieces = jnp.concatenate([hi, mid, lo], axis=1).astype(jnp.bfloat16)
    count = q_state.shape[1]
    parts = UPDATE_PARTS
    share = count // parts
    flags = jnp.stack([migration == 1, migration == -1]).astype(jnp.float32)
    per_part = jnp.sum(flags.reshape(2, parts, share), axis=2)
    starts = jnp.cumsum(per_part, axis=1) - per_part
    starts = jnp.pad(starts.T, ((0, 0), (0, 6)))[:, :, None]
    q_parts, up, down = [], 0.0, 0.0
    for part in range(parts):
        q_part, up_part, down_part = pl.pallas_call(
            functools.partial(
                update_kernel, groups16=groups16, slots16=slots16, first=part * share // CHUNK
            ),
            out_shape=(
                jax.ShapeDtypeStruct((3, share), jnp.float32),
                jax.ShapeDtypeStruct((3 * slots16, 128), jnp.float32),
                jax.ShapeDtypeStruct((3 * slots16, 128), jnp.float32),
            ),
            scratch_shapes=[pltpu.VMEM((CHUNK, CHUNK), jnp.bfloat16)],
            cost_estimate=pl.CostEstimate(
                flops=16 * 3 * (5 * groups16 + 6 * slots16) * 128 * share,
                transcendentals=0,
                bytes_accessed=40 * share,
            ),
        )(
            q_state,
            increments,
            element.reshape(1, -1),
            migration.reshape(1, -1),
            pieces,
            starts[part],
        )
        q_parts.append(q_part)
        up = up + up_part
        down = down + down_part
    q_next = jnp.concatenate(q_parts, axis=1)

    def unpack(acc):
        return acc.reshape(3, slots16, 128)[:, :slots].reshape(3, slots * 128)

    return q_next, unpack(up), unpack(down)


def sweep_kernel(idx_ref, g_ref, s_ref, pt_ref, ft_ref, v_ref, vout_ref, send_ref):
    total = g_ref.shape[0]
    own = v_ref.shape[0]
    width = s_ref.shape[1]
    rows = []
    for b in range(own):
        acc = None
        for n in range(width):
            w = idx_ref[b * width + n]
            inside = jnp.logical_and(w >= 0, w < total)
            near = g_ref[pl.ds(jnp.clip(w, 0, total - 1), 1), :]
            near = jnp.where(inside, near, 0.0)
            term = s_ref[b, n] * near
            acc = term if acc is None else acc + term
        image = jnp.sum(acc, axis=1, keepdims=True)
        rest = ft_ref[:, b : b + 1] - image
        update = jnp.sum(pt_ref[b] * rest, axis=0, keepdims=True)
        rows.append(v_ref[b : b + 1, :] + damping * update)
    fresh = jnp.concatenate(rows, axis=0)
    vout_ref[...] = fresh
    for k in range(send_ref.shape[0] // own):
        send_ref[k * own : (k + 1) * own, :] = fresh


def sweep(where_read, gathered, stiffness, transposed, force_t, velocity, copies):
    own = velocity.shape[0]
    vmem = pl.BlockSpec(memory_space=pltpu.VMEM)
    return pl.pallas_call(
        sweep_kernel,
        out_shape=(
            jax.ShapeDtypeStruct(velocity.shape, jnp.float32),
            jax.ShapeDtypeStruct((copies * own, velocity.shape[1]), jnp.float32),
        ),
        in_specs=[pl.BlockSpec(memory_space=pltpu.SMEM)] + [vmem] * 5,
        out_specs=(vmem, vmem),
        cost_estimate=pl.CostEstimate(
            flops=2 * (stiffness.size + transposed.size),
            transcendentals=0,
            bytes_accessed=4 * (stiffness.size + transposed.size + gathered.size),
        ),
    )(where_read, gathered, stiffness, transposed, force_t, velocity)


def passed_along(array, axis, by):
    size = lax.axis_size(axis)
    pairs = [(i, i + by) for i in range(size) if 0 <= i + by < size]
    return lax.ppermute(array, axis, pairs)


def body(
    q_state,
    increments,
    velocity_grad,
    element,
    migration,
    volume,
    div_map,
    stiffness,
    pattern,
    preconditioner,
):
    capacity = migration.shape[0] // 16
    slab_elems = velocity_grad.shape[1]
    n_slab = lax.axis_size("slab")
    slab = lax.axis_index("slab")

    n_rad = lax.axis_size("rad")
    send = stress_partials(
        slab.reshape(1).astype(jnp.int32), q_state, element, migration, slab_elems, n_slab * n_rad
    )
    received = lax.all_to_all(send, ("slab", "rad"), 0, 0, tiled=True)
    sums = jnp.sum(received, axis=0).reshape(4, slab_elems // n_rad)
    element_stress = sums / volume

    q_next, upward, downward = update_and_pack(
        q_state, increments, element, migration, velocity_grad, capacity
    )
    from_lower = passed_along(upward, "slab", 1)
    from_upper = passed_along(downward, "slab", -1)
    arrivals = jnp.stack([from_lower, from_upper])

    own_blocks = stiffness.shape[0]
    groups = (
        element_stress.reshape(4, own_blocks, BLOCK // 4)
        .transpose(1, 0, 2)
        .reshape(own_blocks, BLOCK)
    )
    force = jnp.dot(groups, div_map, precision=highest)

    def precondition(vector):
        return jnp.einsum("bij,bj->bi", preconditioner, vector, precision=highest)

    slab_blocks = own_blocks * n_rad
    copies = n_slab * n_rad
    where_read = ((slab - 1) * slab_blocks + pattern).reshape(-1).astype(jnp.int32)
    transposed = jnp.swapaxes(preconditioner, 1, 2)
    force_t = force.T
    velocity, send = first_velocity(transposed, force_t, copies)
    for sweep_index in range(1, ITERS):
        gathered = lax.all_to_all(send, ("slab", "rad"), 0, 0, tiled=True)
        velocity, send = sweep(
            where_read, gathered, stiffness, transposed, force_t, velocity, copies
        )
    return (q_next, arrivals, element_stress, velocity)


def solution(mesh):
    placed = (
        P(None, ("slab", "rad")),
        P(None, ("slab", "rad")),
        P(None, "slab"),
        P(("slab", "rad")),
        P(("slab", "rad")),
        P(("slab", "rad")),
        P(),
        P(("slab", "rad"), None, None, None),
        P(("slab", "rad"), None),
        P(("slab", "rad"), None, None),
    )
    return jax.shard_map(
        body,
        mesh=mesh,
        in_specs=placed,
        out_specs=(
            P(None, ("slab", "rad")),
            P(None, None, ("slab", "rad")),
            P(None, ("slab", "rad")),
            P(("slab", "rad"), None),
        ),
        check_vma=False,
    )
```
